32 devices in a mesh: ctx: 8 (over z, y), seq: 4 (over x, core).
Axes of the slice: x: 2, y: 2, z: 4, core: 2. Of those that a mesh axis runs over, the one named last changes fastest.
Arguments:
- tokens: bfloat16 [16384, 1024], P(('ctx', 'seq')), may hold values from -60 to 60
- w_qkv: bfloat16 [1024, 3072], replicated, may hold values from -1 to 1
- w_out: bfloat16 [1024, 1024], replicated, may hold values from -0.1875 to 0.1875
- counts: int32 [256], replicated, may hold values from 1 to 64
- rand_seg: int32 [256, 3], replicated, may hold values from 0 to 7, all different within a row; in each aligned block of 8 rows (0 to 7, 8 to 15, ...) at most 4 rows name the same one
- rand_off: int32 [256, 3], replicated, may hold values from 0 to 7
Outputs:
- mixed: bfloat16 [16384, 1024], P(('ctx', 'seq'))
The draws below stay inside these ranges and needn't reach their ends.
Inputs may be any that keep to these rules, and one draw needn't show every extreme that they name: `rand_seg`: each row names 3 different segments; among the 8 rows of one device no segment is named more than 4 times, a bound that some block reaches.
All inputs are finite; a program needn't handle non-finite values.
Results may differ from the reference program's by a relative error of at most 0.0045.
The reference program's roundings to bfloat16 on the way count: a program that leaves them out, or rounds other values in their place, can miss the bound.
Values may be sent and summed in bfloat16 or wider, within the bound.
No kernel may reach another device: no remote copies, remote signals or barrier semaphores. Data moves between devices by JAX's collectives and lax.ppermute only.
A program may use at most 192 MiB of HBM per device.

```python
import math
import jax
import jax.numpy as jnp
import numpy as np
from jax import lax

D = 1024
H = 16
HD = 64
BLK = 64
RAND = 3
TOKENS = 16384
DB = 8
QB_SEG = 32
NB = 256
G_ALL = 256
CAP = 4
N_CTX = 8
N_SEQ = 4


def draw_tokens(key, part):
    base = jax.random.normal(jax.random.fold_in(key, 11), (TOKENS, D), jnp.float32)
    values = jnp.clip(base, -6.0, 6.0)
    return jnp.clip(values, -60.0, 60.0).astype(jnp.bfloat16)


def draw_w_qkv(key, part):
    keys = jax.random.split(jax.random.fold_in(key, 21), 3)
    inverse = 1.0 / math.sqrt(D)
    query_part = jax.random.normal(keys[0], (D, H, 1, HD), jnp.float32) * (1.5 * inverse)
    key_part = jax.random.normal(keys[1], (D, H, 1, HD), jnp.float32) * (1.5 * inverse)
    value_part = jax.random.normal(keys[2], (D, H, 1, HD), jnp.float32) * inverse
    joined = jnp.concatenate([query_part, key_part, value_part], axis=2).reshape(D, 3 * D)
    return jnp.clip(joined, -1.0, 1.0).astype(jnp.bfloat16)


def plant(entries, key, smallest, top_value):
    place = [jax.random.randint(jax.random.fold_in(key, axis), (), 0, length) for axis, length in enumerate(entries.shape)]
    longest = entries.shape.index(max(entries.shape))
    next_to = place[:longest] + [(place[longest] + 1) % entries.shape[longest]] + place[longest + 1:]
    return entries.at[tuple(place)].set(smallest).at[tuple(next_to)].set(top_value)


def deal_out(own_key, own, number, rows, amount, top, reach, lean):
    ranking = jax.random.permutation(own_key, amount)
    crowded, ordinary = portions_of(amount, rows * top, reach, lean, True), portions_of(amount, rows * top, reach, lean, False)
    places = jnp.arange(amount)

    def named(tallies, turn):
        used = int((tallies > 0).sum())
        fixed = max(1, used // 4)
        shifted = fixed + (places - fixed + turn * (used - fixed)) % max(1, amount - fixed)
        return jnp.zeros((amount,), jnp.int32).at[ranking[jnp.where(places < fixed, places, shifted)]].set(jnp.asarray(tallies, jnp.int32))

    tallies = jnp.where(number % 4 == 0, named(crowded, number // 4), named(ordinary, number - number // 4 - 1))
    mixed = jax.random.permutation(jax.random.fold_in(own, 3), amount)
    donor, taker = mixed[0:amount // 2 * 2:2], mixed[1:amount // 2 * 2:2]
    margin = jnp.minimum(tallies[donor] - 1, reach - tallies[taker]) // 2
    margin = jnp.where((donor == ranking[0]) | (taker == ranking[0]) | (tallies[taker] == 0), 0, jnp.maximum(margin, 0))
    shifted = jax.random.randint(jax.random.fold_in(own, 4), (amount // 2,), 0, 1 << 20) % (margin + 1)
    tallies = tallies.at[donor].add(-shifted).at[taker].add(shifted)
    items = jnp.searchsorted(jnp.cumsum(tallies), jnp.arange(rows * top), side="right").astype(jnp.int32)
    table = items.reshape(top, rows).T
    table = table[jax.random.permutation(jax.random.fold_in(own, 1), rows)]
    turn = jax.random.randint(jax.random.fold_in(own, 2), (rows, 1), 0, top)
    return jnp.take_along_axis(table, (jnp.arange(top)[None, :] + turn) % top, axis=1)


def portions_of(number_of, total, reach, skew, full):
    weights = [(1 << 20) // math.isqrt(standing ** skew) + 1 for standing in range(1, number_of + 1)]
    largest = reach if full else min(reach, max(-(-total // number_of), total * weights[0] // sum(weights)))
    least = 1 if total - largest >= number_of - 1 else 0
    given, surplus = [largest] + [least] * (number_of - 1), total - largest - least * (number_of - 1)
    while surplus > 0:
        candidates = [i for i in range(1, number_of) if given[i] < largest] or [i for i in range(1, number_of) if given[i] < reach]
        mass, budget = sum([weights[i] for i in candidates]), surplus
        for i in candidates:
            addition = min(reach - given[i], max(1, budget * weights[i] // mass), surplus)
            given[i] = given[i] + addition
            surplus = surplus - addition
    return np.array(given)


def scatter_about(key, dims, spread, limit, kind=jnp.bfloat16):
    array = spread * jax.random.normal(key, dims, jnp.float32)
    return jnp.clip(array, min=-limit, max=limit).astype(kind)


def setup_inputs(seed: int = 0) -> dict:
    seeds = jax.random.split(jax.random.key(seed), 7)
    tokens = draw_tokens(jax.random.fold_in(seeds[6], 71), 0)
    w_qkv = draw_w_qkv(jax.random.fold_in(seeds[6], 71), 0)
    w_out = scatter_about(seeds[2], (D, D), D ** -0.5, 0.1875)
    counts = plant(jax.random.randint(seeds[3], (NB,), 1, BLK + 1), jax.random.fold_in(seeds[3], 1), 1, BLK).astype(jnp.int32)
    rand_seg_keys = jax.random.split(jax.random.fold_in(seeds[4], 1), NB // DB)
    rand_seg_turns = jax.random.permutation(jax.random.fold_in(seeds[4], 3), NB // DB)
    rand_seg = jax.vmap(lambda own, number: deal_out(jax.random.fold_in(seeds[4], 2), own, number, DB, N_CTX, RAND, CAP, 1))(rand_seg_keys, rand_seg_turns).reshape((NB, RAND))
    rand_off = plant(jax.random.randint(seeds[5], (NB, RAND), 0, DB), jax.random.fold_in(seeds[5], 1), 0, DB - 1).astype(jnp.int32)
    return {"tokens": tokens, "w_qkv": w_qkv, "w_out": w_out, "counts": counts, "rand_seg": rand_seg, "rand_off": rand_off}


def attend(queries, window, distant, globals_kv, block_ids, far_ids, counts):
    group_len, block_len, head_count, head_dim = queries.shape
    block_total = counts.shape[0]
    local_kv = jnp.concatenate([window, distant], axis=1)
    slot_count = local_kv.shape[1]
    local_kv = local_kv.reshape(group_len, slot_count * block_len, head_count, 2, head_dim).astype(jnp.float32)
    offsets = jnp.arange(-1, 2, dtype=jnp.int32)
    near_ids = block_ids[:, None] + offsets[None, :]
    existing = (near_ids >= 0) & (near_ids < block_total)
    near_counts = jnp.where(existing, jnp.take(counts, jnp.clip(near_ids, 0, block_total - 1)), 0)
    far_counts = jnp.take(counts, far_ids)
    key_counts = jnp.concatenate([near_counts, far_counts], axis=1)
    usable = (jnp.arange(block_len, dtype=jnp.int32)[None, None, :] < key_counts[:, :, None]).reshape(group_len, slot_count * block_len)
    scaling = 1.0 / math.sqrt(head_dim)
    query_wide = queries.astype(jnp.float32)
    global_wide = globals_kv.astype(jnp.float32)
    near_scores = jnp.einsum('bqhd,bkhd->bhqk', query_wide, local_kv[:, :, :, 0]) * scaling
    near_scores = jnp.where(usable[:, None, None, :], near_scores, -jnp.inf)
    wide_scores = jnp.einsum('bqhd,khd->bhqk', query_wide, global_wide[:, :, 0]) * scaling
    peak_score = jnp.maximum(lax.optimization_barrier(jnp.max(near_scores, axis=-1)), lax.optimization_barrier(jnp.max(wide_scores, axis=-1)))[..., None]
    near_exp = jnp.exp(near_scores - peak_score)
    wide_exp = jnp.exp(wide_scores - peak_score)
    denominator = lax.optimization_barrier(jnp.sum(near_exp, axis=-1, keepdims=True)) + lax.optimization_barrier(jnp.sum(wide_exp, axis=-1, keepdims=True))
    near_prob = (near_exp / denominator).astype(jnp.bfloat16).astype(jnp.float32)
    wide_prob = (wide_exp / denominator).astype(jnp.bfloat16).astype(jnp.float32)
    result = jnp.einsum('bhqk,bkhd->bqhd', near_prob, local_kv[:, :, :, 1])
    result = result + jnp.einsum('bhqk,khd->bqhd', wide_prob, global_wide[:, :, 1])
    return result.astype(jnp.bfloat16)

def reference(tokens, w_qkv, w_out, counts, rand_seg, rand_off):
    qkv = jnp.dot(tokens, w_qkv, preferred_element_type=jnp.float32).astype(jnp.bfloat16).reshape(TOKENS, H, 3, HD)
    valid = (jnp.arange(BLK, dtype=jnp.int32)[None, :] < counts[:, None]).reshape(TOKENS)
    weighted = jnp.where(valid[:, None], tokens.astype(jnp.float32), 0.0)
    group_rows = TOKENS // G_ALL
    sums = lax.optimization_barrier(jnp.sum(weighted.reshape(G_ALL, group_rows, D), axis=1))
    members = lax.optimization_barrier(jnp.sum(valid.astype(jnp.float32).reshape(G_ALL, group_rows), axis=1))
    pooled = sums / members[:, None]
    summary = (pooled / jnp.sqrt(lax.optimization_barrier(jnp.mean(pooled * pooled, axis=1, keepdims=True)) + 1e-05)).astype(jnp.bfloat16)
    w_kv = w_qkv.reshape(D, H, 3, HD)[:, :, 1:, :].reshape(D, 2 * D)
    summary_kv = jnp.dot(summary, w_kv, preferred_element_type=jnp.float32).astype(jnp.bfloat16).reshape(G_ALL, H, 2, HD)
    kv_blocks = qkv[:, :, 1:, :].reshape(NB, BLK, H, 2, HD)
    zero_block = jnp.zeros((1, BLK, H, 2, HD), jnp.bfloat16)
    padded = jnp.concatenate([zero_block, kv_blocks, zero_block], axis=0)
    query_blocks = qkv[:, :, 0, :].reshape(NB, BLK, H, HD)
    slot_of_block = (jnp.arange(NB, dtype=jnp.int32) // DB % N_SEQ).astype(jnp.int32)
    far_global = (rand_seg * QB_SEG + slot_of_block[:, None] * DB + rand_off).astype(jnp.int32)
    group_span = 8

    def one_group(start):
        group_queries = lax.dynamic_slice_in_dim(query_blocks, start, group_span, 0)
        nearby = lax.dynamic_slice_in_dim(padded, start, group_span + 2, 0)
        window = jnp.stack([nearby[0:group_span], nearby[1:group_span + 1], nearby[2:group_span + 2]], axis=1)
        far_ids = lax.dynamic_slice_in_dim(far_global, start, group_span, 0)
        distant = jnp.take(kv_blocks, far_ids.reshape(-1), axis=0).reshape(group_span, RAND, BLK, H, 2, HD)
        block_ids = (start + jnp.arange(group_span, dtype=jnp.int32)).astype(jnp.int32)
        return attend(group_queries, window, distant, summary_kv, block_ids, far_ids, counts)
    starts = (jnp.arange(NB // group_span, dtype=jnp.int32) * group_span).astype(jnp.int32)
    outputs = lax.map(one_group, starts)
    attended = outputs.reshape(TOKENS, D)
    mixed = tokens.astype(jnp.float32) + jnp.dot(attended, w_out, preferred_element_type=jnp.float32)
    return mixed.astype(jnp.bfloat16)
```

```python
import math

import jax
import jax.numpy as jnp
from jax import lax
from jax.experimental import pallas as pl
from jax.experimental.pallas import tpu as pltpu
from jax.sharding import PartitionSpec as P

HD = 64
BLK = 64
RAND = 3
LANES = 128


def positions_among(owners, owner_count):
    marks = (owners[..., None] == jnp.arange(owner_count, dtype=jnp.int32)).astype(jnp.int32)
    ranks = jnp.cumsum(marks, axis=-2) - 1
    return jnp.sum(ranks * marks, axis=-1)


def serve_slots(owners, offsets, target, capacity):
    matched = owners == target
    ranks = jnp.cumsum(matched.astype(jnp.int32), axis=-1) - 1
    slot_hit = matched[..., None, :] & (
        ranks[..., None, :] == jnp.arange(capacity, dtype=jnp.int32)[:, None]
    )
    return jnp.sum(jnp.where(slot_hit, offsets[..., None, :], 0), axis=-1)


def split_weights(w_qkv, head_total):
    model_dim = w_qkv.shape[0]
    shaped = w_qkv.reshape(model_dim, head_total, 3, HD)
    return [shaped[:, :, j, :].reshape(model_dim, head_total * HD) for j in range(3)]


def attention_kernel(
    mask_ref, q_ref, kp_ref, kc_ref, kn_ref, vp_ref, vc_ref, vn_ref, kf_ref, vf_ref, ks_ref, vs_ref,
    o_ref,
):
    width = q_ref.shape[-1]
    rows = q_ref.shape[1]
    scaling = 1.0 / math.sqrt(HD)
    valid = mask_ref[0] != 0
    lane = lax.broadcasted_iota(jnp.int32, (rows, LANES), 1)
    low = lane < HD
    far_count = kf_ref.shape[1]
    contract = (((1,), (1,)), ((), ()))
    for tile in range(width // LANES):
        cols = pl.ds(tile * LANES, LANES)
        q = q_ref[0, :, cols]
        k_local = jnp.concatenate(
            [kp_ref[0, :, cols], kc_ref[0, :, cols], kn_ref[0, :, cols]]
            + [kf_ref[0, j, :, cols] for j in range(far_count)],
            axis=0,
        )
        v_local = jnp.concatenate(
            [vp_ref[0, :, cols], vc_ref[0, :, cols], vn_ref[0, :, cols]]
            + [vf_ref[0, j, :, cols] for j in range(far_count)],
            axis=0,
        )
        k_sum = ks_ref[:, cols]
        v_sum = vs_ref[:, cols]
        halves = []
        for part in (low, jnp.logical_not(low)):
            q_head = jnp.where(part, q, jnp.zeros_like(q))
            near = lax.dot_general(q_head, k_local, contract, preferred_element_type=jnp.float32)
            near = jnp.where(valid, near * scaling, -jnp.inf)
            wide = lax.dot_general(q_head, k_sum, contract, preferred_element_type=jnp.float32)
            wide = wide * scaling
            peak = jnp.maximum(
                jnp.max(near, axis=-1, keepdims=True), jnp.max(wide, axis=-1, keepdims=True)
            )
            near_exp = jnp.exp(near - peak)
            wide_exp = jnp.exp(wide - peak)
            denominator = jnp.sum(near_exp, axis=-1, keepdims=True) + jnp.sum(
                wide_exp, axis=-1, keepdims=True
            )
            inverse = 1.0 / denominator
            near_prob = (near_exp * inverse).astype(jnp.bfloat16)
            wide_prob = (wide_exp * inverse).astype(jnp.bfloat16)
            result = jnp.dot(near_prob, v_local, preferred_element_type=jnp.float32)
            result = result + jnp.dot(wide_prob, v_sum, preferred_element_type=jnp.float32)
            halves.append(result)
        o_ref[0, :, cols] = jnp.where(low, halves[0], halves[1]).astype(o_ref.dtype)


def attend(mask, q, k_ext, v_ext, k_far, v_far, k_sum, v_sum):
    blocks, rows, width = q.shape
    far_count = k_far.shape[1]
    keys = k_sum.shape[0]
    block = lambda offset: pl.BlockSpec((1, rows, width), lambda i: (i + offset, 0, 0))
    far_spec = pl.BlockSpec((1, far_count, rows, width), lambda i: (i, 0, 0, 0))
    whole = pl.BlockSpec((keys, width), lambda i: (0, 0))
    local_keys = (3 + far_count) * rows
    heads = width // HD
    flops = blocks * heads * 2 * 2 * rows * 2 * HD * (local_keys + keys)
    bytes_accessed = 2 * (
        blocks * rows * width * (2 + 2 * 3 + 2 * far_count) + 2 * keys * width
    ) + 4 * blocks * local_keys
    return pl.pallas_call(
        attention_kernel,
        grid=(blocks,),
        in_specs=[
            pl.BlockSpec((1, 1, local_keys), lambda i: (i, 0, 0)),
            block(0),
            block(0),
            block(1),
            block(2),
            block(0),
            block(1),
            block(2),
            far_spec,
            far_spec,
            whole,
            whole,
        ],
        out_specs=block(0),
        out_shape=jax.ShapeDtypeStruct((blocks, rows, width), jnp.bfloat16),
        cost_estimate=pl.CostEstimate(
            flops=flops,
            transcendentals=blocks * heads * rows * (local_keys + keys),
            bytes_accessed=bytes_accessed,
        ),
    )(mask, q, k_ext, k_ext, k_ext, v_ext, v_ext, v_ext, k_far, v_far, k_sum, v_sum)


def local(tokens, w_qkv, w_out, counts, rand_seg, rand_off):
    seq_count = lax.axis_size("seq")
    ctx_count = lax.axis_size("ctx")
    seq_index = lax.axis_index("seq")
    ctx_index = lax.axis_index("ctx")
    dev_count = seq_count * ctx_count
    dev_index = ctx_index * seq_count + seq_index
    tok_rows, model_dim = tokens.shape
    head_total = model_dim // HD
    dev_blocks = tok_rows // BLK
    seg_blocks = dev_blocks * seq_count
    block_total = counts.shape[0]
    capacity = (RAND * dev_blocks + ctx_count - 1) // ctx_count + 1
    first_block = dev_index * dev_blocks
    token_blocks = tokens.reshape(dev_blocks, BLK, model_dim)

    all_owner = rand_seg.reshape(ctx_count, seq_count, dev_blocks * RAND)
    all_offset = rand_off.reshape(ctx_count, seq_count, dev_blocks * RAND)
    col_owner = lax.dynamic_index_in_dim(all_owner, seq_index, axis=1, keepdims=False)
    col_offset = lax.dynamic_index_in_dim(all_offset, seq_index, axis=1, keepdims=False)
    send_off = serve_slots(col_owner, col_offset, ctx_index, capacity)
    outgoing = jnp.take(token_blocks, send_off.reshape(-1), axis=0).reshape(
        ctx_count, capacity, BLK, model_dim
    )
    incoming = lax.all_to_all(outgoing, "ctx", split_axis=0, concat_axis=0, tiled=True)
    forward = [(i, i + 1) for i in range(dev_count - 1)]
    backward = [(i + 1, i) for i in range(dev_count - 1)]
    prev_tokens = lax.ppermute(token_blocks[dev_blocks - 1], ("ctx", "seq"), forward)
    next_tokens = lax.ppermute(token_blocks[0], ("ctx", "seq"), backward)

    usable = jnp.arange(BLK, dtype=jnp.int32)[None, :] < lax.dynamic_slice_in_dim(
        counts, first_block, dev_blocks
    )[:, None]
    weighted = jnp.where(usable[:, :, None], token_blocks.astype(jnp.float32), 0.0)
    sums = jnp.sum(weighted, axis=1)
    members = jnp.sum(usable.astype(jnp.float32), axis=1)
    pooled = sums / members[:, None]
    summary = (pooled / jnp.sqrt(jnp.mean(pooled * pooled, axis=1, keepdims=True) + 1e-05)).astype(
        jnp.bfloat16
    )
    summary_all = lax.all_gather(summary, ("ctx", "seq"), axis=0, tiled=True)

    w_q, w_k, w_v = split_weights(w_qkv, head_total)
    project = lambda x, w: jnp.dot(x, w, preferred_element_type=jnp.float32).astype(jnp.bfloat16)
    q_own = project(tokens, w_q).reshape(dev_blocks, BLK, model_dim)
    k_own = project(tokens, w_k).reshape(dev_blocks, BLK, model_dim)
    v_own = project(tokens, w_v).reshape(dev_blocks, BLK, model_dim)
    k_sum = project(summary_all, w_k)
    v_sum = project(summary_all, w_v)

    my_owner = lax.dynamic_slice_in_dim(rand_seg, first_block, dev_blocks)
    my_offset = lax.dynamic_slice_in_dim(rand_off, first_block, dev_blocks)
    mine = my_owner.reshape(dev_blocks * RAND)
    slot_ids = mine * capacity + positions_among(mine, ctx_count)
    fetched = jnp.take(
        incoming.reshape(ctx_count * capacity, BLK, model_dim), slot_ids, axis=0
    )
    extra = jnp.concatenate([fetched, prev_tokens[None], next_tokens[None]], axis=0).reshape(
        -1, model_dim
    )
    k_extra = project(extra, w_k).reshape(-1, BLK, model_dim)
    v_extra = project(extra, w_v).reshape(-1, BLK, model_dim)
    far_blocks = dev_blocks * RAND
    k_far = k_extra[:far_blocks].reshape(dev_blocks, RAND, BLK, model_dim)
    v_far = v_extra[:far_blocks].reshape(dev_blocks, RAND, BLK, model_dim)
    k_ext = jnp.concatenate([k_extra[far_blocks : far_blocks + 1], k_own, k_extra[far_blocks + 1 :]])
    v_ext = jnp.concatenate([v_extra[far_blocks : far_blocks + 1], v_own, v_extra[far_blocks + 1 :]])

    block_ids = first_block + jnp.arange(dev_blocks, dtype=jnp.int32)
    near_ids = block_ids[:, None] + jnp.arange(-1, 2, dtype=jnp.int32)[None, :]
    existing = (near_ids >= 0) & (near_ids < block_total)
    near_counts = jnp.where(existing, jnp.take(counts, jnp.clip(near_ids, 0, block_total - 1)), 0)
    far_global = my_owner * seg_blocks + seq_index * dev_blocks + my_offset
    far_counts = jnp.take(counts, far_global)
    key_counts = jnp.concatenate([near_counts, far_counts], axis=1)
    mask = (jnp.arange(BLK, dtype=jnp.int32)[None, None, :] < key_counts[:, :, None]).astype(
        jnp.int32
    )
    mask = mask.reshape(dev_blocks, 1, -1)

    attended = attend(mask, q_own, k_ext, v_ext, k_far, v_far, k_sum, v_sum).reshape(
        tok_rows, model_dim
    )
    mixed = tokens.astype(jnp.float32) + jnp.dot(attended, w_out, preferred_element_type=jnp.float32)
    return mixed.astype(jnp.bfloat16)


def solution(mesh):
    in_specs = (P(("ctx", "seq"), None), P(), P(), P(), P(), P())
    out_specs = P(("ctx", "seq"), None)
    return jax.shard_map(local, mesh=mesh, in_specs=in_specs, out_specs=out_specs, check_vma=False)
```

```python
import math

import jax
import jax.numpy as jnp
from jax import lax
from jax.experimental import pallas as pl
from jax.experimental.pallas import tpu as pltpu
from jax.sharding import PartitionSpec as P

HD = 64
BLK = 64
RAND = 3
LANES = 128


def positions_among(owners, owner_count):
    marks = (owners[..., None] == jnp.arange(owner_count, dtype=jnp.int32)).astype(jnp.int32)
    ranks = jnp.cumsum(marks, axis=-2) - 1
    return jnp.sum(ranks * marks, axis=-1)


def serve_slots(owners, offsets, target, capacity):
    matched = owners == target
    ranks = jnp.cumsum(matched.astype(jnp.int32), axis=-1) - 1
    slot_hit = matched[..., None, :] & (
        ranks[..., None, :] == jnp.arange(capacity, dtype=jnp.int32)[:, None]
    )
    return jnp.sum(jnp.where(slot_hit, offsets[..., None, :], 0), axis=-1)


def split_weights(w_qkv, head_total):
    model_dim = w_qkv.shape[0]
    shaped = w_qkv.reshape(model_dim, head_total, 3, HD)
    return [shaped[:, :, j, :].reshape(model_dim, head_total * HD) for j in range(3)]


def attention_kernel(
    mask_ref, q_ref, kp_ref, kc_ref, kn_ref, vp_ref, vc_ref, vn_ref, kf_ref, vf_ref, ks_ref, vs_ref,
    o_ref,
):
    width = q_ref.shape[-1]
    rows = q_ref.shape[1]
    scaling = 1.0 / math.sqrt(HD)
    valid = mask_ref[0] != 0
    lane = lax.broadcasted_iota(jnp.int32, (rows, LANES), 1)
    low = lane < HD
    far_count = kf_ref.shape[1]
    contract = (((1,), (1,)), ((), ()))
    for tile in range(width // LANES):
        cols = pl.ds(tile * LANES, LANES)
        q = q_ref[0, :, cols]
        k_local = jnp.concatenate(
            [kp_ref[0, :, cols], kc_ref[0, :, cols], kn_ref[0, :, cols]]
            + [kf_ref[0, j, :, cols] for j in range(far_count)],
            axis=0,
        )
        v_local = jnp.concatenate(
            [vp_ref[0, :, cols], vc_ref[0, :, cols], vn_ref[0, :, cols]]
            + [vf_ref[0, j, :, cols] for j in range(far_count)],
            axis=0,
        )
        k_sum = ks_ref[:, cols]
        v_sum = vs_ref[:, cols]
        blank = jnp.zeros_like(q)
        q_pair = jnp.concatenate([jnp.where(low, q, blank), jnp.where(low, blank, q)], axis=0)
        near = lax.dot_general(q_pair, k_local, contract, preferred_element_type=jnp.float32)
        near = jnp.where(valid, near * scaling, -jnp.inf)
        wide = lax.dot_general(q_pair, k_sum, contract, preferred_element_type=jnp.float32)
        wide = wide * scaling
        peak = jnp.maximum(
            jnp.max(near, axis=-1, keepdims=True), jnp.max(wide, axis=-1, keepdims=True)
        )
        near_exp = jnp.exp(near - peak)
        wide_exp = jnp.exp(wide - peak)
        denominator = jnp.sum(near_exp, axis=-1, keepdims=True) + jnp.sum(
            wide_exp, axis=-1, keepdims=True
        )
        inverse = 1.0 / denominator
        near_prob = (near_exp * inverse).astype(jnp.bfloat16)
        wide_prob = (wide_exp * inverse).astype(jnp.bfloat16)
        result = jnp.dot(near_prob, v_local, preferred_element_type=jnp.float32)
        result = result + jnp.dot(wide_prob, v_sum, preferred_element_type=jnp.float32)
        o_ref[0, :, cols] = jnp.where(low, result[:rows], result[rows:]).astype(o_ref.dtype)


def attend(mask, q, k_ext, v_ext, k_far, v_far, k_sum, v_sum):
    blocks, rows, width = q.shape
    far_count = k_far.shape[1]
    keys = k_sum.shape[0]
    block = lambda offset: pl.BlockSpec((1, rows, width), lambda i: (i + offset, 0, 0))
    far_spec = pl.BlockSpec((1, far_count, rows, width), lambda i: (i, 0, 0, 0))
    whole = pl.BlockSpec((keys, width), lambda i: (0, 0))
    local_keys = (3 + far_count) * rows
    heads = width // HD
    flops = blocks * heads * 2 * rows * 2 * LANES * (local_keys + keys)
    bytes_accessed = 2 * (
        blocks * rows * width * (2 + 2 * 3 + 2 * far_count) + 2 * keys * width
    ) + 4 * blocks * local_keys
    return pl.pallas_call(
        attention_kernel,
        grid=(blocks,),
        in_specs=[
            pl.BlockSpec((1, 1, local_keys), lambda i: (i, 0, 0)),
            block(0),
            block(0),
            block(1),
            block(2),
            block(0),
            block(1),
            block(2),
            far_spec,
            far_spec,
            whole,
            whole,
        ],
        out_specs=block(0),
        out_shape=jax.ShapeDtypeStruct((blocks, rows, width), jnp.bfloat16),
        cost_estimate=pl.CostEstimate(
            flops=flops,
            transcendentals=blocks * heads * rows * (local_keys + keys),
            bytes_accessed=bytes_accessed,
        ),
    )(mask, q, k_ext, k_ext, k_ext, v_ext, v_ext, v_ext, k_far, v_far, k_sum, v_sum)


def local(tokens, w_qkv, w_out, counts, rand_seg, rand_off):
    seq_count = lax.axis_size("seq")
    ctx_count = lax.axis_size("ctx")
    seq_index = lax.axis_index("seq")
    ctx_index = lax.axis_index("ctx")
    dev_count = seq_count * ctx_count
    dev_index = ctx_index * seq_count + seq_index
    tok_rows, model_dim = tokens.shape
    head_total = model_dim // HD
    dev_blocks = tok_rows // BLK
    seg_blocks = dev_blocks * seq_count
    block_total = counts.shape[0]
    capacity = (RAND * dev_blocks + ctx_count - 1) // ctx_count + 1
    first_block = dev_index * dev_blocks
    token_blocks = tokens.reshape(dev_blocks, BLK, model_dim)

    all_owner = rand_seg.reshape(ctx_count, seq_count, dev_blocks * RAND)
    all_offset = rand_off.reshape(ctx_count, seq_count, dev_blocks * RAND)
    col_owner = lax.dynamic_index_in_dim(all_owner, seq_index, axis=1, keepdims=False)
    col_offset = lax.dynamic_index_in_dim(all_offset, seq_index, axis=1, keepdims=False)
    send_off = serve_slots(col_owner, col_offset, ctx_index, capacity)
    outgoing = jnp.take(token_blocks, send_off.reshape(-1), axis=0, mode="clip").reshape(
        ctx_count, capacity, BLK, model_dim
    )
    incoming = lax.all_to_all(outgoing, "ctx", split_axis=0, concat_axis=0, tiled=True)
    forward = [(i, i + 1) for i in range(dev_count - 1)]
    backward = [(i + 1, i) for i in range(dev_count - 1)]
    prev_tokens = lax.ppermute(token_blocks[dev_blocks - 1], ("ctx", "seq"), forward)
    next_tokens = lax.ppermute(token_blocks[0], ("ctx", "seq"), backward)

    usable = jnp.arange(BLK, dtype=jnp.int32)[None, :] < lax.dynamic_slice_in_dim(
        counts, first_block, dev_blocks
    )[:, None]
    weighted = jnp.where(usable[:, :, None], token_blocks.astype(jnp.float32), 0.0)
    sums = jnp.sum(weighted, axis=1)
    members = jnp.sum(usable.astype(jnp.float32), axis=1)
    pooled = sums / members[:, None]
    summary = (pooled / jnp.sqrt(jnp.mean(pooled * pooled, axis=1, keepdims=True) + 1e-05)).astype(
        jnp.bfloat16
    )
    w_q, w_k, w_v = split_weights(w_qkv, head_total)
    project = lambda x, w: jnp.dot(x, w, preferred_element_type=jnp.float32).astype(jnp.bfloat16)
    q_own = project(tokens, w_q).reshape(dev_blocks, BLK, model_dim)
    k_own = project(tokens, w_k).reshape(dev_blocks, BLK, model_dim)
    v_own = project(tokens, w_v).reshape(dev_blocks, BLK, model_dim)
    summary, q_own, k_own, v_own = lax.optimization_barrier((summary, q_own, k_own, v_own))
    summary_all = lax.all_gather(summary, ("ctx", "seq"), axis=0, tiled=True)
    k_sum = project(summary_all, w_k)
    v_sum = project(summary_all, w_v)

    my_owner = lax.dynamic_slice_in_dim(rand_seg, first_block, dev_blocks)
    my_offset = lax.dynamic_slice_in_dim(rand_off, first_block, dev_blocks)
    mine = my_owner.reshape(dev_blocks * RAND)
    slot_ids = mine * capacity + positions_among(mine, ctx_count)
    fetched = jnp.take(
        incoming.reshape(ctx_count * capacity, BLK, model_dim), slot_ids, axis=0, mode="clip"
    )
    extra = jnp.concatenate([fetched, prev_tokens[None], next_tokens[None]], axis=0).reshape(
        -1, model_dim
    )
    k_extra = project(extra, w_k).reshape(-1, BLK, model_dim)
    v_extra = project(extra, w_v).reshape(-1, BLK, model_dim)
    far_blocks = dev_blocks * RAND
    k_far = k_extra[:far_blocks].reshape(dev_blocks, RAND, BLK, model_dim)
    v_far = v_extra[:far_blocks].reshape(dev_blocks, RAND, BLK, model_dim)
    k_ext = jnp.concatenate([k_extra[far_blocks : far_blocks + 1], k_own, k_extra[far_blocks + 1 :]])
    v_ext = jnp.concatenate([v_extra[far_blocks : far_blocks + 1], v_own, v_extra[far_blocks + 1 :]])

    block_ids = first_block + jnp.arange(dev_blocks, dtype=jnp.int32)
    near_ids = block_ids[:, None] + jnp.arange(-1, 2, dtype=jnp.int32)[None, :]
    existing = (near_ids >= 0) & (near_ids < block_total)
    near_counts = jnp.where(existing, jnp.take(counts, jnp.clip(near_ids, 0, block_total - 1)), 0)
    far_global = my_owner * seg_blocks + seq_index * dev_blocks + my_offset
    far_counts = jnp.take(counts, far_global)
    key_counts = jnp.concatenate([near_counts, far_counts], axis=1)
    mask = (jnp.arange(BLK, dtype=jnp.int32)[None, None, :] < key_counts[:, :, None]).astype(
        jnp.int32
    )
    mask = mask.reshape(dev_blocks, 1, -1)

    attended = attend(mask, q_own, k_ext, v_ext, k_far, v_far, k_sum, v_sum).reshape(
        tok_rows, model_dim
    )
    mixed = tokens.astype(jnp.float32) + jnp.dot(attended, w_out, preferred_element_type=jnp.float32)
    return mixed.astype(jnp.bfloat16)


def solution(mesh):
    in_specs = (P(("ctx", "seq"), None), P(), P(), P(), P(), P())
    out_specs = P(("ctx", "seq"), None)
    return jax.shard_map(local, mesh=mesh, in_specs=in_specs, out_specs=out_specs, check_vma=False)
```

```python
import math

import jax
import jax.numpy as jnp
from jax import lax
from jax.experimental import pallas as pl
from jax.experimental.pallas import tpu as pltpu
from jax.sharding import PartitionSpec as P

HD = 64
BLK = 64
RAND = 3
LANES = 128


def positions_among(owners, owner_count):
    marks = (owners[..., None] == jnp.arange(owner_count, dtype=jnp.int32)).astype(jnp.int32)
    ranks = jnp.cumsum(marks, axis=-2) - 1
    return jnp.sum(ranks * marks, axis=-1)


def serve_slots(owners, offsets, target, capacity):
    matched = owners == target
    ranks = jnp.cumsum(matched.astype(jnp.int32), axis=-1) - 1
    slot_hit = matched[..., None, :] & (
        ranks[..., None, :] == jnp.arange(capacity, dtype=jnp.int32)[:, None]
    )
    return jnp.sum(jnp.where(slot_hit, offsets[..., None, :], 0), axis=-1)


def split_weights(w_qkv, head_total):
    model_dim = w_qkv.shape[0]
    shaped = w_qkv.reshape(model_dim, head_total, 3, HD)
    return [shaped[:, :, j, :].reshape(model_dim, head_total * HD) for j in range(3)]


def pair_rows(q, low):
    blank = jnp.zeros_like(q)
    return jnp.concatenate([jnp.where(low, q, blank), jnp.where(low, blank, q)], axis=0)


def pick_rows(x, low, rows):
    return jnp.where(low, x[:rows], x[rows:])


CONTRACT = (((1,), (1,)), ((), ()))


def near_kernel(mask_ref, q_ref, kp_ref, kc_ref, kn_ref, vp_ref, vc_ref, vn_ref, ks_ref, vs_ref,
                o_ref, m_ref, l_ref):
    width = q_ref.shape[-1]
    rows = q_ref.shape[1]
    scaling = 1.0 / math.sqrt(HD)
    valid = mask_ref[0] != 0
    low = lax.broadcasted_iota(jnp.int32, (rows, LANES), 1) < HD
    for tile in range(width // LANES):
        cols = pl.ds(tile * LANES, LANES)
        q_pair = pair_rows(q_ref[0, :, cols], low)
        k_local = jnp.concatenate([kp_ref[0, :, cols], kc_ref[0, :, cols], kn_ref[0, :, cols]], axis=0)
        v_local = jnp.concatenate([vp_ref[0, :, cols], vc_ref[0, :, cols], vn_ref[0, :, cols]], axis=0)
        near = lax.dot_general(q_pair, k_local, CONTRACT, preferred_element_type=jnp.float32)
        near = jnp.where(valid, near * scaling, -jnp.inf)
        wide = lax.dot_general(q_pair, ks_ref[:, cols], CONTRACT, preferred_element_type=jnp.float32)
        wide = wide * scaling
        peak = jnp.maximum(
            jnp.max(near, axis=-1, keepdims=True), jnp.max(wide, axis=-1, keepdims=True)
        )
        near_exp = jnp.exp(near - peak)
        wide_exp = jnp.exp(wide - peak)
        total = jnp.sum(near_exp, axis=-1, keepdims=True) + jnp.sum(wide_exp, axis=-1, keepdims=True)
        result = jnp.dot(near_exp.astype(jnp.bfloat16), v_local, preferred_element_type=jnp.float32)
        result = result + jnp.dot(
            wide_exp.astype(jnp.bfloat16), vs_ref[:, cols], preferred_element_type=jnp.float32
        )
        o_ref[0, :, cols] = pick_rows(result, low, rows)
        m_ref[0, :, cols] = pick_rows(jnp.broadcast_to(peak, result.shape), low, rows)
        l_ref[0, :, cols] = pick_rows(jnp.broadcast_to(total, result.shape), low, rows)


def far_kernel(ids_ref, mask_ref, q_ref, *refs):
    far_count = RAND
    token_refs = refs[:far_count]
    wk_ref, wv_ref, oa_ref, ma_ref, la_ref, out_ref = refs[far_count:]
    width = q_ref.shape[-1]
    rows = q_ref.shape[1]
    scaling = 1.0 / math.sqrt(HD)
    valid = mask_ref[0] != 0
    low = lax.broadcasted_iota(jnp.int32, (rows, LANES), 1) < HD
    far_tokens = jnp.concatenate([ref[0] for ref in token_refs], axis=0)
    k_far = jnp.dot(far_tokens, wk_ref[...], preferred_element_type=jnp.float32).astype(jnp.bfloat16)
    v_far = jnp.dot(far_tokens, wv_ref[...], preferred_element_type=jnp.float32).astype(jnp.bfloat16)
    for tile in range(width // LANES):
        lanes = slice(tile * LANES, (tile + 1) * LANES)
        cols = pl.ds(tile * LANES, LANES)
        q_pair = pair_rows(q_ref[0, :, cols], low)
        scores = lax.dot_general(q_pair, k_far[:, lanes], CONTRACT, preferred_element_type=jnp.float32)
        scores = jnp.where(valid, scores * scaling, -jnp.inf)
        peak = jnp.max(scores, axis=-1, keepdims=True)
        exps = jnp.exp(scores - peak)
        total = jnp.sum(exps, axis=-1, keepdims=True)
        result = jnp.dot(exps.astype(jnp.bfloat16), v_far[:, lanes], preferred_element_type=jnp.float32)
        o_b = pick_rows(result, low, rows)
        m_b = pick_rows(jnp.broadcast_to(peak, result.shape), low, rows)
        l_b = pick_rows(jnp.broadcast_to(total, result.shape), low, rows)
        m_a = ma_ref[0, :, cols]
        peak_all = jnp.maximum(m_a, m_b)
        scale_a = jnp.exp(m_a - peak_all)
        scale_b = jnp.exp(m_b - peak_all)
        numerator = oa_ref[0, :, cols] * scale_a + o_b * scale_b
        denominator = la_ref[0, :, cols] * scale_a + l_b * scale_b
        out_ref[0, :, cols] = (numerator / denominator).astype(out_ref.dtype)


def attend_near(mask, q, k_ext, v_ext, k_sum, v_sum):
    blocks, rows, width = q.shape
    keys = k_sum.shape[0]
    block = lambda offset: pl.BlockSpec((1, rows, width), lambda i: (i + offset, 0, 0))
    whole = pl.BlockSpec((keys, width), lambda i: (0, 0))
    local_keys = 3 * rows
    heads = width // HD
    flops = blocks * heads * 2 * rows * 2 * LANES * (local_keys + keys)
    bytes_accessed = 2 * (blocks * rows * width * 7 + 2 * keys * width) + 12 * blocks * rows * width
    part = jax.ShapeDtypeStruct((blocks, rows, width), jnp.float32)
    return pl.pallas_call(
        near_kernel,
        grid=(blocks,),
        in_specs=[pl.BlockSpec((1, 1, local_keys), lambda i: (i, 0, 0)), block(0)]
        + [block(0), block(1), block(2)] * 2
        + [whole, whole],
        out_specs=[block(0)] * 3,
        out_shape=[part] * 3,
        cost_estimate=pl.CostEstimate(
            flops=flops,
            transcendentals=blocks * heads * rows * (local_keys + keys),
            bytes_accessed=bytes_accessed,
        ),
    )(mask, q, k_ext, k_ext, k_ext, v_ext, v_ext, v_ext, k_sum, v_sum)


def attend_far(slot_ids, mask, q, incoming, w_k, w_v, o_a, m_a, l_a):
    blocks, rows, width = q.shape
    model_dim = incoming.shape[-1]
    block = pl.BlockSpec((1, rows, width), lambda i, ids: (i, 0, 0))
    token_specs = [
        pl.BlockSpec((1, rows, model_dim), lambda i, ids, j=j: (ids[RAND * i + j], 0, 0))
        for j in range(RAND)
    ]
    weight = pl.BlockSpec(w_k.shape, lambda i, ids: (0, 0))
    local_keys = RAND * rows
    heads = width // HD
    flops = blocks * (
        heads * 2 * rows * 2 * LANES * local_keys + 2 * 2 * local_keys * model_dim * width
    )
    bytes_accessed = 2 * blocks * rows * (width * 2 + model_dim * RAND) + 4 * w_k.size + (
        12 * blocks * rows * width
    )
    grid_spec = pltpu.PrefetchScalarGridSpec(
        num_scalar_prefetch=1,
        grid=(blocks,),
        in_specs=[pl.BlockSpec((1, 1, local_keys), lambda i, ids: (i, 0, 0)), block]
        + token_specs
        + [weight, weight, block, block, block],
        out_specs=block,
    )
    return pl.pallas_call(
        far_kernel,
        grid_spec=grid_spec,
        out_shape=jax.ShapeDtypeStruct((blocks, rows, width), jnp.bfloat16),
        cost_estimate=pl.CostEstimate(
            flops=flops,
            transcendentals=blocks * heads * rows * local_keys,
            bytes_accessed=bytes_accessed,
        ),
    )(slot_ids, mask, q, incoming, incoming, incoming, w_k, w_v, o_a, m_a, l_a)


def local(tokens, w_qkv, w_out, counts, rand_seg, rand_off):
    seq_count = lax.axis_size("seq")
    ctx_count = lax.axis_size("ctx")
    seq_index = lax.axis_index("seq")
    ctx_index = lax.axis_index("ctx")
    dev_count = seq_count * ctx_count
    dev_index = ctx_index * seq_count + seq_index
    tok_rows, model_dim = tokens.shape
    head_total = model_dim // HD
    dev_blocks = tok_rows // BLK
    seg_blocks = dev_blocks * seq_count
    block_total = counts.shape[0]
    capacity = (RAND * dev_blocks + ctx_count - 1) // ctx_count + 1
    first_block = dev_index * dev_blocks
    token_blocks = tokens.reshape(dev_blocks, BLK, model_dim)

    all_owner = rand_seg.reshape(ctx_count, seq_count, dev_blocks * RAND)
    all_offset = rand_off.reshape(ctx_count, seq_count, dev_blocks * RAND)
    col_owner = lax.dynamic_index_in_dim(all_owner, seq_index, axis=1, keepdims=False)
    col_offset = lax.dynamic_index_in_dim(all_offset, seq_index, axis=1, keepdims=False)
    send_off = serve_slots(col_owner, col_offset, ctx_index, capacity)
    outgoing = jnp.take(token_blocks, send_off.reshape(-1), axis=0, mode="clip").reshape(
        ctx_count, capacity, BLK, model_dim
    )
    forward = [(i, i + 1) for i in range(dev_count - 1)]
    backward = [(i + 1, i) for i in range(dev_count - 1)]
    prev_tokens = lax.ppermute(token_blocks[dev_blocks - 1], ("ctx", "seq"), forward)
    next_tokens = lax.ppermute(token_blocks[0], ("ctx", "seq"), backward)

    usable = jnp.arange(BLK, dtype=jnp.int32)[None, :] < lax.dynamic_slice_in_dim(
        counts, first_block, dev_blocks
    )[:, None]
    weighted = jnp.where(usable[:, :, None], token_blocks.astype(jnp.float32), 0.0)
    sums = jnp.sum(weighted, axis=1)
    members = jnp.sum(usable.astype(jnp.float32), axis=1)
    pooled = sums / members[:, None]
    summary = (pooled / jnp.sqrt(jnp.mean(pooled * pooled, axis=1, keepdims=True) + 1e-05)).astype(
        jnp.bfloat16
    )
    summary_all = lax.all_gather(summary, ("ctx", "seq"), axis=0, tiled=True)
    summary_all, outgoing = lax.optimization_barrier((summary_all, outgoing))
    incoming = lax.all_to_all(outgoing, "ctx", split_axis=0, concat_axis=0, tiled=True)

    w_q, w_k, w_v = split_weights(w_qkv, head_total)
    project = lambda x, w: jnp.dot(x, w, preferred_element_type=jnp.float32).astype(jnp.bfloat16)
    q_own = project(tokens, w_q).reshape(dev_blocks, BLK, model_dim)
    rimmed = jnp.concatenate([prev_tokens, tokens, next_tokens], axis=0)
    k_ext = project(rimmed, w_k).reshape(dev_blocks + 2, BLK, model_dim)
    v_ext = project(rimmed, w_v).reshape(dev_blocks + 2, BLK, model_dim)
    k_sum = project(summary_all, w_k)
    v_sum = project(summary_all, w_v)

    my_owner = lax.dynamic_slice_in_dim(rand_seg, first_block, dev_blocks)
    my_offset = lax.dynamic_slice_in_dim(rand_off, first_block, dev_blocks)
    mine = my_owner.reshape(dev_blocks * RAND)
    slot_ids = mine * capacity + positions_among(mine, ctx_count)

    block_ids = first_block + jnp.arange(dev_blocks, dtype=jnp.int32)
    near_ids = block_ids[:, None] + jnp.arange(-1, 2, dtype=jnp.int32)[None, :]
    existing = (near_ids >= 0) & (near_ids < block_total)
    near_counts = jnp.where(existing, jnp.take(counts, jnp.clip(near_ids, 0, block_total - 1)), 0)
    far_global = my_owner * seg_blocks + seq_index * dev_blocks + my_offset
    far_counts = jnp.take(counts, far_global)
    positions = jnp.arange(BLK, dtype=jnp.int32)[None, None, :]
    near_mask = (positions < near_counts[:, :, None]).astype(jnp.int32).reshape(dev_blocks, 1, -1)
    far_mask = (positions < far_counts[:, :, None]).astype(jnp.int32).reshape(dev_blocks, 1, -1)

    o_a, m_a, l_a = attend_near(near_mask, q_own, k_ext, v_ext, k_sum, v_sum)
    attended = attend_far(
        slot_ids,
        far_mask,
        q_own,
        incoming.reshape(ctx_count * capacity, BLK, model_dim),
        w_k,
        w_v,
        o_a,
        m_a,
        l_a,
    ).reshape(tok_rows, model_dim)
    mixed = tokens.astype(jnp.float32) + jnp.dot(attended, w_out, preferred_element_type=jnp.float32)
    return mixed.astype(jnp.bfloat16)


def solution(mesh):
    in_specs = (P(("ctx", "seq"), None), P(), P(), P(), P(), P())
    out_specs = P(("ctx", "seq"), None)
    return jax.shard_map(local, mesh=mesh, in_specs=in_specs, out_specs=out_specs, check_vma=False)
```

```python
import math

import jax
import jax.numpy as jnp
from jax import lax
from jax.experimental import pallas as pl
from jax.experimental.pallas import tpu as pltpu
from jax.sharding import PartitionSpec as P

HD = 64
BLK = 64
RAND = 3
LANES = 128


def positions_among(owners, owner_count):
    marks = (owners[..., None] == jnp.arange(owner_count, dtype=jnp.int32)).astype(jnp.int32)
    ranks = jnp.cumsum(marks, axis=-2) - 1
    return jnp.sum(ranks * marks, axis=-1)


def serve_slots(owners, offsets, target, capacity):
    matched = owners == target
    ranks = jnp.cumsum(matched.astype(jnp.int32), axis=-1) - 1
    slot_hit = matched[..., None, :] & (
        ranks[..., None, :] == jnp.arange(capacity, dtype=jnp.int32)[:, None]
    )
    return jnp.sum(jnp.where(slot_hit, offsets[..., None, :], 0), axis=-1)


def split_weights(w_qkv, head_total):
    model_dim = w_qkv.shape[0]
    shaped = w_qkv.reshape(model_dim, head_total, 3, HD)
    return [shaped[:, :, j, :].reshape(model_dim, head_total * HD) for j in range(3)]


def pair_rows(q, low):
    blank = jnp.zeros_like(q)
    return jnp.concatenate([jnp.where(low, q, blank), jnp.where(low, blank, q)], axis=0)


def pick_rows(x, low, rows):
    return jnp.where(low, x[:rows], x[rows:])


CONTRACT = (((1,), (1,)), ((), ()))


def near_kernel(mask_ref, q_ref, kp_ref, kc_ref, kn_ref, vp_ref, vc_ref, vn_ref, ks_ref, vs_ref,
                o_ref, m_ref, l_ref):
    width = q_ref.shape[-1]
    rows = q_ref.shape[1]
    scaling = 1.0 / math.sqrt(HD)
    valid = mask_ref[0] != 0
    low = lax.broadcasted_iota(jnp.int32, (rows, LANES), 1) < HD
    for tile in range(width // LANES):
        cols = pl.ds(tile * LANES, LANES)
        q_pair = pair_rows(q_ref[0, :, cols], low)
        k_local = jnp.concatenate([kp_ref[0, :, cols], kc_ref[0, :, cols], kn_ref[0, :, cols]], axis=0)
        v_local = jnp.concatenate([vp_ref[0, :, cols], vc_ref[0, :, cols], vn_ref[0, :, cols]], axis=0)
        near = lax.dot_general(q_pair, k_local, CONTRACT, preferred_element_type=jnp.float32)
        near = jnp.where(valid, near * scaling, -jnp.inf)
        wide = lax.dot_general(q_pair, ks_ref[:, cols], CONTRACT, preferred_element_type=jnp.float32)
        wide = wide * scaling
        peak = jnp.maximum(
            jnp.max(near, axis=-1, keepdims=True), jnp.max(wide, axis=-1, keepdims=True)
        )
        near_exp = jnp.exp(near - peak)
        wide_exp = jnp.exp(wide - peak)
        total = jnp.sum(near_exp, axis=-1, keepdims=True) + jnp.sum(wide_exp, axis=-1, keepdims=True)
        result = jnp.dot(near_exp.astype(jnp.bfloat16), v_local, preferred_element_type=jnp.float32)
        result = result + jnp.dot(
            wide_exp.astype(jnp.bfloat16), vs_ref[:, cols], preferred_element_type=jnp.float32
        )
        o_ref[0, :, cols] = pick_rows(result, low, rows)
        m_ref[0, :, cols] = pick_rows(jnp.broadcast_to(peak, result.shape), low, rows)
        l_ref[0, :, cols] = pick_rows(jnp.broadcast_to(total, result.shape), low, rows)


def far_kernel(ids_ref, mask_ref, q_ref, *refs):
    far_count = RAND
    token_refs = refs[:far_count]
    wk_ref, wv_ref, oa_ref, ma_ref, la_ref, out_ref = refs[far_count:]
    width = q_ref.shape[-1]
    rows = q_ref.shape[1]
    scaling = 1.0 / math.sqrt(HD)
    valid = mask_ref[0] != 0
    low = lax.broadcasted_iota(jnp.int32, (rows, LANES), 1) < HD
    far_tokens = jnp.concatenate([ref[0] for ref in token_refs], axis=0)
    k_far = jnp.dot(far_tokens, wk_ref[...], preferred_element_type=jnp.float32).astype(jnp.bfloat16)
    v_far = jnp.dot(far_tokens, wv_ref[...], preferred_element_type=jnp.float32).astype(jnp.bfloat16)
    for tile in range(width // LANES):
        lanes = slice(tile * LANES, (tile + 1) * LANES)
        cols = pl.ds(tile * LANES, LANES)
        q_pair = pair_rows(q_ref[0, :, cols], low)
        scores = lax.dot_general(q_pair, k_far[:, lanes], CONTRACT, preferred_element_type=jnp.float32)
        scores = jnp.where(valid, scores * scaling, -jnp.inf)
        peak = jnp.max(scores, axis=-1, keepdims=True)
        exps = jnp.exp(scores - peak)
        total = jnp.sum(exps, axis=-1, keepdims=True)
        result = jnp.dot(exps.astype(jnp.bfloat16), v_far[:, lanes], preferred_element_type=jnp.float32)
        o_b = pick_rows(result, low, rows)
        m_b = pick_rows(jnp.broadcast_to(peak, result.shape), low, rows)
        l_b = pick_rows(jnp.broadcast_to(total, result.shape), low, rows)
        m_a = ma_ref[0, :, cols]
        peak_all = jnp.maximum(m_a, m_b)
        scale_a = jnp.exp(m_a - peak_all)
        scale_b = jnp.exp(m_b - peak_all)
        numerator = oa_ref[0, :, cols] * scale_a + o_b * scale_b
        denominator = la_ref[0, :, cols] * scale_a + l_b * scale_b
        out_ref[0, :, cols] = (numerator / denominator).astype(out_ref.dtype)


def attend_near(mask, q, k_ext, v_ext, k_sum, v_sum):
    blocks, rows, width = q.shape
    keys = k_sum.shape[0]
    block = lambda offset: pl.BlockSpec((1, rows, width), lambda i: (i + offset, 0, 0))
    whole = pl.BlockSpec((keys, width), lambda i: (0, 0))
    local_keys = 3 * rows
    heads = width // HD
    flops = blocks * heads * 2 * rows * 2 * LANES * (local_keys + keys)
    bytes_accessed = 2 * (blocks * rows * width * 7 + 2 * keys * width) + 12 * blocks * rows * width
    part = jax.ShapeDtypeStruct((blocks, rows, width), jnp.float32)
    return pl.pallas_call(
        near_kernel,
        grid=(blocks,),
        in_specs=[pl.BlockSpec((1, 1, local_keys), lambda i: (i, 0, 0)), block(0)]
        + [block(0), block(1), block(2)] * 2
        + [whole, whole],
        out_specs=[block(0)] * 3,
        out_shape=[part] * 3,
        cost_estimate=pl.CostEstimate(
            flops=flops,
            transcendentals=blocks * heads * rows * (local_keys + keys),
            bytes_accessed=bytes_accessed,
        ),
    )(mask, q, k_ext, k_ext, k_ext, v_ext, v_ext, v_ext, k_sum, v_sum)


def attend_far(slot_ids, mask, q, incoming, w_k, w_v, o_a, m_a, l_a):
    blocks, rows, width = q.shape
    model_dim = incoming.shape[-1]
    block = pl.BlockSpec((1, rows, width), lambda i, ids: (i, 0, 0))
    token_specs = [
        pl.BlockSpec((1, rows, model_dim), lambda i, ids, j=j: (ids[RAND * i + j], 0, 0))
        for j in range(RAND)
    ]
    weight = pl.BlockSpec(w_k.shape, lambda i, ids: (0, 0))
    local_keys = RAND * rows
    heads = width // HD
    flops = blocks * (
        heads * 2 * rows * 2 * LANES * local_keys + 2 * 2 * local_keys * model_dim * width
    )
    bytes_accessed = 2 * blocks * rows * (width * 2 + model_dim * RAND) + 4 * w_k.size + (
        12 * blocks * rows * width
    )
    grid_spec = pltpu.PrefetchScalarGridSpec(
        num_scalar_prefetch=1,
        grid=(blocks,),
        in_specs=[pl.BlockSpec((1, 1, local_keys), lambda i, ids: (i, 0, 0)), block]
        + token_specs
        + [weight, weight, block, block, block],
        out_specs=block,
    )
    return pl.pallas_call(
        far_kernel,
        grid_spec=grid_spec,
        out_shape=jax.ShapeDtypeStruct((blocks, rows, width), jnp.bfloat16),
        cost_estimate=pl.CostEstimate(
            flops=flops,
            transcendentals=blocks * heads * rows * local_keys,
            bytes_accessed=bytes_accessed,
        ),
    )(slot_ids, mask, q, incoming, incoming, incoming, w_k, w_v, o_a, m_a, l_a)


def local(tokens, w_qkv, w_out, counts, rand_seg, rand_off):
    seq_count = lax.axis_size("seq")
    ctx_count = lax.axis_size("ctx")
    seq_index = lax.axis_index("seq")
    ctx_index = lax.axis_index("ctx")
    dev_count = seq_count * ctx_count
    dev_index = ctx_index * seq_count + seq_index
    tok_rows, model_dim = tokens.shape
    head_total = model_dim // HD
    dev_blocks = tok_rows // BLK
    seg_blocks = dev_blocks * seq_count
    block_total = counts.shape[0]
    capacity = (RAND * dev_blocks + ctx_count - 1) // ctx_count + 1
    first_block = dev_index * dev_blocks
    token_blocks = tokens.reshape(dev_blocks, BLK, model_dim)

    all_owner = rand_seg.reshape(ctx_count, seq_count, dev_blocks * RAND)
    all_offset = rand_off.reshape(ctx_count, seq_count, dev_blocks * RAND)
    col_owner = lax.dynamic_index_in_dim(all_owner, seq_index, axis=1, keepdims=False)
    col_offset = lax.dynamic_index_in_dim(all_offset, seq_index, axis=1, keepdims=False)
    send_off = serve_slots(col_owner, col_offset, ctx_index, capacity)
    outgoing = jnp.take(token_blocks, send_off.reshape(-1), axis=0, mode="clip").reshape(
        ctx_count, capacity, BLK, model_dim
    )
    forward = [(i, i + 1) for i in range(dev_count - 1)]
    backward = [(i + 1, i) for i in range(dev_count - 1)]
    prev_tokens = lax.ppermute(token_blocks[dev_blocks - 1], ("ctx", "seq"), forward)
    next_tokens = lax.ppermute(token_blocks[0], ("ctx", "seq"), backward)

    usable = jnp.arange(BLK, dtype=jnp.int32)[None, :] < lax.dynamic_slice_in_dim(
        counts, first_block, dev_blocks
    )[:, None]
    weighted = jnp.where(usable[:, :, None], token_blocks.astype(jnp.float32), 0.0)
    sums = jnp.sum(weighted, axis=1)
    members = jnp.sum(usable.astype(jnp.float32), axis=1)
    pooled = sums / members[:, None]
    summary = (pooled / jnp.sqrt(jnp.mean(pooled * pooled, axis=1, keepdims=True) + 1e-05)).astype(
        jnp.bfloat16
    )
    summary_seg = lax.all_gather(summary, "seq", axis=0, tiled=True)
    summary_all = lax.all_gather(summary_seg, "ctx", axis=0, tiled=True)
    summary_all, outgoing = lax.optimization_barrier((summary_all, outgoing))
    incoming = lax.all_to_all(outgoing, "ctx", split_axis=0, concat_axis=0, tiled=True)

    w_q, w_k, w_v = split_weights(w_qkv, head_total)
    project = lambda x, w: jnp.dot(x, w, preferred_element_type=jnp.float32).astype(jnp.bfloat16)
    q_own = project(tokens, w_q).reshape(dev_blocks, BLK, model_dim)
    rimmed = jnp.concatenate([prev_tokens, tokens, next_tokens], axis=0)
    k_ext = project(rimmed, w_k).reshape(dev_blocks + 2, BLK, model_dim)
    v_ext = project(rimmed, w_v).reshape(dev_blocks + 2, BLK, model_dim)
    k_sum = project(summary_all, w_k)
    v_sum = project(summary_all, w_v)

    my_owner = lax.dynamic_slice_in_dim(rand_seg, first_block, dev_blocks)
    my_offset = lax.dynamic_slice_in_dim(rand_off, first_block, dev_blocks)
    mine = my_owner.reshape(dev_blocks * RAND)
    slot_ids = mine * capacity + positions_among(mine, ctx_count)

    block_ids = first_block + jnp.arange(dev_blocks, dtype=jnp.int32)
    near_ids = block_ids[:, None] + jnp.arange(-1, 2, dtype=jnp.int32)[None, :]
    existing = (near_ids >= 0) & (near_ids < block_total)
    near_counts = jnp.where(existing, jnp.take(counts, jnp.clip(near_ids, 0, block_total - 1)), 0)
    far_global = my_owner * seg_blocks + seq_index * dev_blocks + my_offset
    far_counts = jnp.take(counts, far_global)
    positions = jnp.arange(BLK, dtype=jnp.int32)[None, None, :]
    near_mask = (positions < near_counts[:, :, None]).astype(jnp.int32).reshape(dev_blocks, 1, -1)
    far_mask = (positions < far_counts[:, :, None]).astype(jnp.int32).reshape(dev_blocks, 1, -1)

    o_a, m_a, l_a = attend_near(near_mask, q_own, k_ext, v_ext, k_sum, v_sum)
    attended = attend_far(
        slot_ids,
        far_mask,
        q_own,
        incoming.reshape(ctx_count * capacity, BLK, model_dim),
        w_k,
        w_v,
        o_a,
        m_a,
        l_a,
    ).reshape(tok_rows, model_dim)
    mixed = tokens.astype(jnp.float32) + jnp.dot(attended, w_out, preferred_element_type=jnp.float32)
    return mixed.astype(jnp.bfloat16)


def solution(mesh):
    in_specs = (P(("ctx", "seq"), None), P(), P(), P(), P(), P())
    out_specs = P(("ctx", "seq"), None)
    return jax.shard_map(local, mesh=mesh, in_specs=in_specs, out_specs=out_specs, check_vma=False)
```

```python
import math

import jax
import jax.numpy as jnp
from jax import lax
from jax.experimental import pallas as pl
from jax.experimental.pallas import tpu as pltpu
from jax.sharding import PartitionSpec as P

HD = 64
BLK = 64
RAND = 3
LANES = 128


def positions_among(owners, owner_count):
    marks = (owners[..., None] == jnp.arange(owner_count, dtype=jnp.int32)).astype(jnp.int32)
    ranks = jnp.cumsum(marks, axis=-2) - 1
    return jnp.sum(ranks * marks, axis=-1)


def serve_slots(owners, offsets, target, capacity):
    matched = owners == target
    ranks = jnp.cumsum(matched.astype(jnp.int32), axis=-1) - 1
    slot_hit = matched[..., None, :] & (
        ranks[..., None, :] == jnp.arange(capacity, dtype=jnp.int32)[:, None]
    )
    return jnp.sum(jnp.where(slot_hit, offsets[..., None, :], 0), axis=-1)


def split_weights(w_qkv, head_total):
    model_dim = w_qkv.shape[0]
    shaped = w_qkv.reshape(model_dim, head_total, 3, HD)
    return [shaped[:, :, j, :].reshape(model_dim, head_total * HD) for j in range(3)]


def pair_rows(q, low):
    blank = jnp.zeros_like(q)
    return jnp.concatenate([jnp.where(low, q, blank), jnp.where(low, blank, q)], axis=0)


def pick_rows(x, low, rows):
    return jnp.where(low, x[:rows], x[rows:])


CONTRACT = (((1,), (1,)), ((), ()))


def near_kernel(mask_ref, q_ref, kp_ref, kc_ref, kn_ref, vp_ref, vc_ref, vn_ref, ks_ref, vs_ref,
                o_ref, m_ref, l_ref):
    width = q_ref.shape[-1]
    rows = q_ref.shape[1]
    scaling = 1.0 / math.sqrt(HD)
    valid = mask_ref[0] != 0
    low = lax.broadcasted_iota(jnp.int32, (rows, LANES), 1) < HD
    for tile in range(width // LANES):
        cols = pl.ds(tile * LANES, LANES)
        q_pair = pair_rows(q_ref[0, :, cols], low)
        k_local = jnp.concatenate([kp_ref[0, :, cols], kc_ref[0, :, cols], kn_ref[0, :, cols]], axis=0)
        v_local = jnp.concatenate([vp_ref[0, :, cols], vc_ref[0, :, cols], vn_ref[0, :, cols]], axis=0)
        near = lax.dot_general(q_pair, k_local, CONTRACT, preferred_element_type=jnp.float32)
        near = jnp.where(valid, near * scaling, -jnp.inf)
        wide = lax.dot_general(q_pair, ks_ref[:, cols], CONTRACT, preferred_element_type=jnp.float32)
        wide = wide * scaling
        peak = jnp.maximum(
            jnp.max(near, axis=-1, keepdims=True), jnp.max(wide, axis=-1, keepdims=True)
        )
        near_exp = jnp.exp(near - peak)
        wide_exp = jnp.exp(wide - peak)
        total = jnp.sum(near_exp, axis=-1, keepdims=True) + jnp.sum(wide_exp, axis=-1, keepdims=True)
        result = jnp.dot(near_exp.astype(jnp.bfloat16), v_local, preferred_element_type=jnp.float32)
        result = result + jnp.dot(
            wide_exp.astype(jnp.bfloat16), vs_ref[:, cols], preferred_element_type=jnp.float32
        )
        o_ref[0, :, cols] = pick_rows(result, low, rows)
        m_ref[0, :, cols] = pick_rows(jnp.broadcast_to(peak, result.shape), low, rows)
        l_ref[0, :, cols] = pick_rows(jnp.broadcast_to(total, result.shape), low, rows)


def far_kernel(ids_ref, mask_ref, q_ref, *refs):
    far_count = RAND
    token_refs = refs[:far_count]
    wk_ref, wv_ref, oa_ref, ma_ref, la_ref, out_ref = refs[far_count:]
    width = q_ref.shape[-1]
    rows = q_ref.shape[1]
    scaling = 1.0 / math.sqrt(HD)
    valid = mask_ref[0] != 0
    low = lax.broadcasted_iota(jnp.int32, (rows, LANES), 1) < HD
    far_tokens = jnp.concatenate([ref[0] for ref in token_refs], axis=0)
    k_far = jnp.dot(far_tokens, wk_ref[...], preferred_element_type=jnp.float32).astype(jnp.bfloat16)
    v_far = jnp.dot(far_tokens, wv_ref[...], preferred_element_type=jnp.float32).astype(jnp.bfloat16)
    for tile in range(width // LANES):
        lanes = slice(tile * LANES, (tile + 1) * LANES)
        cols = pl.ds(tile * LANES, LANES)
        q_pair = pair_rows(q_ref[0, :, cols], low)
        scores = lax.dot_general(q_pair, k_far[:, lanes], CONTRACT, preferred_element_type=jnp.float32)
        scores = jnp.where(valid, scores * scaling, -jnp.inf)
        peak = jnp.max(scores, axis=-1, keepdims=True)
        exps = jnp.exp(scores - peak)
        total = jnp.sum(exps, axis=-1, keepdims=True)
        result = jnp.dot(exps.astype(jnp.bfloat16), v_far[:, lanes], preferred_element_type=jnp.float32)
        o_b = pick_rows(result, low, rows)
        m_b = pick_rows(jnp.broadcast_to(peak, result.shape), low, rows)
        l_b = pick_rows(jnp.broadcast_to(total, result.shape), low, rows)
        m_a = ma_ref[0, :, cols]
        peak_all = jnp.maximum(m_a, m_b)
        scale_a = jnp.exp(m_a - peak_all)
        scale_b = jnp.exp(m_b - peak_all)
        numerator = oa_ref[0, :, cols] * scale_a + o_b * scale_b
        denominator = la_ref[0, :, cols] * scale_a + l_b * scale_b
        out_ref[0, :, cols] = (numerator / denominator).astype(out_ref.dtype)


def attend_near(mask, q, k_ext, v_ext, k_sum, v_sum):
    blocks, rows, width = q.shape
    keys = k_sum.shape[0]
    block = lambda offset: pl.BlockSpec((1, rows, width), lambda i: (i + offset, 0, 0))
    whole = pl.BlockSpec((keys, width), lambda i: (0, 0))
    local_keys = 3 * rows
    heads = width // HD
    flops = blocks * heads * 2 * rows * 2 * LANES * (local_keys + keys)
    bytes_accessed = 2 * (blocks * rows * width * 7 + 2 * keys * width) + 12 * blocks * rows * width
    part = jax.ShapeDtypeStruct((blocks, rows, width), jnp.float32)
    return pl.pallas_call(
        near_kernel,
        grid=(blocks,),
        in_specs=[pl.BlockSpec((1, 1, local_keys), lambda i: (i, 0, 0)), block(0)]
        + [block(0), block(1), block(2)] * 2
        + [whole, whole],
        out_specs=[block(0)] * 3,
        out_shape=[part] * 3,
        cost_estimate=pl.CostEstimate(
            flops=flops,
            transcendentals=blocks * heads * rows * (local_keys + keys),
            bytes_accessed=bytes_accessed,
        ),
    )(mask, q, k_ext, k_ext, k_ext, v_ext, v_ext, v_ext, k_sum, v_sum)


def attend_far(slot_ids, mask, q, incoming, w_k, w_v, o_a, m_a, l_a):
    blocks, rows, width = q.shape
    model_dim = incoming.shape[-1]
    block = pl.BlockSpec((1, rows, width), lambda i, ids: (i, 0, 0))
    token_specs = [
        pl.BlockSpec((1, rows, model_dim), lambda i, ids, j=j: (ids[RAND * i + j], 0, 0))
        for j in range(RAND)
    ]
    weight = pl.BlockSpec(w_k.shape, lambda i, ids: (0, 0))
    local_keys = RAND * rows
    heads = width // HD
    flops = blocks * (
        heads * 2 * rows * 2 * LANES * local_keys + 2 * 2 * local_keys * model_dim * width
    )
    bytes_accessed = 2 * blocks * rows * (width * 2 + model_dim * RAND) + 4 * w_k.size + (
        12 * blocks * rows * width
    )
    grid_spec = pltpu.PrefetchScalarGridSpec(
        num_scalar_prefetch=1,
        grid=(blocks,),
        in_specs=[pl.BlockSpec((1, 1, local_keys), lambda i, ids: (i, 0, 0)), block]
        + token_specs
        + [weight, weight, block, block, block],
        out_specs=block,
    )
    return pl.pallas_call(
        far_kernel,
        grid_spec=grid_spec,
        out_shape=jax.ShapeDtypeStruct((blocks, rows, width), jnp.bfloat16),
        cost_estimate=pl.CostEstimate(
            flops=flops,
            transcendentals=blocks * heads * rows * local_keys,
            bytes_accessed=bytes_accessed,
        ),
    )(slot_ids, mask, q, incoming, incoming, incoming, w_k, w_v, o_a, m_a, l_a)


def local(tokens, w_qkv, w_out, counts, rand_seg, rand_off):
    seq_count = lax.axis_size("seq")
    ctx_count = lax.axis_size("ctx")
    seq_index = lax.axis_index("seq")
    ctx_index = lax.axis_index("ctx")
    dev_count = seq_count * ctx_count
    dev_index = ctx_index * seq_count + seq_index
    tok_rows, model_dim = tokens.shape
    head_total = model_dim // HD
    dev_blocks = tok_rows // BLK
    seg_blocks = dev_blocks * seq_count
    block_total = counts.shape[0]
    capacity = (RAND * dev_blocks + ctx_count - 1) // ctx_count + 1
    first_block = dev_index * dev_blocks
    token_blocks = tokens.reshape(dev_blocks, BLK, model_dim)

    all_owner = rand_seg.reshape(ctx_count, seq_count, dev_blocks * RAND)
    all_offset = rand_off.reshape(ctx_count, seq_count, dev_blocks * RAND)
    col_owner = lax.dynamic_index_in_dim(all_owner, seq_index, axis=1, keepdims=False)
    col_offset = lax.dynamic_index_in_dim(all_offset, seq_index, axis=1, keepdims=False)
    send_off = serve_slots(col_owner, col_offset, ctx_index, capacity)
    outgoing = jnp.take(token_blocks, send_off.reshape(-1), axis=0, mode="clip").reshape(
        ctx_count, capacity, BLK, model_dim
    )
    forward = [(i, i + 1) for i in range(dev_count - 1)]
    backward = [(i + 1, i) for i in range(dev_count - 1)]
    prev_tokens = lax.ppermute(token_blocks[dev_blocks - 1], ("ctx", "seq"), forward)
    next_tokens = lax.ppermute(token_blocks[0], ("ctx", "seq"), backward)

    usable = jnp.arange(BLK, dtype=jnp.int32)[None, :] < lax.dynamic_slice_in_dim(
        counts, first_block, dev_blocks
    )[:, None]
    weighted = jnp.where(usable[:, :, None], token_blocks.astype(jnp.float32), 0.0)
    sums = jnp.sum(weighted, axis=1)
    members = jnp.sum(usable.astype(jnp.float32), axis=1)
    pooled = sums / members[:, None]
    summary = (pooled / jnp.sqrt(jnp.mean(pooled * pooled, axis=1, keepdims=True) + 1e-05)).astype(
        jnp.bfloat16
    )
    copies = jnp.broadcast_to(summary[None], (dev_count,) + summary.shape)
    summary_all = lax.all_to_all(copies, ("ctx", "seq"), 0, 0, tiled=True).reshape(-1, model_dim)
    summary_all, outgoing = lax.optimization_barrier((summary_all, outgoing))
    incoming = lax.all_to_all(outgoing, "ctx", split_axis=0, concat_axis=0, tiled=True)

    w_q, w_k, w_v = split_weights(w_qkv, head_total)
    project = lambda x, w: jnp.dot(x, w, preferred_element_type=jnp.float32).astype(jnp.bfloat16)
    q_own = project(tokens, w_q).reshape(dev_blocks, BLK, model_dim)
    rimmed = jnp.concatenate([prev_tokens, tokens, next_tokens], axis=0)
    k_ext = project(rimmed, w_k).reshape(dev_blocks + 2, BLK, model_dim)
    v_ext = project(rimmed, w_v).reshape(dev_blocks + 2, BLK, model_dim)
    k_sum = project(summary_all, w_k)
    v_sum = project(summary_all, w_v)

    my_owner = lax.dynamic_slice_in_dim(rand_seg, first_block, dev_blocks)
    my_offset = lax.dynamic_slice_in_dim(rand_off, first_block, dev_blocks)
    mine = my_owner.reshape(dev_blocks * RAND)
    slot_ids = mine * capacity + positions_among(mine, ctx_count)

    block_ids = first_block + jnp.arange(dev_blocks, dtype=jnp.int32)
    near_ids = block_ids[:, None] + jnp.arange(-1, 2, dtype=jnp.int32)[None, :]
    existing = (near_ids >= 0) & (near_ids < block_total)
    near_counts = jnp.where(existing, jnp.take(counts, jnp.clip(near_ids, 0, block_total - 1)), 0)
    far_global = my_owner * seg_blocks + seq_index * dev_blocks + my_offset
    far_counts = jnp.take(counts, far_global)
    positions = jnp.arange(BLK, dtype=jnp.int32)[None, None, :]
    near_mask = (positions < near_counts[:, :, None]).astype(jnp.int32).reshape(dev_blocks, 1, -1)
    far_mask = (positions < far_counts[:, :, None]).astype(jnp.int32).reshape(dev_blocks, 1, -1)

    o_a, m_a, l_a = attend_near(near_mask, q_own, k_ext, v_ext, k_sum, v_sum)
    attended = attend_far(
        slot_ids,
        far_mask,
        q_own,
        incoming.reshape(ctx_count * capacity, BLK, model_dim),
        w_k,
        w_v,
        o_a,
        m_a,
        l_a,
    ).reshape(tok_rows, model_dim)
    mixed = tokens.astype(jnp.float32) + jnp.dot(attended, w_out, preferred_element_type=jnp.float32)
    return mixed.astype(jnp.bfloat16)


def solution(mesh):
    in_specs = (P(("ctx", "seq"), None), P(), P(), P(), P(), P())
    out_specs = P(("ctx", "seq"), None)
    return jax.shard_map(local, mesh=mesh, in_specs=in_specs, out_specs=out_specs, check_vma=False)
```

```python
import functools
import math

import jax
import jax.numpy as jnp
from jax import lax
from jax.experimental import pallas as pl
from jax.experimental.pallas import tpu as pltpu
from jax.sharding import PartitionSpec as P

HD = 64
BLK = 64
RAND = 3
LANES = 128


def positions_among(owners, owner_count):
    marks = (owners[..., None] == jnp.arange(owner_count, dtype=jnp.int32)).astype(jnp.int32)
    ranks = jnp.cumsum(marks, axis=-2) - 1
    return jnp.sum(ranks * marks, axis=-1)


def serve_slots(owners, offsets, target, capacity):
    matched = owners == target
    ranks = jnp.cumsum(matched.astype(jnp.int32), axis=-1) - 1
    slot_hit = matched[..., None, :] & (
        ranks[..., None, :] == jnp.arange(capacity, dtype=jnp.int32)[:, None]
    )
    return jnp.sum(jnp.where(slot_hit, offsets[..., None, :], 0), axis=-1)


def split_weights(w_qkv, head_total):
    model_dim = w_qkv.shape[0]
    shaped = w_qkv.reshape(model_dim, head_total, 3, HD)
    return [shaped[:, :, j, :].reshape(model_dim, head_total * HD) for j in range(3)]


def pair_rows(q, low):
    blank = jnp.zeros_like(q)
    return jnp.concatenate([jnp.where(low, q, blank), jnp.where(low, blank, q)], axis=0)


def pick_rows(x, low, rows):
    return jnp.where(low, x[:rows], x[rows:])


CONTRACT = (((1,), (1,)), ((), ()))


def near_kernel(mask_ref, q_ref, kp_ref, kc_ref, kn_ref, vp_ref, vc_ref, vn_ref, ks_ref, vs_ref,
                o_ref, m_ref, l_ref):
    width = q_ref.shape[-1]
    rows = q_ref.shape[1]
    scaling = 1.0 / math.sqrt(HD)
    valid = mask_ref[0] != 0
    low = lax.broadcasted_iota(jnp.int32, (rows, LANES), 1) < HD
    for tile in range(width // LANES):
        cols = pl.ds(tile * LANES, LANES)
        q_pair = pair_rows(q_ref[0, :, cols], low)
        k_local = jnp.concatenate([kp_ref[0, :, cols], kc_ref[0, :, cols], kn_ref[0, :, cols]], axis=0)
        v_local = jnp.concatenate([vp_ref[0, :, cols], vc_ref[0, :, cols], vn_ref[0, :, cols]], axis=0)
        near = lax.dot_general(q_pair, k_local, CONTRACT, preferred_element_type=jnp.float32)
        near = jnp.where(valid, near * scaling, -jnp.inf)
        wide = lax.dot_general(q_pair, ks_ref[:, cols], CONTRACT, preferred_element_type=jnp.float32)
        wide = wide * scaling
        peak = jnp.maximum(
            jnp.max(near, axis=-1, keepdims=True), jnp.max(wide, axis=-1, keepdims=True)
        )
        near_exp = jnp.exp(near - peak)
        wide_exp = jnp.exp(wide - peak)
        total = jnp.sum(near_exp, axis=-1, keepdims=True) + jnp.sum(wide_exp, axis=-1, keepdims=True)
        result = jnp.dot(near_exp.astype(jnp.bfloat16), v_local, preferred_element_type=jnp.float32)
        result = result + jnp.dot(
            wide_exp.astype(jnp.bfloat16), vs_ref[:, cols], preferred_element_type=jnp.float32
        )
        o_ref[0, :, cols] = pick_rows(result, low, rows)
        m_ref[0, :, cols] = pick_rows(jnp.broadcast_to(peak, result.shape), low, rows)
        l_ref[0, :, cols] = pick_rows(jnp.broadcast_to(total, result.shape), low, rows)


def far_kernel(final, ids_ref, mask_ref, q_ref, *refs):
    k_refs = refs[:RAND]
    v_refs = refs[RAND : 2 * RAND]
    oa_ref, ma_ref, la_ref = refs[2 * RAND : 2 * RAND + 3]
    out_refs = refs[2 * RAND + 3 :]
    width = q_ref.shape[-1]
    rows = q_ref.shape[1]
    scaling = 1.0 / math.sqrt(HD)
    valid = mask_ref[0] != 0
    low = lax.broadcasted_iota(jnp.int32, (rows, LANES), 1) < HD
    for tile in range(width // LANES):
        cols = pl.ds(tile * LANES, LANES)
        q_pair = pair_rows(q_ref[0, :, cols], low)
        k_far = jnp.concatenate([ref[0, :, cols] for ref in k_refs], axis=0)
        v_far = jnp.concatenate([ref[0, :, cols] for ref in v_refs], axis=0)
        scores = lax.dot_general(q_pair, k_far, CONTRACT, preferred_element_type=jnp.float32)
        scores = jnp.where(valid, scores * scaling, -jnp.inf)
        peak = jnp.maximum(jnp.max(scores, axis=-1, keepdims=True), -1e30)
        exps = jnp.exp(scores - peak)
        total = jnp.sum(exps, axis=-1, keepdims=True)
        result = jnp.dot(exps.astype(jnp.bfloat16), v_far, preferred_element_type=jnp.float32)
        o_b = pick_rows(result, low, rows)
        m_b = pick_rows(jnp.broadcast_to(peak, result.shape), low, rows)
        l_b = pick_rows(jnp.broadcast_to(total, result.shape), low, rows)
        m_a = ma_ref[0, :, cols]
        peak_all = jnp.maximum(m_a, m_b)
        scale_a = jnp.exp(m_a - peak_all)
        scale_b = jnp.exp(m_b - peak_all)
        numerator = oa_ref[0, :, cols] * scale_a + o_b * scale_b
        denominator = la_ref[0, :, cols] * scale_a + l_b * scale_b
        if final:
            out_refs[0][0, :, cols] = (numerator / denominator).astype(out_refs[0].dtype)
        else:
            out_refs[0][0, :, cols] = numerator
            out_refs[1][0, :, cols] = peak_all
            out_refs[2][0, :, cols] = denominator


def attend_near(mask, q, k_ext, v_ext, k_sum, v_sum):
    blocks, rows, width = q.shape
    keys = k_sum.shape[0]
    block = lambda offset: pl.BlockSpec((1, rows, width), lambda i: (i + offset, 0, 0))
    whole = pl.BlockSpec((keys, width), lambda i: (0, 0))
    local_keys = 3 * rows
    heads = width // HD
    flops = blocks * heads * 2 * rows * 2 * LANES * (local_keys + keys)
    bytes_accessed = 2 * (blocks * rows * width * 7 + 2 * keys * width) + 12 * blocks * rows * width
    part = jax.ShapeDtypeStruct((blocks, rows, width), jnp.float32)
    return pl.pallas_call(
        near_kernel,
        grid=(blocks,),
        in_specs=[pl.BlockSpec((1, 1, local_keys), lambda i: (i, 0, 0)), block(0)]
        + [block(0), block(1), block(2)] * 2
        + [whole, whole],
        out_specs=[block(0)] * 3,
        out_shape=[part] * 3,
        cost_estimate=pl.CostEstimate(
            flops=flops,
            transcendentals=blocks * heads * rows * (local_keys + keys),
            bytes_accessed=bytes_accessed,
        ),
    )(mask, q, k_ext, k_ext, k_ext, v_ext, v_ext, v_ext, k_sum, v_sum)


def attend_far(final, slot_ids, mask, q, k_slots, v_slots, o_a, m_a, l_a):
    blocks, rows, width = q.shape
    block = pl.BlockSpec((1, rows, width), lambda i, ids: (i, 0, 0))
    slot_specs = [
        pl.BlockSpec((1, rows, width), lambda i, ids, j=j: (ids[RAND * i + j], 0, 0))
        for j in range(RAND)
    ]
    local_keys = RAND * rows
    heads = width // HD
    flops = blocks * heads * 2 * rows * 2 * LANES * local_keys
    bytes_accessed = 2 * blocks * rows * width * (2 + 2 * RAND) + 24 * blocks * rows * width
    part = jax.ShapeDtypeStruct((blocks, rows, width), jnp.float32)
    if final:
        out_shape = jax.ShapeDtypeStruct((blocks, rows, width), jnp.bfloat16)
        out_specs = block
    else:
        out_shape = [part] * 3
        out_specs = [block] * 3
    grid_spec = pltpu.PrefetchScalarGridSpec(
        num_scalar_prefetch=1,
        grid=(blocks,),
        in_specs=[pl.BlockSpec((1, 1, local_keys), lambda i, ids: (i, 0, 0)), block]
        + slot_specs * 2
        + [block, block, block],
        out_specs=out_specs,
    )
    return pl.pallas_call(
        functools.partial(far_kernel, final),
        grid_spec=grid_spec,
        out_shape=out_shape,
        cost_estimate=pl.CostEstimate(
            flops=flops,
            transcendentals=blocks * heads * rows * local_keys,
            bytes_accessed=bytes_accessed,
        ),
    )(slot_ids, mask, q, *([k_slots] * RAND), *([v_slots] * RAND), o_a, m_a, l_a)


def local(tokens, w_qkv, w_out, counts, rand_seg, rand_off):
    seq_count = lax.axis_size("seq")
    ctx_count = lax.axis_size("ctx")
    seq_index = lax.axis_index("seq")
    ctx_index = lax.axis_index("ctx")
    dev_count = seq_count * ctx_count
    dev_index = ctx_index * seq_count + seq_index
    tok_rows, model_dim = tokens.shape
    head_total = model_dim // HD
    dev_blocks = tok_rows // BLK
    seg_blocks = dev_blocks * seq_count
    block_total = counts.shape[0]
    capacity = (RAND * dev_blocks + ctx_count - 1) // ctx_count + 1
    first_block = dev_index * dev_blocks
    token_blocks = tokens.reshape(dev_blocks, BLK, model_dim)

    all_owner = rand_seg.reshape(ctx_count, seq_count, dev_blocks * RAND)
    all_offset = rand_off.reshape(ctx_count, seq_count, dev_blocks * RAND)
    col_owner = lax.dynamic_index_in_dim(all_owner, seq_index, axis=1, keepdims=False)
    col_offset = lax.dynamic_index_in_dim(all_offset, seq_index, axis=1, keepdims=False)
    send_off = serve_slots(col_owner, col_offset, ctx_index, capacity)
    outgoing = jnp.take(token_blocks, send_off.reshape(-1), axis=0, mode="clip").reshape(
        ctx_count, capacity, BLK, model_dim
    )
    cap_a = capacity - 1
    forward = [(i, i + 1) for i in range(dev_count - 1)]
    backward = [(i + 1, i) for i in range(dev_count - 1)]
    prev_tokens = lax.ppermute(token_blocks[dev_blocks - 1], ("ctx", "seq"), forward)
    next_tokens = lax.ppermute(token_blocks[0], ("ctx", "seq"), backward)

    usable = jnp.arange(BLK, dtype=jnp.int32)[None, :] < lax.dynamic_slice_in_dim(
        counts, first_block, dev_blocks
    )[:, None]
    weighted = jnp.where(usable[:, :, None], token_blocks.astype(jnp.float32), 0.0)
    sums = jnp.sum(weighted, axis=1)
    members = jnp.sum(usable.astype(jnp.float32), axis=1)
    pooled = sums / members[:, None]
    summary = (pooled / jnp.sqrt(jnp.mean(pooled * pooled, axis=1, keepdims=True) + 1e-05)).astype(
        jnp.bfloat16
    )
    copies = jnp.broadcast_to(summary[None], (dev_count,) + summary.shape)
    summary_all = lax.all_to_all(copies, ("ctx", "seq"), 0, 0, tiled=True).reshape(-1, model_dim)
    summary_all, outgoing = lax.optimization_barrier((summary_all, outgoing))
    incoming_a = lax.all_to_all(outgoing[:, :cap_a], "ctx", split_axis=0, concat_axis=0, tiled=True)

    w_q, w_k, w_v = split_weights(w_qkv, head_total)
    project = lambda x, w: jnp.dot(x, w, preferred_element_type=jnp.float32).astype(jnp.bfloat16)
    q_own = project(tokens, w_q).reshape(dev_blocks, BLK, model_dim)
    rimmed = jnp.concatenate([prev_tokens, tokens, next_tokens], axis=0)
    k_ext = project(rimmed, w_k).reshape(dev_blocks + 2, BLK, model_dim)
    v_ext = project(rimmed, w_v).reshape(dev_blocks + 2, BLK, model_dim)
    k_sum = project(summary_all, w_k)
    v_sum = project(summary_all, w_v)

    my_owner = lax.dynamic_slice_in_dim(rand_seg, first_block, dev_blocks)
    my_offset = lax.dynamic_slice_in_dim(rand_off, first_block, dev_blocks)
    mine = my_owner.reshape(dev_blocks * RAND)
    ranks = positions_among(mine, ctx_count)
    in_a = ranks < cap_a
    ids_a = jnp.where(in_a, mine * cap_a + ranks, 0)
    ids_b = jnp.where(in_a, 0, mine * (capacity - cap_a) + ranks - cap_a)

    block_ids = first_block + jnp.arange(dev_blocks, dtype=jnp.int32)
    near_ids = block_ids[:, None] + jnp.arange(-1, 2, dtype=jnp.int32)[None, :]
    existing = (near_ids >= 0) & (near_ids < block_total)
    near_counts = jnp.where(existing, jnp.take(counts, jnp.clip(near_ids, 0, block_total - 1)), 0)
    far_global = my_owner * seg_blocks + seq_index * dev_blocks + my_offset
    far_counts = jnp.take(counts, far_global)
    positions = jnp.arange(BLK, dtype=jnp.int32)[None, None, :]
    near_mask = (positions < near_counts[:, :, None]).astype(jnp.int32).reshape(dev_blocks, 1, -1)
    far_valid = positions < far_counts[:, :, None]
    chunk_a = in_a.reshape(dev_blocks, RAND)[:, :, None]
    mask_a = (far_valid & chunk_a).astype(jnp.int32).reshape(dev_blocks, 1, -1)
    mask_b = (far_valid & ~chunk_a).astype(jnp.int32).reshape(dev_blocks, 1, -1)

    o_a, m_a, l_a = attend_near(near_mask, q_own, k_ext, v_ext, k_sum, v_sum)
    incoming_a, outgoing_b, o_a, m_a, l_a = lax.optimization_barrier(
        (incoming_a, outgoing[:, cap_a:], o_a, m_a, l_a)
    )
    incoming_b = lax.all_to_all(outgoing_b, "ctx", split_axis=0, concat_axis=0, tiled=True)
    slots_a = incoming_a.reshape(-1, model_dim)
    k_a = project(slots_a, w_k).reshape(-1, BLK, model_dim)
    v_a = project(slots_a, w_v).reshape(-1, BLK, model_dim)
    o_a, m_a, l_a = attend_far(False, ids_a, mask_a, q_own, k_a, v_a, o_a, m_a, l_a)
    slots_b = incoming_b.reshape(-1, model_dim)
    k_b = project(slots_b, w_k).reshape(-1, BLK, model_dim)
    v_b = project(slots_b, w_v).reshape(-1, BLK, model_dim)
    attended = attend_far(True, ids_b, mask_b, q_own, k_b, v_b, o_a, m_a, l_a).reshape(
        tok_rows, model_dim
    )
    mixed = tokens.astype(jnp.float32) + jnp.dot(attended, w_out, preferred_element_type=jnp.float32)
    return mixed.astype(jnp.bfloat16)


def solution(mesh):
    in_specs = (P(("ctx", "seq"), None), P(), P(), P(), P(), P())
    out_specs = P(("ctx", "seq"), None)
    return jax.shard_map(local, mesh=mesh, in_specs=in_specs, out_specs=out_specs, check_vma=False)
```

```python
import functools
import math

import jax
import jax.numpy as jnp
from jax import lax
from jax.experimental import pallas as pl
from jax.experimental.pallas import tpu as pltpu
from jax.sharding import PartitionSpec as P

HD = 64
BLK = 64
RAND = 3
LANES = 128


def positions_among(owners, owner_count):
    marks = (owners[..., None] == jnp.arange(owner_count, dtype=jnp.int32)).astype(jnp.int32)
    ranks = jnp.cumsum(marks, axis=-2) - 1
    return jnp.sum(ranks * marks, axis=-1)


def serve_slots(owners, offsets, target, capacity):
    matched = owners == target
    ranks = jnp.cumsum(matched.astype(jnp.int32), axis=-1) - 1
    slot_hit = matched[..., None, :] & (
        ranks[..., None, :] == jnp.arange(capacity, dtype=jnp.int32)[:, None]
    )
    return jnp.sum(jnp.where(slot_hit, offsets[..., None, :], 0), axis=-1)


def split_weights(w_qkv, head_total):
    model_dim = w_qkv.shape[0]
    shaped = w_qkv.reshape(model_dim, head_total, 3, HD)
    return [shaped[:, :, j, :].reshape(model_dim, head_total * HD) for j in range(3)]


def pair_rows(q, low):
    blank = jnp.zeros_like(q)
    return jnp.concatenate([jnp.where(low, q, blank), jnp.where(low, blank, q)], axis=0)


def pick_rows(x, low, rows):
    return jnp.where(low, x[:rows], x[rows:])


CONTRACT = (((1,), (1,)), ((), ()))


def near_kernel(mask_ref, q_ref, kp_ref, kc_ref, kn_ref, vp_ref, vc_ref, vn_ref, ks_ref, vs_ref,
                o_ref, m_ref, l_ref):
    width = q_ref.shape[-1]
    rows = q_ref.shape[1]
    scaling = 1.0 / math.sqrt(HD)
    valid = mask_ref[0] != 0
    low = lax.broadcasted_iota(jnp.int32, (rows, LANES), 1) < HD
    for tile in range(width // LANES):
        cols = pl.ds(tile * LANES, LANES)
        q_pair = pair_rows(q_ref[0, :, cols], low)
        k_local = jnp.concatenate([kp_ref[0, :, cols], kc_ref[0, :, cols], kn_ref[0, :, cols]], axis=0)
        v_local = jnp.concatenate([vp_ref[0, :, cols], vc_ref[0, :, cols], vn_ref[0, :, cols]], axis=0)
        near = lax.dot_general(q_pair, k_local, CONTRACT, preferred_element_type=jnp.float32)
        near = jnp.where(valid, near * scaling, -jnp.inf)
        wide = lax.dot_general(q_pair, ks_ref[:, cols], CONTRACT, preferred_element_type=jnp.float32)
        wide = wide * scaling
        peak = jnp.maximum(
            jnp.max(near, axis=-1, keepdims=True), jnp.max(wide, axis=-1, keepdims=True)
        )
        near_exp = jnp.exp(near - peak)
        wide_exp = jnp.exp(wide - peak)
        total = jnp.sum(near_exp, axis=-1, keepdims=True) + jnp.sum(wide_exp, axis=-1, keepdims=True)
        result = jnp.dot(near_exp.astype(jnp.bfloat16), v_local, preferred_element_type=jnp.float32)
        result = result + jnp.dot(
            wide_exp.astype(jnp.bfloat16), vs_ref[:, cols], preferred_element_type=jnp.float32
        )
        o_ref[0, :, cols] = pick_rows(result, low, rows)
        m_ref[0, :, cols] = pick_rows(jnp.broadcast_to(peak, result.shape), low, rows)
        l_ref[0, :, cols] = pick_rows(jnp.broadcast_to(total, result.shape), low, rows)


def far_kernel(group, ids_ref, mask_ref, q_ref, *refs):
    token_refs = refs[: group * RAND]
    wkv_ref, oa_ref, ma_ref, la_ref, out_ref = refs[group * RAND :]
    width = q_ref.shape[-1]
    rows = q_ref.shape[1]
    scaling = 1.0 / math.sqrt(HD)
    low = lax.broadcasted_iota(jnp.int32, (rows, LANES), 1) < HD
    far_tokens = jnp.concatenate([ref[0] for ref in token_refs], axis=0)
    kv_far = jnp.dot(far_tokens, wkv_ref[...], preferred_element_type=jnp.float32).astype(
        jnp.bfloat16
    )
    keys = RAND * rows
    for g in range(group):
        valid = mask_ref[g] != 0
        kv_rows = kv_far[g * keys : (g + 1) * keys]
        for tile in range(width // LANES):
            lanes = slice(tile * LANES, (tile + 1) * LANES)
            value_lanes = slice(width + tile * LANES, width + (tile + 1) * LANES)
            cols = pl.ds(tile * LANES, LANES)
            q_pair = pair_rows(q_ref[g, :, cols], low)
            scores = lax.dot_general(
                q_pair, kv_rows[:, lanes], CONTRACT, preferred_element_type=jnp.float32
            )
            scores = jnp.where(valid, scores * scaling, -jnp.inf)
            peak = jnp.max(scores, axis=-1, keepdims=True)
            exps = jnp.exp(scores - peak)
            total = jnp.sum(exps, axis=-1, keepdims=True)
            result = jnp.dot(
                exps.astype(jnp.bfloat16), kv_rows[:, value_lanes], preferred_element_type=jnp.float32
            )
            o_b = pick_rows(result, low, rows)
            m_b = pick_rows(jnp.broadcast_to(peak, result.shape), low, rows)
            l_b = pick_rows(jnp.broadcast_to(total, result.shape), low, rows)
            m_a = ma_ref[g, :, cols]
            peak_all = jnp.maximum(m_a, m_b)
            scale_a = jnp.exp(m_a - peak_all)
            scale_b = jnp.exp(m_b - peak_all)
            numerator = oa_ref[g, :, cols] * scale_a + o_b * scale_b
            denominator = la_ref[g, :, cols] * scale_a + l_b * scale_b
            out_ref[g, :, cols] = (numerator / denominator).astype(out_ref.dtype)


def attend_near(mask, q, k_ext, v_ext, k_sum, v_sum):
    blocks, rows, width = q.shape
    keys = k_sum.shape[0]
    block = lambda offset: pl.BlockSpec((1, rows, width), lambda i: (i + offset, 0, 0))
    whole = pl.BlockSpec((keys, width), lambda i: (0, 0))
    local_keys = 3 * rows
    heads = width // HD
    flops = blocks * heads * 2 * rows * 2 * LANES * (local_keys + keys)
    bytes_accessed = 2 * (blocks * rows * width * 7 + 2 * keys * width) + 12 * blocks * rows * width
    part = jax.ShapeDtypeStruct((blocks, rows, width), jnp.float32)
    return pl.pallas_call(
        near_kernel,
        grid=(blocks,),
        in_specs=[pl.BlockSpec((1, 1, local_keys), lambda i: (i, 0, 0)), block(0)]
        + [block(0), block(1), block(2)] * 2
        + [whole, whole],
        out_specs=[block(0)] * 3,
        out_shape=[part] * 3,
        cost_estimate=pl.CostEstimate(
            flops=flops,
            transcendentals=blocks * heads * rows * (local_keys + keys),
            bytes_accessed=bytes_accessed,
        ),
    )(mask, q, k_ext, k_ext, k_ext, v_ext, v_ext, v_ext, k_sum, v_sum)


def attend_far(slot_ids, mask, q, incoming, w_kv, o_a, m_a, l_a):
    blocks, rows, width = q.shape
    model_dim = incoming.shape[-1]
    group = 2 if blocks % 2 == 0 else 1
    block = pl.BlockSpec((group, rows, width), lambda i, ids: (i, 0, 0))
    token_specs = [
        pl.BlockSpec(
            (1, rows, model_dim), lambda i, ids, n=n: (ids[RAND * group * i + n], 0, 0)
        )
        for n in range(group * RAND)
    ]
    weight = pl.BlockSpec(w_kv.shape, lambda i, ids: (0, 0))
    local_keys = RAND * rows
    heads = width // HD
    flops = blocks * (
        heads * 2 * rows * 2 * LANES * local_keys + 2 * local_keys * model_dim * 2 * width
    )
    bytes_accessed = 2 * blocks * rows * (width * 2 + model_dim * RAND) + 2 * w_kv.size + (
        12 * blocks * rows * width
    )
    grid_spec = pltpu.PrefetchScalarGridSpec(
        num_scalar_prefetch=1,
        grid=(blocks // group,),
        in_specs=[pl.BlockSpec((group, 1, local_keys), lambda i, ids: (i, 0, 0)), block]
        + token_specs
        + [weight, block, block, block],
        out_specs=block,
    )
    return pl.pallas_call(
        functools.partial(far_kernel, group),
        grid_spec=grid_spec,
        out_shape=jax.ShapeDtypeStruct((blocks, rows, width), jnp.bfloat16),
        cost_estimate=pl.CostEstimate(
            flops=flops,
            transcendentals=blocks * heads * rows * local_keys,
            bytes_accessed=bytes_accessed,
        ),
    )(slot_ids, mask, q, *([incoming] * (group * RAND)), w_kv, o_a, m_a, l_a)


def local(tokens, w_qkv, w_out, counts, rand_seg, rand_off):
    seq_count = lax.axis_size("seq")
    ctx_count = lax.axis_size("ctx")
    seq_index = lax.axis_index("seq")
    ctx_index = lax.axis_index("ctx")
    dev_count = seq_count * ctx_count
    dev_index = ctx_index * seq_count + seq_index
    tok_rows, model_dim = tokens.shape
    head_total = model_dim // HD
    dev_blocks = tok_rows // BLK
    seg_blocks = dev_blocks * seq_count
    block_total = counts.shape[0]
    capacity = (RAND * dev_blocks + ctx_count - 1) // ctx_count + 1
    first_block = dev_index * dev_blocks
    token_blocks = tokens.reshape(dev_blocks, BLK, model_dim)

    all_owner = rand_seg.reshape(ctx_count, seq_count, dev_blocks * RAND)
    all_offset = rand_off.reshape(ctx_count, seq_count, dev_blocks * RAND)
    col_owner = lax.dynamic_index_in_dim(all_owner, seq_index, axis=1, keepdims=False)
    col_offset = lax.dynamic_index_in_dim(all_offset, seq_index, axis=1, keepdims=False)
    send_off = serve_slots(col_owner, col_offset, ctx_index, capacity)
    outgoing = jnp.take(token_blocks, send_off.reshape(-1), axis=0, mode="clip").reshape(
        ctx_count, capacity, BLK, model_dim
    )
    forward = [(i, i + 1) for i in range(dev_count - 1)]
    backward = [(i + 1, i) for i in range(dev_count - 1)]
    prev_tokens = lax.ppermute(token_blocks[dev_blocks - 1], ("ctx", "seq"), forward)
    next_tokens = lax.ppermute(token_blocks[0], ("ctx", "seq"), backward)

    usable = jnp.arange(BLK, dtype=jnp.int32)[None, :] < lax.dynamic_slice_in_dim(
        counts, first_block, dev_blocks
    )[:, None]
    weighted = jnp.where(usable[:, :, None], token_blocks.astype(jnp.float32), 0.0)
    sums = jnp.sum(weighted, axis=1)
    members = jnp.sum(usable.astype(jnp.float32), axis=1)
    pooled = sums / members[:, None]
    summary = (pooled / jnp.sqrt(jnp.mean(pooled * pooled, axis=1, keepdims=True) + 1e-05)).astype(
        jnp.bfloat16
    )
    copies = jnp.broadcast_to(summary[None], (dev_count,) + summary.shape)
    summary_all = lax.all_to_all(copies, ("ctx", "seq"), 0, 0, tiled=True).reshape(-1, model_dim)
    summary_all, outgoing = lax.optimization_barrier((summary_all, outgoing))
    incoming = lax.all_to_all(outgoing, "ctx", split_axis=0, concat_axis=0, tiled=True)

    w_q, w_k, w_v = split_weights(w_qkv, head_total)
    project = lambda x, w: jnp.dot(x, w, preferred_element_type=jnp.float32).astype(jnp.bfloat16)
    q_own = project(tokens, w_q).reshape(dev_blocks, BLK, model_dim)
    rimmed = jnp.concatenate([prev_tokens, tokens, next_tokens], axis=0)
    k_ext = project(rimmed, w_k).reshape(dev_blocks + 2, BLK, model_dim)
    v_ext = project(rimmed, w_v).reshape(dev_blocks + 2, BLK, model_dim)
    k_sum = project(summary_all, w_k)
    v_sum = project(summary_all, w_v)

    my_owner = lax.dynamic_slice_in_dim(rand_seg, first_block, dev_blocks)
    my_offset = lax.dynamic_slice_in_dim(rand_off, first_block, dev_blocks)
    mine = my_owner.reshape(dev_blocks * RAND)
    slot_ids = mine * capacity + positions_among(mine, ctx_count)

    block_ids = first_block + jnp.arange(dev_blocks, dtype=jnp.int32)
    near_ids = block_ids[:, None] + jnp.arange(-1, 2, dtype=jnp.int32)[None, :]
    existing = (near_ids >= 0) & (near_ids < block_total)
    near_counts = jnp.where(existing, jnp.take(counts, jnp.clip(near_ids, 0, block_total - 1)), 0)
    far_global = my_owner * seg_blocks + seq_index * dev_blocks + my_offset
    far_counts = jnp.take(counts, far_global)
    positions = jnp.arange(BLK, dtype=jnp.int32)[None, None, :]
    near_mask = (positions < near_counts[:, :, None]).astype(jnp.int32).reshape(dev_blocks, 1, -1)
    far_mask = (positions < far_counts[:, :, None]).astype(jnp.int32).reshape(dev_blocks, 1, -1)

    o_a, m_a, l_a = attend_near(near_mask, q_own, k_ext, v_ext, k_sum, v_sum)
    attended = attend_far(
        slot_ids,
        far_mask,
        q_own,
        incoming.reshape(ctx_count * capacity, BLK, model_dim),
        jnp.concatenate([w_k, w_v], axis=1),
        o_a,
        m_a,
        l_a,
    ).reshape(tok_rows, model_dim)
    mixed = tokens.astype(jnp.float32) + jnp.dot(attended, w_out, preferred_element_type=jnp.float32)
    return mixed.astype(jnp.bfloat16)


def solution(mesh):
    in_specs = (P(("ctx", "seq"), None), P(), P(), P(), P(), P())
    out_specs = P(("ctx", "seq"), None)
    return jax.shard_map(local, mesh=mesh, in_specs=in_specs, out_specs=out_specs, check_vma=False)
```

```python
import functools
import math

import jax
import jax.numpy as jnp
from jax import lax
from jax.experimental import pallas as pl
from jax.experimental.pallas import tpu as pltpu
from jax.sharding import PartitionSpec as P

HD = 64
BLK = 64
RAND = 3
LANES = 128


def positions_among(owners, owner_count):
    marks = (owners[..., None] == jnp.arange(owner_count, dtype=jnp.int32)).astype(jnp.int32)
    ranks = jnp.cumsum(marks, axis=-2) - 1
    return jnp.sum(ranks * marks, axis=-1)


def serve_slots(owners, offsets, target, capacity):
    matched = owners == target
    ranks = jnp.cumsum(matched.astype(jnp.int32), axis=-1) - 1
    slot_hit = matched[..., None, :] & (
        ranks[..., None, :] == jnp.arange(capacity, dtype=jnp.int32)[:, None]
    )
    return jnp.sum(jnp.where(slot_hit, offsets[..., None, :], 0), axis=-1)


def split_weights(w_qkv, head_total):
    model_dim = w_qkv.shape[0]
    shaped = w_qkv.reshape(model_dim, head_total, 3, HD)
    return [shaped[:, :, j, :].reshape(model_dim, head_total * HD) for j in range(3)]


def pair_rows(q, low):
    blank = jnp.zeros_like(q)
    return jnp.concatenate([jnp.where(low, q, blank), jnp.where(low, blank, q)], axis=0)


def pick_rows(x, low, rows):
    return jnp.where(low, x[:rows], x[rows:])


CONTRACT = (((1,), (1,)), ((), ()))


def near_kernel(mask_ref, q_ref, kp_ref, kc_ref, kn_ref, vp_ref, vc_ref, vn_ref, ks_ref, vs_ref,
                o_ref, m_ref, l_ref):
    width = q_ref.shape[-1]
    rows = q_ref.shape[1]
    scaling = 1.0 / math.sqrt(HD)
    valid = mask_ref[0] != 0
    low = lax.broadcasted_iota(jnp.int32, (rows, LANES), 1) < HD
    for tile in range(width // LANES):
        cols = pl.ds(tile * LANES, LANES)
        q_pair = pair_rows(q_ref[0, :, cols], low)
        k_local = jnp.concatenate([kp_ref[0, :, cols], kc_ref[0, :, cols], kn_ref[0, :, cols]], axis=0)
        v_local = jnp.concatenate([vp_ref[0, :, cols], vc_ref[0, :, cols], vn_ref[0, :, cols]], axis=0)
        near = lax.dot_general(q_pair, k_local, CONTRACT, preferred_element_type=jnp.float32)
        near = jnp.where(valid, near * scaling, -jnp.inf)
        wide = lax.dot_general(q_pair, ks_ref[:, cols], CONTRACT, preferred_element_type=jnp.float32)
        wide = wide * scaling
        peak = jnp.maximum(
            jnp.max(near, axis=-1, keepdims=True), jnp.max(wide, axis=-1, keepdims=True)
        )
        near_exp = jnp.exp(near - peak)
        wide_exp = jnp.exp(wide - peak)
        total = jnp.sum(near_exp, axis=-1, keepdims=True) + jnp.sum(wide_exp, axis=-1, keepdims=True)
        result = jnp.dot(near_exp.astype(jnp.bfloat16), v_local, preferred_element_type=jnp.float32)
        result = result + jnp.dot(
            wide_exp.astype(jnp.bfloat16), vs_ref[:, cols], preferred_element_type=jnp.float32
        )
        o_ref[0, :, cols] = pick_rows(result, low, rows)
        m_ref[0, :, cols] = pick_rows(jnp.broadcast_to(peak, result.shape), low, rows)
        l_ref[0, :, cols] = pick_rows(jnp.broadcast_to(total, result.shape), low, rows)


def far_kernel(ids_ref, mask_ref, q_ref, *refs):
    token_refs = refs[:RAND]
    wkv_ref, oa_ref, ma_ref, la_ref, out_ref, kv_ref = refs[RAND:]
    width = q_ref.shape[-1]
    rows = q_ref.shape[1]
    scaling = 1.0 / math.sqrt(HD)
    low = lax.broadcasted_iota(jnp.int32, (rows, LANES), 1) < HD

    @pl.when(pl.program_id(0) == 0)
    def _():
        kv_ref[...] = jnp.zeros_like(kv_ref)

    valid = mask_ref[0] != 0
    for tile in range(width // LANES):
        lanes = pl.ds(tile * LANES, LANES)
        value_lanes = pl.ds(width + tile * LANES, LANES)
        q_pair = pair_rows(q_ref[0, :, lanes], low)
        scores = lax.dot_general(
            q_pair, kv_ref[:, lanes], CONTRACT, preferred_element_type=jnp.float32
        )
        scores = jnp.where(valid, scores * scaling, -jnp.inf)
        peak = jnp.max(scores, axis=-1, keepdims=True)
        exps = jnp.exp(scores - peak)
        total = jnp.sum(exps, axis=-1, keepdims=True)
        result = jnp.dot(
            exps.astype(jnp.bfloat16), kv_ref[:, value_lanes], preferred_element_type=jnp.float32
        )
        o_b = pick_rows(result, low, rows)
        m_b = pick_rows(jnp.broadcast_to(peak, result.shape), low, rows)
        l_b = pick_rows(jnp.broadcast_to(total, result.shape), low, rows)
        m_a = ma_ref[0, :, lanes]
        peak_all = jnp.maximum(m_a, m_b)
        scale_a = jnp.exp(m_a - peak_all)
        scale_b = jnp.exp(m_b - peak_all)
        numerator = oa_ref[0, :, lanes] * scale_a + o_b * scale_b
        denominator = la_ref[0, :, lanes] * scale_a + l_b * scale_b
        out_ref[0, :, lanes] = (numerator / denominator).astype(out_ref.dtype)

    far_tokens = jnp.concatenate([ref[0] for ref in token_refs], axis=0)
    kv_ref[...] = jnp.dot(far_tokens, wkv_ref[...], preferred_element_type=jnp.float32).astype(
        kv_ref.dtype
    )


def attend_near(mask, q, k_ext, v_ext, k_sum, v_sum):
    blocks, rows, width = q.shape
    keys = k_sum.shape[0]
    block = lambda offset: pl.BlockSpec((1, rows, width), lambda i: (i + offset, 0, 0))
    whole = pl.BlockSpec((keys, width), lambda i: (0, 0))
    local_keys = 3 * rows
    heads = width // HD
    flops = blocks * heads * 2 * rows * 2 * LANES * (local_keys + keys)
    bytes_accessed = 2 * (blocks * rows * width * 7 + 2 * keys * width) + 12 * blocks * rows * width
    part = jax.ShapeDtypeStruct((blocks, rows, width), jnp.float32)
    return pl.pallas_call(
        near_kernel,
        grid=(blocks,),
        in_specs=[pl.BlockSpec((1, 1, local_keys), lambda i: (i, 0, 0)), block(0)]
        + [block(0), block(1), block(2)] * 2
        + [whole, whole],
        out_specs=[block(0)] * 3,
        out_shape=[part] * 3,
        cost_estimate=pl.CostEstimate(
            flops=flops,
            transcendentals=blocks * heads * rows * (local_keys + keys),
            bytes_accessed=bytes_accessed,
        ),
    )(mask, q, k_ext, k_ext, k_ext, v_ext, v_ext, v_ext, k_sum, v_sum)


def attend_far(slot_ids, mask, q, incoming, w_kv, o_a, m_a, l_a):
    blocks, rows, width = q.shape
    model_dim = incoming.shape[-1]
    behind = lambda i: jnp.maximum(i - 1, 0)
    block = pl.BlockSpec((1, rows, width), lambda i, ids: (behind(i), 0, 0))
    token_specs = [
        pl.BlockSpec(
            (1, rows, model_dim),
            lambda i, ids, j=j: (ids[RAND * jnp.minimum(i, blocks - 1) + j], 0, 0),
        )
        for j in range(RAND)
    ]
    weight = pl.BlockSpec(w_kv.shape, lambda i, ids: (0, 0))
    local_keys = RAND * rows
    heads = width // HD
    flops = blocks * (
        heads * 2 * rows * 2 * LANES * local_keys + 2 * local_keys * model_dim * 2 * width
    )
    bytes_accessed = 2 * blocks * rows * (width * 2 + model_dim * RAND) + 2 * w_kv.size + (
        12 * blocks * rows * width
    )
    grid_spec = pltpu.PrefetchScalarGridSpec(
        num_scalar_prefetch=1,
        grid=(blocks + 1,),
        in_specs=[pl.BlockSpec((1, 1, local_keys), lambda i, ids: (behind(i), 0, 0)), block]
        + token_specs
        + [weight, block, block, block],
        out_specs=block,
        scratch_shapes=[pltpu.VMEM((local_keys, 2 * width), jnp.bfloat16)],
    )
    return pl.pallas_call(
        far_kernel,
        grid_spec=grid_spec,
        out_shape=jax.ShapeDtypeStruct((blocks, rows, width), jnp.bfloat16),
        cost_estimate=pl.CostEstimate(
            flops=flops,
            transcendentals=blocks * heads * rows * local_keys,
            bytes_accessed=bytes_accessed,
        ),
    )(slot_ids, mask, q, *([incoming] * RAND), w_kv, o_a, m_a, l_a)


def local(tokens, w_qkv, w_out, counts, rand_seg, rand_off):
    seq_count = lax.axis_size("seq")
    ctx_count = lax.axis_size("ctx")
    seq_index = lax.axis_index("seq")
    ctx_index = lax.axis_index("ctx")
    dev_count = seq_count * ctx_count
    dev_index = ctx_index * seq_count + seq_index
    tok_rows, model_dim = tokens.shape
    head_total = model_dim // HD
    dev_blocks = tok_rows // BLK
    seg_blocks = dev_blocks * seq_count
    block_total = counts.shape[0]
    capacity = (RAND * dev_blocks + ctx_count - 1) // ctx_count + 1
    first_block = dev_index * dev_blocks
    token_blocks = tokens.reshape(dev_blocks, BLK, model_dim)

    all_owner = rand_seg.reshape(ctx_count, seq_count, dev_blocks * RAND)
    all_offset = rand_off.reshape(ctx_count, seq_count, dev_blocks * RAND)
    col_owner = lax.dynamic_index_in_dim(all_owner, seq_index, axis=1, keepdims=False)
    col_offset = lax.dynamic_index_in_dim(all_offset, seq_index, axis=1, keepdims=False)
    send_off = serve_slots(col_owner, col_offset, ctx_index, capacity)
    outgoing = jnp.take(token_blocks, send_off.reshape(-1), axis=0, mode="clip").reshape(
        ctx_count, capacity, BLK, model_dim
    )
    forward = [(i, i + 1) for i in range(dev_count - 1)]
    backward = [(i + 1, i) for i in range(dev_count - 1)]
    prev_tokens = lax.ppermute(token_blocks[dev_blocks - 1], ("ctx", "seq"), forward)
    next_tokens = lax.ppermute(token_blocks[0], ("ctx", "seq"), backward)

    usable = jnp.arange(BLK, dtype=jnp.int32)[None, :] < lax.dynamic_slice_in_dim(
        counts, first_block, dev_blocks
    )[:, None]
    weighted = jnp.where(usable[:, :, None], token_blocks.astype(jnp.float32), 0.0)
    sums = jnp.sum(weighted, axis=1)
    members = jnp.sum(usable.astype(jnp.float32), axis=1)
    pooled = sums / members[:, None]
    summary = (pooled / jnp.sqrt(jnp.mean(pooled * pooled, axis=1, keepdims=True) + 1e-05)).astype(
        jnp.bfloat16
    )
    copies = jnp.broadcast_to(summary[None], (dev_count,) + summary.shape)
    summary_all = lax.all_to_all(copies, ("ctx", "seq"), 0, 0, tiled=True).reshape(-1, model_dim)
    summary_all, outgoing = lax.optimization_barrier((summary_all, outgoing))
    incoming = lax.all_to_all(outgoing, "ctx", split_axis=0, concat_axis=0, tiled=True)

    w_q, w_k, w_v = split_weights(w_qkv, head_total)
    project = lambda x, w: jnp.dot(x, w, preferred_element_type=jnp.float32).astype(jnp.bfloat16)
    q_own = project(tokens, w_q).reshape(dev_blocks, BLK, model_dim)
    rimmed = jnp.concatenate([prev_tokens, tokens, next_tokens], axis=0)
    k_ext = project(rimmed, w_k).reshape(dev_blocks + 2, BLK, model_dim)
    v_ext = project(rimmed, w_v).reshape(dev_blocks + 2, BLK, model_dim)
    k_sum = project(summary_all, w_k)
    v_sum = project(summary_all, w_v)

    my_owner = lax.dynamic_slice_in_dim(rand_seg, first_block, dev_blocks)
    my_offset = lax.dynamic_slice_in_dim(rand_off, first_block, dev_blocks)
    mine = my_owner.reshape(dev_blocks * RAND)
    slot_ids = mine * capacity + positions_among(mine, ctx_count)

    block_ids = first_block + jnp.arange(dev_blocks, dtype=jnp.int32)
    near_ids = block_ids[:, None] + jnp.arange(-1, 2, dtype=jnp.int32)[None, :]
    existing = (near_ids >= 0) & (near_ids < block_total)
    near_counts = jnp.where(existing, jnp.take(counts, jnp.clip(near_ids, 0, block_total - 1)), 0)
    far_global = my_owner * seg_blocks + seq_index * dev_blocks + my_offset
    far_counts = jnp.take(counts, far_global)
    positions = jnp.arange(BLK, dtype=jnp.int32)[None, None, :]
    near_mask = (positions < near_counts[:, :, None]).astype(jnp.int32).reshape(dev_blocks, 1, -1)
    far_mask = (positions < far_counts[:, :, None]).astype(jnp.int32).reshape(dev_blocks, 1, -1)

    o_a, m_a, l_a = attend_near(near_mask, q_own, k_ext, v_ext, k_sum, v_sum)
    attended = attend_far(
        slot_ids,
        far_mask,
        q_own,
        incoming.reshape(ctx_count * capacity, BLK, model_dim),
        jnp.concatenate([w_k, w_v], axis=1),
        o_a,
        m_a,
        l_a,
    ).reshape(tok_rows, model_dim)
    mixed = tokens.astype(jnp.float32) + jnp.dot(attended, w_out, preferred_element_type=jnp.float32)
    return mixed.astype(jnp.bfloat16)


def solution(mesh):
    in_specs = (P(("ctx", "seq"), None), P(), P(), P(), P(), P())
    out_specs = P(("ctx", "seq"), None)
    return jax.shard_map(local, mesh=mesh, in_specs=in_specs, out_specs=out_specs, check_vma=False)
```

```python
import functools
import math

import jax
import jax.numpy as jnp
from jax import lax
from jax.experimental import pallas as pl
from jax.experimental.pallas import tpu as pltpu
from jax.sharding import PartitionSpec as P

HD = 64
BLK = 64
RAND = 3
LANES = 128


def positions_among(owners, owner_count):
    marks = (owners[..., None] == jnp.arange(owner_count, dtype=jnp.int32)).astype(jnp.int32)
    ranks = jnp.cumsum(marks, axis=-2) - 1
    return jnp.sum(ranks * marks, axis=-1)


def serve_slots(owners, offsets, target, capacity):
    matched = owners == target
    ranks = jnp.cumsum(matched.astype(jnp.int32), axis=-1) - 1
    slot_hit = matched[..., None, :] & (
        ranks[..., None, :] == jnp.arange(capacity, dtype=jnp.int32)[:, None]
    )
    return jnp.sum(jnp.where(slot_hit, offsets[..., None, :], 0), axis=-1)


def ring_gather(x, axis):
    count = lax.axis_size(axis)
    pieces = [x] + [
        lax.ppermute(x, axis, [(i, (i + shift) % count) for i in range(count)])
        for shift in range(1, count)
    ]
    order = (lax.axis_index(axis) - jnp.arange(count, dtype=jnp.int32)) % count
    return jnp.take(jnp.stack(pieces), order, axis=0, mode="clip").reshape(-1, x.shape[-1])


def split_weights(w_qkv, head_total):
    model_dim = w_qkv.shape[0]
    shaped = w_qkv.reshape(model_dim, head_total, 3, HD)
    return [shaped[:, :, j, :].reshape(model_dim, head_total * HD) for j in range(3)]


def pair_rows(q, low):
    blank = jnp.zeros_like(q)
    return jnp.concatenate([jnp.where(low, q, blank), jnp.where(low, blank, q)], axis=0)


def pick_rows(x, low, rows):
    return jnp.where(low, x[:rows], x[rows:])


CONTRACT = (((1,), (1,)), ((), ()))


def near_kernel(mask_ref, q_ref, kp_ref, kc_ref, kn_ref, vp_ref, vc_ref, vn_ref, ks_ref, vs_ref,
                o_ref, m_ref, l_ref):
    width = q_ref.shape[-1]
    rows = q_ref.shape[1]
    scaling = 1.0 / math.sqrt(HD)
    valid = mask_ref[0] != 0
    low = lax.broadcasted_iota(jnp.int32, (rows, LANES), 1) < HD
    for tile in range(width // LANES):
        cols = pl.ds(tile * LANES, LANES)
        q_pair = pair_rows(q_ref[0, :, cols], low)
        k_local = jnp.concatenate([kp_ref[0, :, cols], kc_ref[0, :, cols], kn_ref[0, :, cols]], axis=0)
        v_local = jnp.concatenate([vp_ref[0, :, cols], vc_ref[0, :, cols], vn_ref[0, :, cols]], axis=0)
        near = lax.dot_general(q_pair, k_local, CONTRACT, preferred_element_type=jnp.float32)
        near = jnp.where(valid, near * scaling, -jnp.inf)
        wide = lax.dot_general(q_pair, ks_ref[:, cols], CONTRACT, preferred_element_type=jnp.float32)
        wide = wide * scaling
        peak = jnp.maximum(
            jnp.max(near, axis=-1, keepdims=True), jnp.max(wide, axis=-1, keepdims=True)
        )
        near_exp = jnp.exp(near - peak)
        wide_exp = jnp.exp(wide - peak)
        total = jnp.sum(near_exp, axis=-1, keepdims=True) + jnp.sum(wide_exp, axis=-1, keepdims=True)
        result = jnp.dot(near_exp.astype(jnp.bfloat16), v_local, preferred_element_type=jnp.float32)
        result = result + jnp.dot(
            wide_exp.astype(jnp.bfloat16), vs_ref[:, cols], preferred_element_type=jnp.float32
        )
        o_ref[0, :, cols] = pick_rows(result, low, rows)
        m_ref[0, :, cols] = pick_rows(jnp.broadcast_to(peak, result.shape), low, rows)
        l_ref[0, :, cols] = pick_rows(jnp.broadcast_to(total, result.shape), low, rows)


def far_kernel(group, ids_ref, mask_ref, q_ref, *refs):
    token_refs = refs[: group * RAND]
    wkv_ref, oa_ref, ma_ref, la_ref, out_ref = refs[group * RAND :]
    width = q_ref.shape[-1]
    rows = q_ref.shape[1]
    scaling = 1.0 / math.sqrt(HD)
    low = lax.broadcasted_iota(jnp.int32, (rows, LANES), 1) < HD
    far_tokens = jnp.concatenate([ref[0] for ref in token_refs], axis=0)
    kv_far = jnp.dot(far_tokens, wkv_ref[...], preferred_element_type=jnp.float32).astype(
        jnp.bfloat16
    )
    keys = RAND * rows
    for g in range(group):
        valid = mask_ref[g] != 0
        kv_rows = kv_far[g * keys : (g + 1) * keys]
        for tile in range(width // LANES):
            lanes = slice(tile * LANES, (tile + 1) * LANES)
            value_lanes = slice(width + tile * LANES, width + (tile + 1) * LANES)
            cols = pl.ds(tile * LANES, LANES)
            q_pair = pair_rows(q_ref[g, :, cols], low)
            scores = lax.dot_general(
                q_pair, kv_rows[:, lanes], CONTRACT, preferred_element_type=jnp.float32
            )
            scores = jnp.where(valid, scores * scaling, -jnp.inf)
            peak = jnp.max(scores, axis=-1, keepdims=True)
            exps = jnp.exp(scores - peak)
            total = jnp.sum(exps, axis=-1, keepdims=True)
            result = jnp.dot(
                exps.astype(jnp.bfloat16), kv_rows[:, value_lanes], preferred_element_type=jnp.float32
            )
            o_b = pick_rows(result, low, rows)
            m_b = pick_rows(jnp.broadcast_to(peak, result.shape), low, rows)
            l_b = pick_rows(jnp.broadcast_to(total, result.shape), low, rows)
            m_a = ma_ref[g, :, cols]
            peak_all = jnp.maximum(m_a, m_b)
            scale_a = jnp.exp(m_a - peak_all)
            scale_b = jnp.exp(m_b - peak_all)
            numerator = oa_ref[g, :, cols] * scale_a + o_b * scale_b
            denominator = la_ref[g, :, cols] * scale_a + l_b * scale_b
            out_ref[g, :, cols] = (numerator / denominator).astype(out_ref.dtype)


def attend_near(mask, q, k_ext, v_ext, k_sum, v_sum):
    blocks, rows, width = q.shape
    keys = k_sum.shape[0]
    block = lambda offset: pl.BlockSpec((1, rows, width), lambda i: (i + offset, 0, 0))
    whole = pl.BlockSpec((keys, width), lambda i: (0, 0))
    local_keys = 3 * rows
    heads = width // HD
    flops = blocks * heads * 2 * rows * 2 * LANES * (local_keys + keys)
    bytes_accessed = 2 * (blocks * rows * width * 7 + 2 * keys * width) + 12 * blocks * rows * width
    part = jax.ShapeDtypeStruct((blocks, rows, width), jnp.float32)
    return pl.pallas_call(
        near_kernel,
        grid=(blocks,),
        in_specs=[pl.BlockSpec((1, 1, local_keys), lambda i: (i, 0, 0)), block(0)]
        + [block(0), block(1), block(2)] * 2
        + [whole, whole],
        out_specs=[block(0)] * 3,
        out_shape=[part] * 3,
        cost_estimate=pl.CostEstimate(
            flops=flops,
            transcendentals=blocks * heads * rows * (local_keys + keys),
            bytes_accessed=bytes_accessed,
        ),
    )(mask, q, k_ext, k_ext, k_ext, v_ext, v_ext, v_ext, k_sum, v_sum)


def attend_far(slot_ids, mask, q, incoming, w_kv, o_a, m_a, l_a):
    blocks, rows, width = q.shape
    model_dim = incoming.shape[-1]
    group = 2 if blocks % 2 == 0 else 1
    block = pl.BlockSpec((group, rows, width), lambda i, ids: (i, 0, 0))
    token_specs = [
        pl.BlockSpec(
            (1, rows, model_dim), lambda i, ids, n=n: (ids[RAND * group * i + n], 0, 0)
        )
        for n in range(group * RAND)
    ]
    weight = pl.BlockSpec(w_kv.shape, lambda i, ids: (0, 0))
    local_keys = RAND * rows
    heads = width // HD
    flops = blocks * (
        heads * 2 * rows * 2 * LANES * local_keys + 2 * local_keys * model_dim * 2 * width
    )
    bytes_accessed = 2 * blocks * rows * (width * 2 + model_dim * RAND) + 2 * w_kv.size + (
        12 * blocks * rows * width
    )
    grid_spec = pltpu.PrefetchScalarGridSpec(
        num_scalar_prefetch=1,
        grid=(blocks // group,),
        in_specs=[pl.BlockSpec((group, 1, local_keys), lambda i, ids: (i, 0, 0)), block]
        + token_specs
        + [weight, block, block, block],
        out_specs=block,
    )
    return pl.pallas_call(
        functools.partial(far_kernel, group),
        grid_spec=grid_spec,
        out_shape=jax.ShapeDtypeStruct((blocks, rows, width), jnp.bfloat16),
        cost_estimate=pl.CostEstimate(
            flops=flops,
            transcendentals=blocks * heads * rows * local_keys,
            bytes_accessed=bytes_accessed,
        ),
    )(slot_ids, mask, q, *([incoming] * (group * RAND)), w_kv, o_a, m_a, l_a)


def local(tokens, w_qkv, w_out, counts, rand_seg, rand_off):
    seq_count = lax.axis_size("seq")
    ctx_count = lax.axis_size("ctx")
    seq_index = lax.axis_index("seq")
    ctx_index = lax.axis_index("ctx")
    dev_count = seq_count * ctx_count
    dev_index = ctx_index * seq_count + seq_index
    tok_rows, model_dim = tokens.shape
    head_total = model_dim // HD
    dev_blocks = tok_rows // BLK
    seg_blocks = dev_blocks * seq_count
    block_total = counts.shape[0]
    capacity = (RAND * dev_blocks + ctx_count - 1) // ctx_count + 1
    first_block = dev_index * dev_blocks
    token_blocks = tokens.reshape(dev_blocks, BLK, model_dim)

    all_owner = rand_seg.reshape(ctx_count, seq_count, dev_blocks * RAND)
    all_offset = rand_off.reshape(ctx_count, seq_count, dev_blocks * RAND)
    col_owner = lax.dynamic_index_in_dim(all_owner, seq_index, axis=1, keepdims=False)
    col_offset = lax.dynamic_index_in_dim(all_offset, seq_index, axis=1, keepdims=False)
    send_off = serve_slots(col_owner, col_offset, ctx_index, capacity)
    outgoing = jnp.take(token_blocks, send_off.reshape(-1), axis=0, mode="clip").reshape(
        ctx_count, capacity, BLK, model_dim
    )
    forward = [(i, i + 1) for i in range(dev_count - 1)]
    backward = [(i + 1, i) for i in range(dev_count - 1)]
    prev_tokens = lax.ppermute(token_blocks[dev_blocks - 1], ("ctx", "seq"), forward)
    next_tokens = lax.ppermute(token_blocks[0], ("ctx", "seq"), backward)

    usable = jnp.arange(BLK, dtype=jnp.int32)[None, :] < lax.dynamic_slice_in_dim(
        counts, first_block, dev_blocks
    )[:, None]
    weighted = jnp.where(usable[:, :, None], token_blocks.astype(jnp.float32), 0.0)
    sums = jnp.sum(weighted, axis=1)
    members = jnp.sum(usable.astype(jnp.float32), axis=1)
    pooled = sums / members[:, None]
    summary = (pooled / jnp.sqrt(jnp.mean(pooled * pooled, axis=1, keepdims=True) + 1e-05)).astype(
        jnp.bfloat16
    )
    summary_all = ring_gather(ring_gather(summary, "seq"), "ctx")
    incoming = lax.all_to_all(outgoing, "ctx", split_axis=0, concat_axis=0, tiled=True)

    w_q, w_k, w_v = split_weights(w_qkv, head_total)
    project = lambda x, w: jnp.dot(x, w, preferred_element_type=jnp.float32).astype(jnp.bfloat16)
    q_own = project(tokens, w_q).reshape(dev_blocks, BLK, model_dim)
    rimmed = jnp.concatenate([prev_tokens, tokens, next_tokens], axis=0)
    k_ext = project(rimmed, w_k).reshape(dev_blocks + 2, BLK, model_dim)
    v_ext = project(rimmed, w_v).reshape(dev_blocks + 2, BLK, model_dim)
    k_sum = project(summary_all, w_k)
    v_sum = project(summary_all, w_v)

    my_owner = lax.dynamic_slice_in_dim(rand_seg, first_block, dev_blocks)
    my_offset = lax.dynamic_slice_in_dim(rand_off, first_block, dev_blocks)
    mine = my_owner.reshape(dev_blocks * RAND)
    slot_ids = mine * capacity + positions_among(mine, ctx_count)

    block_ids = first_block + jnp.arange(dev_blocks, dtype=jnp.int32)
    near_ids = block_ids[:, None] + jnp.arange(-1, 2, dtype=jnp.int32)[None, :]
    existing = (near_ids >= 0) & (near_ids < block_total)
    near_counts = jnp.where(existing, jnp.take(counts, jnp.clip(near_ids, 0, block_total - 1)), 0)
    far_global = my_owner * seg_blocks + seq_index * dev_blocks + my_offset
    far_counts = jnp.take(counts, far_global)
    positions = jnp.arange(BLK, dtype=jnp.int32)[None, None, :]
    near_mask = (positions < near_counts[:, :, None]).astype(jnp.int32).reshape(dev_blocks, 1, -1)
    far_mask = (positions < far_counts[:, :, None]).astype(jnp.int32).reshape(dev_blocks, 1, -1)

    o_a, m_a, l_a = attend_near(near_mask, q_own, k_ext, v_ext, k_sum, v_sum)
    attended = attend_far(
        slot_ids,
        far_mask,
        q_own,
        incoming.reshape(ctx_count * capacity, BLK, model_dim),
        jnp.concatenate([w_k, w_v], axis=1),
        o_a,
        m_a,
        l_a,
    ).reshape(tok_rows, model_dim)
    mixed = tokens.astype(jnp.float32) + jnp.dot(attended, w_out, preferred_element_type=jnp.float32)
    return mixed.astype(jnp.bfloat16)


def solution(mesh):
    in_specs = (P(("ctx", "seq"), None), P(), P(), P(), P(), P())
    out_specs = P(("ctx", "seq"), None)
    return jax.shard_map(local, mesh=mesh, in_specs=in_specs, out_specs=out_specs, check_vma=False)
```

```python
import functools
import math

import jax
import jax.numpy as jnp
from jax import lax
from jax.experimental import pallas as pl
from jax.experimental.pallas import tpu as pltpu
from jax.sharding import PartitionSpec as P

HD = 64
BLK = 64
RAND = 3
LANES = 128


def positions_among(owners, owner_count):
    marks = (owners[..., None] == jnp.arange(owner_count, dtype=jnp.int32)).astype(jnp.int32)
    ranks = jnp.cumsum(marks, axis=-2) - 1
    return jnp.sum(ranks * marks, axis=-1)


def serve_slots(owners, offsets, target, capacity):
    matched = owners == target
    ranks = jnp.cumsum(matched.astype(jnp.int32), axis=-1) - 1
    slot_hit = matched[..., None, :] & (
        ranks[..., None, :] == jnp.arange(capacity, dtype=jnp.int32)[:, None]
    )
    return jnp.sum(jnp.where(slot_hit, offsets[..., None, :], 0), axis=-1)


def ring_gather(x, axis):
    count = lax.axis_size(axis)
    pieces = [x] + [
        lax.ppermute(x, axis, [(i, (i + shift) % count) for i in range(count)])
        for shift in range(1, count)
    ]
    order = (lax.axis_index(axis) - jnp.arange(count, dtype=jnp.int32)) % count
    return jnp.take(jnp.stack(pieces), order, axis=0, mode="clip").reshape(-1, x.shape[-1])


def split_weights(w_qkv, head_total):
    model_dim = w_qkv.shape[0]
    shaped = w_qkv.reshape(model_dim, head_total, 3, HD)
    return [shaped[:, :, j, :].reshape(model_dim, head_total * HD) for j in range(3)]


def pair_rows(q, low):
    q = q * jnp.asarray(1.0 / math.sqrt(HD), q.dtype)
    blank = jnp.zeros_like(q)
    return jnp.concatenate([jnp.where(low, q, blank), jnp.where(low, blank, q)], axis=0)


def pick_rows(x, low, rows):
    return jnp.where(low, x[:rows], x[rows:])


CONTRACT = (((1,), (1,)), ((), ()))


def near_kernel(mask_ref, q_ref, kp_ref, kc_ref, kn_ref, vp_ref, vc_ref, vn_ref, ks_ref, vs_ref,
                o_ref, m_ref, l_ref):
    width = q_ref.shape[-1]
    rows = q_ref.shape[1]
    valid = mask_ref[0] != 0
    low = lax.broadcasted_iota(jnp.int32, (rows, LANES), 1) < HD
    for tile in range(width // LANES):
        cols = pl.ds(tile * LANES, LANES)
        q_pair = pair_rows(q_ref[0, :, cols], low)
        k_local = jnp.concatenate([kp_ref[0, :, cols], kc_ref[0, :, cols], kn_ref[0, :, cols]], axis=0)
        v_local = jnp.concatenate([vp_ref[0, :, cols], vc_ref[0, :, cols], vn_ref[0, :, cols]], axis=0)
        near = lax.dot_general(q_pair, k_local, CONTRACT, preferred_element_type=jnp.float32)
        near = jnp.where(valid, near, -jnp.inf)
        wide = lax.dot_general(q_pair, ks_ref[:, cols], CONTRACT, preferred_element_type=jnp.float32)
        peak = jnp.maximum(
            jnp.max(near, axis=-1, keepdims=True), jnp.max(wide, axis=-1, keepdims=True)
        )
        near_exp = jnp.exp(near - peak)
        wide_exp = jnp.exp(wide - peak)
        total = jnp.sum(near_exp, axis=-1, keepdims=True) + jnp.sum(wide_exp, axis=-1, keepdims=True)
        result = jnp.dot(near_exp.astype(jnp.bfloat16), v_local, preferred_element_type=jnp.float32)
        result = result + jnp.dot(
            wide_exp.astype(jnp.bfloat16), vs_ref[:, cols], preferred_element_type=jnp.float32
        )
        o_ref[0, :, cols] = pick_rows(result, low, rows)
        m_ref[0, :, cols] = pick_rows(jnp.broadcast_to(peak, result.shape), low, rows)
        l_ref[0, :, cols] = pick_rows(jnp.broadcast_to(total, result.shape), low, rows)


def far_kernel(group, ids_ref, mask_ref, q_ref, *refs):
    token_refs = refs[: group * RAND]
    wkv_ref, oa_ref, ma_ref, la_ref, out_ref = refs[group * RAND :]
    width = q_ref.shape[-1]
    rows = q_ref.shape[1]
    low = lax.broadcasted_iota(jnp.int32, (rows, LANES), 1) < HD
    far_tokens = jnp.concatenate([ref[0] for ref in token_refs], axis=0)
    kv_far = jnp.dot(far_tokens, wkv_ref[...], preferred_element_type=jnp.float32).astype(
        jnp.bfloat16
    )
    keys = RAND * rows
    for g in range(group):
        valid = mask_ref[g] != 0
        kv_rows = kv_far[g * keys : (g + 1) * keys]
        for tile in range(width // LANES):
            lanes = slice(tile * LANES, (tile + 1) * LANES)
            value_lanes = slice(width + tile * LANES, width + (tile + 1) * LANES)
            cols = pl.ds(tile * LANES, LANES)
            q_pair = pair_rows(q_ref[g, :, cols], low)
            scores = lax.dot_general(
                q_pair, kv_rows[:, lanes], CONTRACT, preferred_element_type=jnp.float32
            )
            scores = jnp.where(valid, scores, -jnp.inf)
            peak = jnp.max(scores, axis=-1, keepdims=True)
            exps = jnp.exp(scores - peak)
            total = jnp.sum(exps, axis=-1, keepdims=True)
            result = jnp.dot(
                exps.astype(jnp.bfloat16), kv_rows[:, value_lanes], preferred_element_type=jnp.float32
            )
            o_b = pick_rows(result, low, rows)
            m_b = pick_rows(jnp.broadcast_to(peak, result.shape), low, rows)
            l_b = pick_rows(jnp.broadcast_to(total, result.shape), low, rows)
            m_a = ma_ref[g, :, cols]
            peak_all = jnp.maximum(m_a, m_b)
            scale_a = jnp.exp(m_a - peak_all)
            scale_b = jnp.exp(m_b - peak_all)
            numerator = oa_ref[g, :, cols] * scale_a + o_b * scale_b
            denominator = la_ref[g, :, cols] * scale_a + l_b * scale_b
            out_ref[g, :, cols] = (numerator / denominator).astype(out_ref.dtype)


def attend_near(mask, q, k_ext, v_ext, k_sum, v_sum):
    blocks, rows, width = q.shape
    keys = k_sum.shape[0]
    block = lambda offset: pl.BlockSpec((1, rows, width), lambda i: (i + offset, 0, 0))
    whole = pl.BlockSpec((keys, width), lambda i: (0, 0))
    local_keys = 3 * rows
    heads = width // HD
    flops = blocks * heads * 2 * rows * 2 * LANES * (local_keys + keys)
    bytes_accessed = 2 * (blocks * rows * width * 7 + 2 * keys * width) + 12 * blocks * rows * width
    part = jax.ShapeDtypeStruct((blocks, rows, width), jnp.float32)
    return pl.pallas_call(
        near_kernel,
        grid=(blocks,),
        in_specs=[pl.BlockSpec((1, 1, local_keys), lambda i: (i, 0, 0)), block(0)]
        + [block(0), block(1), block(2)] * 2
        + [whole, whole],
        out_specs=[block(0)] * 3,
        out_shape=[part] * 3,
        cost_estimate=pl.CostEstimate(
            flops=flops,
            transcendentals=blocks * heads * rows * (local_keys + keys),
            bytes_accessed=bytes_accessed,
        ),
    )(mask, q, k_ext, k_ext, k_ext, v_ext, v_ext, v_ext, k_sum, v_sum)


def attend_far(slot_ids, mask, q, incoming, w_kv, o_a, m_a, l_a):
    blocks, rows, width = q.shape
    model_dim = incoming.shape[-1]
    group = 2 if blocks % 2 == 0 else 1
    block = pl.BlockSpec((group, rows, width), lambda i, ids: (i, 0, 0))
    token_specs = [
        pl.BlockSpec(
            (1, rows, model_dim), lambda i, ids, n=n: (ids[RAND * group * i + n], 0, 0)
        )
        for n in range(group * RAND)
    ]
    weight = pl.BlockSpec(w_kv.shape, lambda i, ids: (0, 0))
    local_keys = RAND * rows
    heads = width // HD
    flops = blocks * (
        heads * 2 * rows * 2 * LANES * local_keys + 2 * local_keys * model_dim * 2 * width
    )
    bytes_accessed = 2 * blocks * rows * (width * 2 + model_dim * RAND) + 2 * w_kv.size + (
        12 * blocks * rows * width
    )
    grid_spec = pltpu.PrefetchScalarGridSpec(
        num_scalar_prefetch=1,
        grid=(blocks // group,),
        in_specs=[pl.BlockSpec((group, 1, local_keys), lambda i, ids: (i, 0, 0)), block]
        + token_specs
        + [weight, block, block, block],
        out_specs=block,
    )
    return pl.pallas_call(
        functools.partial(far_kernel, group),
        grid_spec=grid_spec,
        out_shape=jax.ShapeDtypeStruct((blocks, rows, width), jnp.bfloat16),
        cost_estimate=pl.CostEstimate(
            flops=flops,
            transcendentals=blocks * heads * rows * local_keys,
            bytes_accessed=bytes_accessed,
        ),
    )(slot_ids, mask, q, *([incoming] * (group * RAND)), w_kv, o_a, m_a, l_a)


def local(tokens, w_qkv, w_out, counts, rand_seg, rand_off):
    seq_count = lax.axis_size("seq")
    ctx_count = lax.axis_size("ctx")
    seq_index = lax.axis_index("seq")
    ctx_index = lax.axis_index("ctx")
    dev_count = seq_count * ctx_count
    dev_index = ctx_index * seq_count + seq_index
    tok_rows, model_dim = tokens.shape
    head_total = model_dim // HD
    dev_blocks = tok_rows // BLK
    seg_blocks = dev_blocks * seq_count
    block_total = counts.shape[0]
    capacity = (RAND * dev_blocks + ctx_count - 1) // ctx_count + 1
    first_block = dev_index * dev_blocks
    token_blocks = tokens.reshape(dev_blocks, BLK, model_dim)

    all_owner = rand_seg.reshape(ctx_count, seq_count, dev_blocks * RAND)
    all_offset = rand_off.reshape(ctx_count, seq_count, dev_blocks * RAND)
    col_owner = lax.dynamic_index_in_dim(all_owner, seq_index, axis=1, keepdims=False)
    col_offset = lax.dynamic_index_in_dim(all_offset, seq_index, axis=1, keepdims=False)
    send_off = serve_slots(col_owner, col_offset, ctx_index, capacity)
    outgoing = jnp.take(token_blocks, send_off.reshape(-1), axis=0, mode="clip").reshape(
        ctx_count, capacity, BLK, model_dim
    )
    forward = [(i, i + 1) for i in range(dev_count - 1)]
    backward = [(i + 1, i) for i in range(dev_count - 1)]
    prev_tokens = lax.ppermute(token_blocks[dev_blocks - 1], ("ctx", "seq"), forward)
    next_tokens = lax.ppermute(token_blocks[0], ("ctx", "seq"), backward)

    usable = jnp.arange(BLK, dtype=jnp.int32)[None, :] < lax.dynamic_slice_in_dim(
        counts, first_block, dev_blocks
    )[:, None]
    weighted = jnp.where(usable[:, :, None], token_blocks.astype(jnp.float32), 0.0)
    sums = jnp.sum(weighted, axis=1)
    members = jnp.sum(usable.astype(jnp.float32), axis=1)
    pooled = sums / members[:, None]
    summary = (pooled / jnp.sqrt(jnp.mean(pooled * pooled, axis=1, keepdims=True) + 1e-05)).astype(
        jnp.bfloat16
    )
    summary_all = ring_gather(ring_gather(summary, "seq"), "ctx")
    summary_all, outgoing = lax.optimization_barrier((summary_all, outgoing))
    incoming = lax.all_to_all(outgoing, "ctx", split_axis=0, concat_axis=0, tiled=True)

    w_q, w_k, w_v = split_weights(w_qkv, head_total)
    project = lambda x, w: jnp.dot(x, w, preferred_element_type=jnp.float32).astype(jnp.bfloat16)
    q_own = project(tokens, w_q).reshape(dev_blocks, BLK, model_dim)
    rimmed = jnp.concatenate([prev_tokens, tokens, next_tokens], axis=0)
    k_ext = project(rimmed, w_k).reshape(dev_blocks + 2, BLK, model_dim)
    v_ext = project(rimmed, w_v).reshape(dev_blocks + 2, BLK, model_dim)
    k_sum = project(summary_all, w_k)
    v_sum = project(summary_all, w_v)

    my_owner = lax.dynamic_slice_in_dim(rand_seg, first_block, dev_blocks)
    my_offset = lax.dynamic_slice_in_dim(rand_off, first_block, dev_blocks)
    mine = my_owner.reshape(dev_blocks * RAND)
    slot_ids = mine * capacity + positions_among(mine, ctx_count)

    block_ids = first_block + jnp.arange(dev_blocks, dtype=jnp.int32)
    near_ids = block_ids[:, None] + jnp.arange(-1, 2, dtype=jnp.int32)[None, :]
    existing = (near_ids >= 0) & (near_ids < block_total)
    near_counts = jnp.where(existing, jnp.take(counts, jnp.clip(near_ids, 0, block_total - 1)), 0)
    far_global = my_owner * seg_blocks + seq_index * dev_blocks + my_offset
    far_counts = jnp.take(counts, far_global)
    positions = jnp.arange(BLK, dtype=jnp.int32)[None, None, :]
    near_mask = (positions < near_counts[:, :, None]).astype(jnp.int32).reshape(dev_blocks, 1, -1)
    far_mask = (positions < far_counts[:, :, None]).astype(jnp.int32).reshape(dev_blocks, 1, -1)

    o_a, m_a, l_a = attend_near(near_mask, q_own, k_ext, v_ext, k_sum, v_sum)
    attended = attend_far(
        slot_ids,
        far_mask,
        q_own,
        incoming.reshape(ctx_count * capacity, BLK, model_dim),
        jnp.concatenate([w_k, w_v], axis=1),
        o_a,
        m_a,
        l_a,
    ).reshape(tok_rows, model_dim)
    mixed = tokens.astype(jnp.float32) + jnp.dot(attended, w_out, preferred_element_type=jnp.float32)
    return mixed.astype(jnp.bfloat16)


def solution(mesh):
    in_specs = (P(("ctx", "seq"), None), P(), P(), P(), P(), P())
    out_specs = P(("ctx", "seq"), None)
    return jax.shard_map(local, mesh=mesh, in_specs=in_specs, out_specs=out_specs, check_vma=False)
```

```python
import functools
import math

import jax
import jax.numpy as jnp
from jax import lax
from jax.experimental import pallas as pl
from jax.experimental.pallas import tpu as pltpu
from jax.sharding import PartitionSpec as P

HD = 64
BLK = 64
RAND = 3
LANES = 128


def positions_among(owners, owner_count):
    marks = (owners[..., None] == jnp.arange(owner_count, dtype=jnp.int32)).astype(jnp.int32)
    ranks = jnp.cumsum(marks, axis=-2) - 1
    return jnp.sum(ranks * marks, axis=-1)


def serve_slots(owners, offsets, target, capacity):
    matched = owners == target
    ranks = jnp.cumsum(matched.astype(jnp.int32), axis=-1) - 1
    slot_hit = matched[..., None, :] & (
        ranks[..., None, :] == jnp.arange(capacity, dtype=jnp.int32)[:, None]
    )
    return jnp.sum(jnp.where(slot_hit, offsets[..., None, :], 0), axis=-1)


def split_weights(w_qkv, head_total):
    model_dim = w_qkv.shape[0]
    shaped = w_qkv.reshape(model_dim, head_total, 3, HD)
    return [shaped[:, :, j, :].reshape(model_dim, head_total * HD) for j in range(3)]


def pair_rows(q, low):
    blank = jnp.zeros_like(q)
    return jnp.concatenate([jnp.where(low, q, blank), jnp.where(low, blank, q)], axis=0)


def pick_rows(x, low, rows):
    return jnp.where(low, x[:rows], x[rows:])


CONTRACT = (((1,), (1,)), ((), ()))


def near_kernel(mask_ref, q_ref, kp_ref, kc_ref, kn_ref, vp_ref, vc_ref, vn_ref, ks_ref, vs_ref,
                o_ref, m_ref, l_ref):
    width = q_ref.shape[-1]
    rows = q_ref.shape[1]
    scaling = 1.0 / math.sqrt(HD)
    valid = mask_ref[0] != 0
    low = lax.broadcasted_iota(jnp.int32, (rows, LANES), 1) < HD
    for tile in range(width // LANES):
        cols = pl.ds(tile * LANES, LANES)
        q_pair = pair_rows(q_ref[0, :, cols], low)
        k_local = jnp.concatenate([kp_ref[0, :, cols], kc_ref[0, :, cols], kn_ref[0, :, cols]], axis=0)
        v_local = jnp.concatenate([vp_ref[0, :, cols], vc_ref[0, :, cols], vn_ref[0, :, cols]], axis=0)
        near = lax.dot_general(q_pair, k_local, CONTRACT, preferred_element_type=jnp.float32)
        near = jnp.where(valid, near * scaling, -jnp.inf)
        wide = lax.dot_general(q_pair, ks_ref[:, cols], CONTRACT, preferred_element_type=jnp.float32)
        wide = wide * scaling
        peak = jnp.maximum(
            jnp.max(near, axis=-1, keepdims=True), jnp.max(wide, axis=-1, keepdims=True)
        )
        near_exp = jnp.exp(near - peak)
        wide_exp = jnp.exp(wide - peak)
        total = jnp.sum(near_exp, axis=-1, keepdims=True) + jnp.sum(wide_exp, axis=-1, keepdims=True)
        result = jnp.dot(near_exp.astype(jnp.bfloat16), v_local, preferred_element_type=jnp.float32)
        result = result + jnp.dot(
            wide_exp.astype(jnp.bfloat16), vs_ref[:, cols], preferred_element_type=jnp.float32
        )
        o_ref[0, :, cols] = pick_rows(result, low, rows)
        m_ref[0, :, cols] = pick_rows(jnp.broadcast_to(peak, result.shape), low, rows)
        l_ref[0, :, cols] = pick_rows(jnp.broadcast_to(total, result.shape), low, rows)


def far_kernel(group, ids_ref, mask_ref, q_ref, *refs):
    token_refs = refs[: group * RAND]
    wkv_ref, oa_ref, ma_ref, la_ref, out_ref = refs[group * RAND :]
    width = q_ref.shape[-1]
    rows = q_ref.shape[1]
    scaling = 1.0 / math.sqrt(HD)
    low = lax.broadcasted_iota(jnp.int32, (rows, LANES), 1) < HD
    far_tokens = jnp.concatenate([ref[0] for ref in token_refs], axis=0)
    kv_far = jnp.dot(far_tokens, wkv_ref[...], preferred_element_type=jnp.float32).astype(
        jnp.bfloat16
    )
    keys = RAND * rows
    for g in range(group):
        valid = mask_ref[g] != 0
        kv_rows = kv_far[g * keys : (g + 1) * keys]
        for tile in range(width // LANES):
            lanes = slice(tile * LANES, (tile + 1) * LANES)
            value_lanes = slice(width + tile * LANES, width + (tile + 1) * LANES)
            cols = pl.ds(tile * LANES, LANES)
            q_pair = pair_rows(q_ref[g, :, cols], low)
            scores = lax.dot_general(
                q_pair, kv_rows[:, lanes], CONTRACT, preferred_element_type=jnp.float32
            )
            scores = jnp.where(valid, scores * scaling, -jnp.inf)
            peak = jnp.max(scores, axis=-1, keepdims=True)
            exps = jnp.exp(scores - peak)
            total = jnp.sum(exps, axis=-1, keepdims=True)
            result = jnp.dot(
                exps.astype(jnp.bfloat16), kv_rows[:, value_lanes], preferred_element_type=jnp.float32
            )
            o_b = pick_rows(result, low, rows)
            m_b = pick_rows(jnp.broadcast_to(peak, result.shape), low, rows)
            l_b = pick_rows(jnp.broadcast_to(total, result.shape), low, rows)
            m_a = ma_ref[g, :, cols]
            peak_all = jnp.maximum(m_a, m_b)
            scale_a = jnp.exp(m_a - peak_all)
            scale_b = jnp.exp(m_b - peak_all)
            numerator = oa_ref[g, :, cols] * scale_a + o_b * scale_b
            denominator = la_ref[g, :, cols] * scale_a + l_b * scale_b
            out_ref[g, :, cols] = (numerator / denominator).astype(out_ref.dtype)


def attend_near(mask, q, k_ext, v_ext, k_sum, v_sum):
    blocks, rows, width = q.shape
    keys = k_sum.shape[0]
    block = lambda offset: pl.BlockSpec((1, rows, width), lambda i: (i + offset, 0, 0))
    whole = pl.BlockSpec((keys, width), lambda i: (0, 0))
    local_keys = 3 * rows
    heads = width // HD
    flops = blocks * heads * 2 * rows * 2 * LANES * (local_keys + keys)
    bytes_accessed = 2 * (blocks * rows * width * 7 + 2 * keys * width) + 12 * blocks * rows * width
    part = jax.ShapeDtypeStruct((blocks, rows, width), jnp.float32)
    return pl.pallas_call(
        near_kernel,
        grid=(blocks,),
        in_specs=[pl.BlockSpec((1, 1, local_keys), lambda i: (i, 0, 0)), block(0)]
        + [block(0), block(1), block(2)] * 2
        + [whole, whole],
        out_specs=[block(0)] * 3,
        out_shape=[part] * 3,
        cost_estimate=pl.CostEstimate(
            flops=flops,
            transcendentals=blocks * heads * rows * (local_keys + keys),
            bytes_accessed=bytes_accessed,
        ),
    )(mask, q, k_ext, k_ext, k_ext, v_ext, v_ext, v_ext, k_sum, v_sum)


def attend_far(slot_ids, mask, q, incoming, w_kv, o_a, m_a, l_a):
    blocks, rows, width = q.shape
    model_dim = incoming.shape[-1]
    group = 4 if blocks % 4 == 0 else 1
    block = pl.BlockSpec((group, rows, width), lambda i, ids: (i, 0, 0))
    token_specs = [
        pl.BlockSpec(
            (1, rows, model_dim), lambda i, ids, n=n: (ids[RAND * group * i + n], 0, 0)
        )
        for n in range(group * RAND)
    ]
    weight = pl.BlockSpec(w_kv.shape, lambda i, ids: (0, 0))
    local_keys = RAND * rows
    heads = width // HD
    flops = blocks * (
        heads * 2 * rows * 2 * LANES * local_keys + 2 * local_keys * model_dim * 2 * width
    )
    bytes_accessed = 2 * blocks * rows * (width * 2 + model_dim * RAND) + 2 * w_kv.size + (
        12 * blocks * rows * width
    )
    grid_spec = pltpu.PrefetchScalarGridSpec(
        num_scalar_prefetch=1,
        grid=(blocks // group,),
        in_specs=[pl.BlockSpec((group, 1, local_keys), lambda i, ids: (i, 0, 0)), block]
        + token_specs
        + [weight, block, block, block],
        out_specs=block,
    )
    return pl.pallas_call(
        functools.partial(far_kernel, group),
        grid_spec=grid_spec,
        out_shape=jax.ShapeDtypeStruct((blocks, rows, width), jnp.bfloat16),
        cost_estimate=pl.CostEstimate(
            flops=flops,
            transcendentals=blocks * heads * rows * local_keys,
            bytes_accessed=bytes_accessed,
        ),
    )(slot_ids, mask, q, *([incoming] * (group * RAND)), w_kv, o_a, m_a, l_a)


def local(tokens, w_qkv, w_out, counts, rand_seg, rand_off):
    seq_count = lax.axis_size("seq")
    ctx_count = lax.axis_size("ctx")
    seq_index = lax.axis_index("seq")
    ctx_index = lax.axis_index("ctx")
    dev_count = seq_count * ctx_count
    dev_index = ctx_index * seq_count + seq_index
    tok_rows, model_dim = tokens.shape
    head_total = model_dim // HD
    dev_blocks = tok_rows // BLK
    seg_blocks = dev_blocks * seq_count
    block_total = counts.shape[0]
    capacity = (RAND * dev_blocks + ctx_count - 1) // ctx_count + 1
    first_block = dev_index * dev_blocks
    token_blocks = tokens.reshape(dev_blocks, BLK, model_dim)

    all_owner = rand_seg.reshape(ctx_count, seq_count, dev_blocks * RAND)
    all_offset = rand_off.reshape(ctx_count, seq_count, dev_blocks * RAND)
    col_owner = lax.dynamic_index_in_dim(all_owner, seq_index, axis=1, keepdims=False)
    col_offset = lax.dynamic_index_in_dim(all_offset, seq_index, axis=1, keepdims=False)
    send_off = serve_slots(col_owner, col_offset, ctx_index, capacity)
    outgoing = jnp.take(token_blocks, send_off.reshape(-1), axis=0, mode="clip").reshape(
        ctx_count, capacity, BLK, model_dim
    )
    forward = [(i, i + 1) for i in range(dev_count - 1)]
    backward = [(i + 1, i) for i in range(dev_count - 1)]
    prev_tokens = lax.ppermute(token_blocks[dev_blocks - 1], ("ctx", "seq"), forward)
    next_tokens = lax.ppermute(token_blocks[0], ("ctx", "seq"), backward)

    usable = jnp.arange(BLK, dtype=jnp.int32)[None, :] < lax.dynamic_slice_in_dim(
        counts, first_block, dev_blocks
    )[:, None]
    weighted = jnp.where(usable[:, :, None], token_blocks.astype(jnp.float32), 0.0)
    sums = jnp.sum(weighted, axis=1)
    members = jnp.sum(usable.astype(jnp.float32), axis=1)
    pooled = sums / members[:, None]
    summary = (pooled / jnp.sqrt(jnp.mean(pooled * pooled, axis=1, keepdims=True) + 1e-05)).astype(
        jnp.bfloat16
    )
    copies = jnp.broadcast_to(summary[None], (dev_count,) + summary.shape)
    summary_all = lax.all_to_all(copies, ("ctx", "seq"), 0, 0, tiled=True).reshape(-1, model_dim)
    summary_all, outgoing = lax.optimization_barrier((summary_all, outgoing))
    incoming = lax.all_to_all(outgoing, "ctx", split_axis=0, concat_axis=0, tiled=True)

    w_q, w_k, w_v = split_weights(w_qkv, head_total)
    project = lambda x, w: jnp.dot(x, w, preferred_element_type=jnp.float32).astype(jnp.bfloat16)
    q_own = project(tokens, w_q).reshape(dev_blocks, BLK, model_dim)
    rimmed = jnp.concatenate([prev_tokens, tokens, next_tokens], axis=0)
    k_ext = project(rimmed, w_k).reshape(dev_blocks + 2, BLK, model_dim)
    v_ext = project(rimmed, w_v).reshape(dev_blocks + 2, BLK, model_dim)
    k_sum = project(summary_all, w_k)
    v_sum = project(summary_all, w_v)

    my_owner = lax.dynamic_slice_in_dim(rand_seg, first_block, dev_blocks)
    my_offset = lax.dynamic_slice_in_dim(rand_off, first_block, dev_blocks)
    mine = my_owner.reshape(dev_blocks * RAND)
    slot_ids = mine * capacity + positions_among(mine, ctx_count)

    block_ids = first_block + jnp.arange(dev_blocks, dtype=jnp.int32)
    near_ids = block_ids[:, None] + jnp.arange(-1, 2, dtype=jnp.int32)[None, :]
    existing = (near_ids >= 0) & (near_ids < block_total)
    near_counts = jnp.where(existing, jnp.take(counts, jnp.clip(near_ids, 0, block_total - 1)), 0)
    far_global = my_owner * seg_blocks + seq_index * dev_blocks + my_offset
    far_counts = jnp.take(counts, far_global)
    positions = jnp.arange(BLK, dtype=jnp.int32)[None, None, :]
    near_mask = (positions < near_counts[:, :, None]).astype(jnp.int32).reshape(dev_blocks, 1, -1)
    far_mask = (positions < far_counts[:, :, None]).astype(jnp.int32).reshape(dev_blocks, 1, -1)

    o_a, m_a, l_a = attend_near(near_mask, q_own, k_ext, v_ext, k_sum, v_sum)
    attended = attend_far(
        slot_ids,
        far_mask,
        q_own,
        incoming.reshape(ctx_count * capacity, BLK, model_dim),
        jnp.concatenate([w_k, w_v], axis=1),
        o_a,
        m_a,
        l_a,
    ).reshape(tok_rows, model_dim)
    mixed = tokens.astype(jnp.float32) + jnp.dot(attended, w_out, preferred_element_type=jnp.float32)
    return mixed.astype(jnp.bfloat16)


def solution(mesh):
    in_specs = (P(("ctx", "seq"), None), P(), P(), P(), P(), P())
    out_specs = P(("ctx", "seq"), None)
    return jax.shard_map(local, mesh=mesh, in_specs=in_specs, out_specs=out_specs, check_vma=False)
```

```python
import functools
import math

import jax
import jax.numpy as jnp
from jax import lax
from jax.experimental import pallas as pl
from jax.experimental.pallas import tpu as pltpu
from jax.sharding import PartitionSpec as P

HD = 64
BLK = 64
RAND = 3
LANES = 128


def positions_among(owners, owner_count):
    marks = (owners[..., None] == jnp.arange(owner_count, dtype=jnp.int32)).astype(jnp.int32)
    ranks = jnp.cumsum(marks, axis=-2) - 1
    return jnp.sum(ranks * marks, axis=-1)


def serve_slots(owners, offsets, target, capacity):
    matched = owners == target
    ranks = jnp.cumsum(matched.astype(jnp.int32), axis=-1) - 1
    slot_hit = matched[..., None, :] & (
        ranks[..., None, :] == jnp.arange(capacity, dtype=jnp.int32)[:, None]
    )
    return jnp.sum(jnp.where(slot_hit, offsets[..., None, :], 0), axis=-1)


def split_weights(w_qkv, head_total):
    model_dim = w_qkv.shape[0]
    shaped = w_qkv.reshape(model_dim, head_total, 3, HD)
    return [shaped[:, :, j, :].reshape(model_dim, head_total * HD) for j in range(3)]


def pair_rows(q, low):
    blank = jnp.zeros_like(q)
    return jnp.concatenate([jnp.where(low, q, blank), jnp.where(low, blank, q)], axis=0)


def pick_rows(x, low, rows):
    return jnp.where(low, x[:rows], x[rows:])


CONTRACT = (((1,), (1,)), ((), ()))


def near_kernel(mask_ref, q_ref, kp_ref, kc_ref, kn_ref, vp_ref, vc_ref, vn_ref, ks_ref, vs_ref,
                o_ref, m_ref, l_ref):
    width = q_ref.shape[-1]
    rows = q_ref.shape[1]
    scaling = 1.0 / math.sqrt(HD)
    valid = mask_ref[0] != 0
    low = lax.broadcasted_iota(jnp.int32, (rows, LANES), 1) < HD
    for tile in range(width // LANES):
        cols = pl.ds(tile * LANES, LANES)
        q_pair = pair_rows(q_ref[0, :, cols], low)
        k_local = jnp.concatenate([kp_ref[0, :, cols], kc_ref[0, :, cols], kn_ref[0, :, cols]], axis=0)
        v_local = jnp.concatenate([vp_ref[0, :, cols], vc_ref[0, :, cols], vn_ref[0, :, cols]], axis=0)
        near = lax.dot_general(q_pair, k_local, CONTRACT, preferred_element_type=jnp.float32)
        near = jnp.where(valid, near * scaling, -jnp.inf)
        wide = lax.dot_general(q_pair, ks_ref[:, cols], CONTRACT, preferred_element_type=jnp.float32)
        wide = wide * scaling
        peak = jnp.maximum(
            jnp.max(near, axis=-1, keepdims=True), jnp.max(wide, axis=-1, keepdims=True)
        )
        near_exp = jnp.exp(near - peak)
        wide_exp = jnp.exp(wide - peak)
        total = jnp.sum(near_exp, axis=-1, keepdims=True) + jnp.sum(wide_exp, axis=-1, keepdims=True)
        result = jnp.dot(near_exp.astype(jnp.bfloat16), v_local, preferred_element_type=jnp.float32)
        result = result + jnp.dot(
            wide_exp.astype(jnp.bfloat16), vs_ref[:, cols], preferred_element_type=jnp.float32
        )
        o_ref[0, :, cols] = pick_rows(result, low, rows)
        m_ref[0, :, cols] = pick_rows(jnp.broadcast_to(peak, result.shape), low, rows)
        l_ref[0, :, cols] = pick_rows(jnp.broadcast_to(total, result.shape), low, rows)


def far_kernel(group, ids_ref, mask_ref, q_ref, *refs):
    token_refs = refs[: group * RAND]
    wkv_ref, oa_ref, ma_ref, la_ref, out_ref = refs[group * RAND :]
    width = q_ref.shape[-1]
    rows = q_ref.shape[1]
    scaling = 1.0 / math.sqrt(HD)
    low = lax.broadcasted_iota(jnp.int32, (rows, LANES), 1) < HD
    far_tokens = jnp.concatenate([ref[0] for ref in token_refs], axis=0)
    kv_far = jnp.dot(far_tokens, wkv_ref[...], preferred_element_type=jnp.float32).astype(
        jnp.bfloat16
    )
    keys = RAND * rows
    for g in range(group):
        valid = mask_ref[g] != 0
        kv_rows = kv_far[g * keys : (g + 1) * keys]
        for tile in range(width // LANES):
            lanes = slice(tile * LANES, (tile + 1) * LANES)
            value_lanes = slice(width + tile * LANES, width + (tile + 1) * LANES)
            cols = pl.ds(tile * LANES, LANES)
            q_pair = pair_rows(q_ref[g, :, cols], low)
            scores = lax.dot_general(
                q_pair, kv_rows[:, lanes], CONTRACT, preferred_element_type=jnp.float32
            )
            scores = jnp.where(valid, scores * scaling, -jnp.inf)
            peak = jnp.max(scores, axis=-1, keepdims=True)
            exps = jnp.exp(scores - peak)
            total = jnp.sum(exps, axis=-1, keepdims=True)
            result = jnp.dot(
                exps.astype(jnp.bfloat16), kv_rows[:, value_lanes], preferred_element_type=jnp.float32
            )
            o_b = pick_rows(result, low, rows)
            m_b = pick_rows(jnp.broadcast_to(peak, result.shape), low, rows)
            l_b = pick_rows(jnp.broadcast_to(total, result.shape), low, rows)
            m_a = ma_ref[g, :, cols]
            peak_all = jnp.maximum(m_a, m_b)
            scale_a = jnp.exp(m_a - peak_all)
            scale_b = jnp.exp(m_b - peak_all)
            numerator = oa_ref[g, :, cols] * scale_a + o_b * scale_b
            denominator = la_ref[g, :, cols] * scale_a + l_b * scale_b
            out_ref[g, :, cols] = (numerator / denominator).astype(out_ref.dtype)


def attend_near(mask, q, k_ext, v_ext, k_sum, v_sum):
    blocks, rows, width = q.shape
    keys = k_sum.shape[0]
    block = lambda offset: pl.BlockSpec((1, rows, width), lambda i: (i + offset, 0, 0))
    whole = pl.BlockSpec((keys, width), lambda i: (0, 0))
    local_keys = 3 * rows
    heads = width // HD
    flops = blocks * heads * 2 * rows * 2 * LANES * (local_keys + keys)
    bytes_accessed = 2 * (blocks * rows * width * 7 + 2 * keys * width) + 12 * blocks * rows * width
    part = jax.ShapeDtypeStruct((blocks, rows, width), jnp.float32)
    return pl.pallas_call(
        near_kernel,
        grid=(blocks,),
        in_specs=[pl.BlockSpec((1, 1, local_keys), lambda i: (i, 0, 0)), block(0)]
        + [block(0), block(1), block(2)] * 2
        + [whole, whole],
        out_specs=[block(0)] * 3,
        out_shape=[part] * 3,
        cost_estimate=pl.CostEstimate(
            flops=flops,
            transcendentals=blocks * heads * rows * (local_keys + keys),
            bytes_accessed=bytes_accessed,
        ),
    )(mask, q, k_ext, k_ext, k_ext, v_ext, v_ext, v_ext, k_sum, v_sum)


def attend_far(slot_ids, mask, q, incoming, w_kv, o_a, m_a, l_a):
    blocks, rows, width = q.shape
    model_dim = incoming.shape[-1]
    group = 2 if blocks % 2 == 0 else 1
    block = pl.BlockSpec((group, rows, width), lambda i, ids: (i, 0, 0))
    token_specs = [
        pl.BlockSpec(
            (1, rows, model_dim), lambda i, ids, n=n: (ids[RAND * group * i + n], 0, 0)
        )
        for n in range(group * RAND)
    ]
    weight = pl.BlockSpec(w_kv.shape, lambda i, ids: (0, 0))
    local_keys = RAND * rows
    heads = width // HD
    flops = blocks * (
        heads * 2 * rows * 2 * LANES * local_keys + 2 * local_keys * model_dim * 2 * width
    )
    bytes_accessed = 2 * blocks * rows * (width * 2 + model_dim * RAND) + 2 * w_kv.size + (
        12 * blocks * rows * width
    )
    grid_spec = pltpu.PrefetchScalarGridSpec(
        num_scalar_prefetch=1,
        grid=(blocks // group,),
        in_specs=[pl.BlockSpec((group, 1, local_keys), lambda i, ids: (i, 0, 0)), block]
        + token_specs
        + [weight, block, block, block],
        out_specs=block,
    )
    return pl.pallas_call(
        functools.partial(far_kernel, group),
        grid_spec=grid_spec,
        out_shape=jax.ShapeDtypeStruct((blocks, rows, width), jnp.bfloat16),
        cost_estimate=pl.CostEstimate(
            flops=flops,
            transcendentals=blocks * heads * rows * local_keys,
            bytes_accessed=bytes_accessed,
        ),
    )(slot_ids, mask, q, *([incoming] * (group * RAND)), w_kv, o_a, m_a, l_a)


def local(tokens, w_qkv, w_out, counts, rand_seg, rand_off):
    seq_count = lax.axis_size("seq")
    ctx_count = lax.axis_size("ctx")
    seq_index = lax.axis_index("seq")
    ctx_index = lax.axis_index("ctx")
    dev_count = seq_count * ctx_count
    dev_index = ctx_index * seq_count + seq_index
    tok_rows, model_dim = tokens.shape
    head_total = model_dim // HD
    dev_blocks = tok_rows // BLK
    seg_blocks = dev_blocks * seq_count
    block_total = counts.shape[0]
    capacity = (RAND * dev_blocks + ctx_count - 1) // ctx_count + 1
    first_block = dev_index * dev_blocks
    token_blocks = tokens.reshape(dev_blocks, BLK, model_dim)

    all_owner = rand_seg.reshape(ctx_count, seq_count, dev_blocks * RAND)
    all_offset = rand_off.reshape(ctx_count, seq_count, dev_blocks * RAND)
    col_owner = lax.dynamic_index_in_dim(all_owner, seq_index, axis=1, keepdims=False)
    col_offset = lax.dynamic_index_in_dim(all_offset, seq_index, axis=1, keepdims=False)
    send_off = serve_slots(col_owner, col_offset, ctx_index, capacity)
    outgoing = jnp.take(token_blocks, send_off.reshape(-1), axis=0, mode="clip").reshape(
        ctx_count, capacity, BLK, model_dim
    )
    forward = [(i, i + 1) for i in range(dev_count - 1)]
    backward = [(i + 1, i) for i in range(dev_count - 1)]
    prev_tokens = lax.ppermute(token_blocks[dev_blocks - 1], ("ctx", "seq"), forward)
    next_tokens = lax.ppermute(token_blocks[0], ("ctx", "seq"), backward)

    usable = jnp.arange(BLK, dtype=jnp.int32)[None, :] < lax.dynamic_slice_in_dim(
        counts, first_block, dev_blocks
    )[:, None]
    weighted = jnp.where(usable[:, :, None], token_blocks.astype(jnp.float32), 0.0)
    sums = jnp.sum(weighted, axis=1)
    members = jnp.sum(usable.astype(jnp.float32), axis=1)
    pooled = sums / members[:, None]
    summary = (pooled / jnp.sqrt(jnp.mean(pooled * pooled, axis=1, keepdims=True) + 1e-05)).astype(
        jnp.bfloat16
    )
    summary_all = summary
    for axis, count in (("seq", seq_count), ("ctx", ctx_count)):
        copies = jnp.broadcast_to(summary_all[None], (count,) + summary_all.shape)
        summary_all = lax.all_to_all(copies, axis, 0, 0, tiled=True).reshape(-1, model_dim)
    summary_all, outgoing = lax.optimization_barrier((summary_all, outgoing))
    incoming = lax.all_to_all(outgoing, "ctx", split_axis=0, concat_axis=0, tiled=True)

    w_q, w_k, w_v = split_weights(w_qkv, head_total)
    project = lambda x, w: jnp.dot(x, w, preferred_element_type=jnp.float32).astype(jnp.bfloat16)
    q_own = project(tokens, w_q).reshape(dev_blocks, BLK, model_dim)
    rimmed = jnp.concatenate([prev_tokens, tokens, next_tokens], axis=0)
    k_ext = project(rimmed, w_k).reshape(dev_blocks + 2, BLK, model_dim)
    v_ext = project(rimmed, w_v).reshape(dev_blocks + 2, BLK, model_dim)
    k_sum = project(summary_all, w_k)
    v_sum = project(summary_all, w_v)

    my_owner = lax.dynamic_slice_in_dim(rand_seg, first_block, dev_blocks)
    my_offset = lax.dynamic_slice_in_dim(rand_off, first_block, dev_blocks)
    mine = my_owner.reshape(dev_blocks * RAND)
    slot_ids = mine * capacity + positions_among(mine, ctx_count)

    block_ids = first_block + jnp.arange(dev_blocks, dtype=jnp.int32)
    near_ids = block_ids[:, None] + jnp.arange(-1, 2, dtype=jnp.int32)[None, :]
    existing = (near_ids >= 0) & (near_ids < block_total)
    near_counts = jnp.where(existing, jnp.take(counts, jnp.clip(near_ids, 0, block_total - 1)), 0)
    far_global = my_owner * seg_blocks + seq_index * dev_blocks + my_offset
    far_counts = jnp.take(counts, far_global)
    positions = jnp.arange(BLK, dtype=jnp.int32)[None, None, :]
    near_mask = (positions < near_counts[:, :, None]).astype(jnp.int32).reshape(dev_blocks, 1, -1)
    far_mask = (positions < far_counts[:, :, None]).astype(jnp.int32).reshape(dev_blocks, 1, -1)

    o_a, m_a, l_a = attend_near(near_mask, q_own, k_ext, v_ext, k_sum, v_sum)
    attended = attend_far(
        slot_ids,
        far_mask,
        q_own,
        incoming.reshape(ctx_count * capacity, BLK, model_dim),
        jnp.concatenate([w_k, w_v], axis=1),
        o_a,
        m_a,
        l_a,
    ).reshape(tok_rows, model_dim)
    mixed = tokens.astype(jnp.float32) + jnp.dot(attended, w_out, preferred_element_type=jnp.float32)
    return mixed.astype(jnp.bfloat16)


def solution(mesh):
    in_specs = (P(("ctx", "seq"), None), P(), P(), P(), P(), P())
    out_specs = P(("ctx", "seq"), None)
    return jax.shard_map(local, mesh=mesh, in_specs=in_specs, out_specs=out_specs, check_vma=False)
```

```python
import functools
import math

import jax
import jax.numpy as jnp
from jax import lax
from jax.experimental import pallas as pl
from jax.experimental.pallas import tpu as pltpu
from jax.sharding import PartitionSpec as P

HD = 64
BLK = 64
RAND = 3
LANES = 128


def positions_among(owners, owner_count):
    marks = (owners[..., None] == jnp.arange(owner_count, dtype=jnp.int32)).astype(jnp.int32)
    ranks = jnp.cumsum(marks, axis=-2) - 1
    return jnp.sum(ranks * marks, axis=-1)


def serve_slots(owners, offsets, target, capacity):
    matched = owners == target
    ranks = jnp.cumsum(matched.astype(jnp.int32), axis=-1) - 1
    slot_hit = matched[..., None, :] & (
        ranks[..., None, :] == jnp.arange(capacity, dtype=jnp.int32)[:, None]
    )
    return jnp.sum(jnp.where(slot_hit, offsets[..., None, :], 0), axis=-1)


def split_weights(w_qkv, head_total):
    model_dim = w_qkv.shape[0]
    shaped = w_qkv.reshape(model_dim, head_total, 3, HD)
    return [shaped[:, :, j, :].reshape(model_dim, head_total * HD) for j in range(3)]


def pair_rows(q, low):
    blank = jnp.zeros_like(q)
    return jnp.concatenate([jnp.where(low, q, blank), jnp.where(low, blank, q)], axis=0)


def pick_rows(x, low, rows):
    return jnp.where(low, x[:rows], x[rows:])


CONTRACT = (((1,), (1,)), ((), ()))


def near_kernel(mask_ref, q_ref, kp_ref, kc_ref, kn_ref, vp_ref, vc_ref, vn_ref, ks_ref, vs_ref,
                o_ref, m_ref, l_ref):
    width = q_ref.shape[-1]
    rows = q_ref.shape[1]
    scaling = 1.0 / math.sqrt(HD)
    valid = mask_ref[0] != 0
    low = lax.broadcasted_iota(jnp.int32, (rows, LANES), 1) < HD
    for tile in range(width // LANES):
        cols = pl.ds(tile * LANES, LANES)
        q_pair = pair_rows(q_ref[0, :, cols], low)
        k_local = jnp.concatenate([kp_ref[0, :, cols], kc_ref[0, :, cols], kn_ref[0, :, cols]], axis=0)
        v_local = jnp.concatenate([vp_ref[0, :, cols], vc_ref[0, :, cols], vn_ref[0, :, cols]], axis=0)
        near = lax.dot_general(q_pair, k_local, CONTRACT, preferred_element_type=jnp.float32)
        near = jnp.where(valid, near * scaling, -jnp.inf)
        wide = lax.dot_general(q_pair, ks_ref[:, cols], CONTRACT, preferred_element_type=jnp.float32)
        wide = wide * scaling
        peak = jnp.maximum(
            jnp.max(near, axis=-1, keepdims=True), jnp.max(wide, axis=-1, keepdims=True)
        )
        near_exp = jnp.exp(near - peak)
        wide_exp = jnp.exp(wide - peak)
        total = jnp.sum(near_exp, axis=-1, keepdims=True) + jnp.sum(wide_exp, axis=-1, keepdims=True)
        result = jnp.dot(near_exp.astype(jnp.bfloat16), v_local, preferred_element_type=jnp.float32)
        result = result + jnp.dot(
            wide_exp.astype(jnp.bfloat16), vs_ref[:, cols], preferred_element_type=jnp.float32
        )
        o_ref[0, :, cols] = pick_rows(result, low, rows)
        m_ref[0, :, cols] = pick_rows(jnp.broadcast_to(peak, result.shape), low, rows)
        l_ref[0, :, cols] = pick_rows(jnp.broadcast_to(total, result.shape), low, rows)


def far_kernel(group, ids_ref, mask_ref, q_ref, *refs):
    token_refs = refs[: group * RAND]
    wkv_ref, oa_ref, ma_ref, la_ref, out_ref = refs[group * RAND :]
    width = q_ref.shape[-1]
    rows = q_ref.shape[1]
    scaling = 1.0 / math.sqrt(HD)
    low = lax.broadcasted_iota(jnp.int32, (rows, LANES), 1) < HD
    far_tokens = jnp.concatenate([ref[0] for ref in token_refs], axis=0)
    kv_far = jnp.dot(far_tokens, wkv_ref[...], preferred_element_type=jnp.float32).astype(
        jnp.bfloat16
    )
    keys = RAND * rows
    for g in range(group):
        valid = mask_ref[g] != 0
        kv_rows = kv_far[g * keys : (g + 1) * keys]
        for tile in range(width // LANES):
            lanes = slice(tile * LANES, (tile + 1) * LANES)
            value_lanes = slice(width + tile * LANES, width + (tile + 1) * LANES)
            cols = pl.ds(tile * LANES, LANES)
            q_pair = pair_rows(q_ref[g, :, cols], low)
            scores = lax.dot_general(
                q_pair, kv_rows[:, lanes], CONTRACT, preferred_element_type=jnp.float32
            )
            scores = jnp.where(valid, scores * scaling, -jnp.inf)
            m_a = ma_ref[g, :, cols]
            m_a_col = jnp.concatenate([m_a[:, :1], m_a[:, HD : HD + 1]], axis=0)
            peak = jnp.maximum(jnp.max(scores, axis=-1, keepdims=True), m_a_col)
            exps = jnp.exp(scores - peak)
            total = jnp.sum(exps, axis=-1, keepdims=True)
            result = jnp.dot(
                exps.astype(jnp.bfloat16), kv_rows[:, value_lanes], preferred_element_type=jnp.float32
            )
            scale_a = pick_rows(jnp.broadcast_to(jnp.exp(m_a_col - peak), result.shape), low, rows)
            numerator = oa_ref[g, :, cols] * scale_a + pick_rows(result, low, rows)
            denominator = la_ref[g, :, cols] * scale_a + pick_rows(
                jnp.broadcast_to(total, result.shape), low, rows
            )
            out_ref[g, :, cols] = (numerator / denominator).astype(out_ref.dtype)


def attend_near(mask, q, k_ext, v_ext, k_sum, v_sum):
    blocks, rows, width = q.shape
    keys = k_sum.shape[0]
    block = lambda offset: pl.BlockSpec((1, rows, width), lambda i: (i + offset, 0, 0))
    whole = pl.BlockSpec((keys, width), lambda i: (0, 0))
    local_keys = 3 * rows
    heads = width // HD
    flops = blocks * heads * 2 * rows * 2 * LANES * (local_keys + keys)
    bytes_accessed = 2 * (blocks * rows * width * 7 + 2 * keys * width) + 12 * blocks * rows * width
    part = jax.ShapeDtypeStruct((blocks, rows, width), jnp.float32)
    return pl.pallas_call(
        near_kernel,
        grid=(blocks,),
        in_specs=[pl.BlockSpec((1, 1, local_keys), lambda i: (i, 0, 0)), block(0)]
        + [block(0), block(1), block(2)] * 2
        + [whole, whole],
        out_specs=[block(0)] * 3,
        out_shape=[part] * 3,
        cost_estimate=pl.CostEstimate(
            flops=flops,
            transcendentals=blocks * heads * rows * (local_keys + keys),
            bytes_accessed=bytes_accessed,
        ),
    )(mask, q, k_ext, k_ext, k_ext, v_ext, v_ext, v_ext, k_sum, v_sum)


def attend_far(slot_ids, mask, q, incoming, w_kv, o_a, m_a, l_a):
    blocks, rows, width = q.shape
    model_dim = incoming.shape[-1]
    group = 2 if blocks % 2 == 0 else 1
    block = pl.BlockSpec((group, rows, width), lambda i, ids: (i, 0, 0))
    token_specs = [
        pl.BlockSpec(
            (1, rows, model_dim), lambda i, ids, n=n: (ids[RAND * group * i + n], 0, 0)
        )
        for n in range(group * RAND)
    ]
    weight = pl.BlockSpec(w_kv.shape, lambda i, ids: (0, 0))
    local_keys = RAND * rows
    heads = width // HD
    flops = blocks * (
        heads * 2 * rows * 2 * LANES * local_keys + 2 * local_keys * model_dim * 2 * width
    )
    bytes_accessed = 2 * blocks * rows * (width * 2 + model_dim * RAND) + 2 * w_kv.size + (
        12 * blocks * rows * width
    )
    grid_spec = pltpu.PrefetchScalarGridSpec(
        num_scalar_prefetch=1,
        grid=(blocks // group,),
        in_specs=[pl.BlockSpec((group, 1, local_keys), lambda i, ids: (i, 0, 0)), block]
        + token_specs
        + [weight, block, block, block],
        out_specs=block,
    )
    return pl.pallas_call(
        functools.partial(far_kernel, group),
        grid_spec=grid_spec,
        out_shape=jax.ShapeDtypeStruct((blocks, rows, width), jnp.bfloat16),
        cost_estimate=pl.CostEstimate(
            flops=flops,
            transcendentals=blocks * heads * rows * local_keys,
            bytes_accessed=bytes_accessed,
        ),
    )(slot_ids, mask, q, *([incoming] * (group * RAND)), w_kv, o_a, m_a, l_a)


def local(tokens, w_qkv, w_out, counts, rand_seg, rand_off):
    seq_count = lax.axis_size("seq")
    ctx_count = lax.axis_size("ctx")
    seq_index = lax.axis_index("seq")
    ctx_index = lax.axis_index("ctx")
    dev_count = seq_count * ctx_count
    dev_index = ctx_index * seq_count + seq_index
    tok_rows, model_dim = tokens.shape
    head_total = model_dim // HD
    dev_blocks = tok_rows // BLK
    seg_blocks = dev_blocks * seq_count
    block_total = counts.shape[0]
    capacity = (RAND * dev_blocks + ctx_count - 1) // ctx_count + 1
    first_block = dev_index * dev_blocks
    token_blocks = tokens.reshape(dev_blocks, BLK, model_dim)

    all_owner = rand_seg.reshape(ctx_count, seq_count, dev_blocks * RAND)
    all_offset = rand_off.reshape(ctx_count, seq_count, dev_blocks * RAND)
    col_owner = lax.dynamic_index_in_dim(all_owner, seq_index, axis=1, keepdims=False)
    col_offset = lax.dynamic_index_in_dim(all_offset, seq_index, axis=1, keepdims=False)
    send_off = serve_slots(col_owner, col_offset, ctx_index, capacity)
    outgoing = jnp.take(token_blocks, send_off.reshape(-1), axis=0, mode="clip").reshape(
        ctx_count, capacity, BLK, model_dim
    )
    forward = [(i, i + 1) for i in range(dev_count - 1)]
    backward = [(i + 1, i) for i in range(dev_count - 1)]
    prev_tokens = lax.ppermute(token_blocks[dev_blocks - 1], ("ctx", "seq"), forward)
    next_tokens = lax.ppermute(token_blocks[0], ("ctx", "seq"), backward)

    usable = jnp.arange(BLK, dtype=jnp.int32)[None, :] < lax.dynamic_slice_in_dim(
        counts, first_block, dev_blocks
    )[:, None]
    weighted = jnp.where(usable[:, :, None], token_blocks.astype(jnp.float32), 0.0)
    sums = jnp.sum(weighted, axis=1)
    members = jnp.sum(usable.astype(jnp.float32), axis=1)
    pooled = sums / members[:, None]
    summary = (pooled / jnp.sqrt(jnp.mean(pooled * pooled, axis=1, keepdims=True) + 1e-05)).astype(
        jnp.bfloat16
    )
    copies = jnp.broadcast_to(summary[None], (dev_count,) + summary.shape)
    summary_all = lax.all_to_all(copies, ("ctx", "seq"), 0, 0, tiled=True).reshape(-1, model_dim)
    summary_all, outgoing = lax.optimization_barrier((summary_all, outgoing))
    incoming = lax.all_to_all(outgoing, "ctx", split_axis=0, concat_axis=0, tiled=True)

    w_q, w_k, w_v = split_weights(w_qkv, head_total)
    project = lambda x, w: jnp.dot(x, w, preferred_element_type=jnp.float32).astype(jnp.bfloat16)
    q_own = project(tokens, w_q).reshape(dev_blocks, BLK, model_dim)
    rimmed = jnp.concatenate([prev_tokens, tokens, next_tokens], axis=0)
    k_ext = project(rimmed, w_k).reshape(dev_blocks + 2, BLK, model_dim)
    v_ext = project(rimmed, w_v).reshape(dev_blocks + 2, BLK, model_dim)
    k_sum = project(summary_all, w_k)
    v_sum = project(summary_all, w_v)

    my_owner = lax.dynamic_slice_in_dim(rand_seg, first_block, dev_blocks)
    my_offset = lax.dynamic_slice_in_dim(rand_off, first_block, dev_blocks)
    mine = my_owner.reshape(dev_blocks * RAND)
    slot_ids = mine * capacity + positions_among(mine, ctx_count)

    block_ids = first_block + jnp.arange(dev_blocks, dtype=jnp.int32)
    near_ids = block_ids[:, None] + jnp.arange(-1, 2, dtype=jnp.int32)[None, :]
    existing = (near_ids >= 0) & (near_ids < block_total)
    near_counts = jnp.where(existing, jnp.take(counts, jnp.clip(near_ids, 0, block_total - 1)), 0)
    far_global = my_owner * seg_blocks + seq_index * dev_blocks + my_offset
    far_counts = jnp.take(counts, far_global)
    positions = jnp.arange(BLK, dtype=jnp.int32)[None, None, :]
    near_mask = (positions < near_counts[:, :, None]).astype(jnp.int32).reshape(dev_blocks, 1, -1)
    far_mask = (positions < far_counts[:, :, None]).astype(jnp.int32).reshape(dev_blocks, 1, -1)

    o_a, m_a, l_a = attend_near(near_mask, q_own, k_ext, v_ext, k_sum, v_sum)
    attended = attend_far(
        slot_ids,
        far_mask,
        q_own,
        incoming.reshape(ctx_count * capacity, BLK, model_dim),
        jnp.concatenate([w_k, w_v], axis=1),
        o_a,
        m_a,
        l_a,
    ).reshape(tok_rows, model_dim)
    mixed = tokens.astype(jnp.float32) + jnp.dot(attended, w_out, preferred_element_type=jnp.float32)
    return mixed.astype(jnp.bfloat16)


def solution(mesh):
    in_specs = (P(("ctx", "seq"), None), P(), P(), P(), P(), P())
    out_specs = P(("ctx", "seq"), None)
    return jax.shard_map(local, mesh=mesh, in_specs=in_specs, out_specs=out_specs, check_vma=False)
```

```python
import functools
import math

import jax
import jax.numpy as jnp
from jax import lax
from jax.experimental import pallas as pl
from jax.experimental.pallas import tpu as pltpu
from jax.sharding import PartitionSpec as P

HD = 64
BLK = 64
RAND = 3
LANES = 128


def positions_among(owners, owner_count):
    marks = (owners[..., None] == jnp.arange(owner_count, dtype=jnp.int32)).astype(jnp.int32)
    ranks = jnp.cumsum(marks, axis=-2) - 1
    return jnp.sum(ranks * marks, axis=-1)


def serve_slots(owners, offsets, target, capacity):
    matched = owners == target
    ranks = jnp.cumsum(matched.astype(jnp.int32), axis=-1) - 1
    slot_hit = matched[..., None, :] & (
        ranks[..., None, :] == jnp.arange(capacity, dtype=jnp.int32)[:, None]
    )
    return jnp.sum(jnp.where(slot_hit, offsets[..., None, :], 0), axis=-1)


def split_weights(w_qkv, head_total):
    model_dim = w_qkv.shape[0]
    shaped = w_qkv.reshape(model_dim, head_total, 3, HD)
    return [shaped[:, :, j, :].reshape(model_dim, head_total * HD) for j in range(3)]


def pair_rows(q, low):
    blank = jnp.zeros_like(q)
    return jnp.concatenate([jnp.where(low, q, blank), jnp.where(low, blank, q)], axis=0)


def pick_rows(x, low, rows):
    return jnp.where(low, x[:rows], x[rows:])


CONTRACT = (((1,), (1,)), ((), ()))


def near_kernel(mask_ref, q_ref, kp_ref, kc_ref, kn_ref, vp_ref, vc_ref, vn_ref, ks_ref, vs_ref,
                o_ref, m_ref, l_ref):
    width = q_ref.shape[-1]
    rows = q_ref.shape[1]
    scaling = 1.0 / math.sqrt(HD)
    valid = mask_ref[0] != 0
    low = lax.broadcasted_iota(jnp.int32, (rows, LANES), 1) < HD
    for tile in range(width // LANES):
        cols = pl.ds(tile * LANES, LANES)
        q_pair = pair_rows(q_ref[0, :, cols], low)
        k_local = jnp.concatenate([kp_ref[0, :, cols], kc_ref[0, :, cols], kn_ref[0, :, cols]], axis=0)
        v_local = jnp.concatenate([vp_ref[0, :, cols], vc_ref[0, :, cols], vn_ref[0, :, cols]], axis=0)
        near = lax.dot_general(q_pair, k_local, CONTRACT, preferred_element_type=jnp.float32)
        near = jnp.where(valid, near * scaling, -jnp.inf)
        wide = lax.dot_general(q_pair, ks_ref[:, cols], CONTRACT, preferred_element_type=jnp.float32)
        wide = wide * scaling
        peak = jnp.maximum(
            jnp.max(near, axis=-1, keepdims=True), jnp.max(wide, axis=-1, keepdims=True)
        )
        near_exp = jnp.exp(near - peak)
        wide_exp = jnp.exp(wide - peak)
        total = jnp.sum(near_exp, axis=-1, keepdims=True) + jnp.sum(wide_exp, axis=-1, keepdims=True)
        result = jnp.dot(near_exp.astype(jnp.bfloat16), v_local, preferred_element_type=jnp.float32)
        result = result + jnp.dot(
            wide_exp.astype(jnp.bfloat16), vs_ref[:, cols], preferred_element_type=jnp.float32
        )
        o_ref[0, :, cols] = pick_rows(result, low, rows)
        m_ref[0, :, cols] = pick_rows(jnp.broadcast_to(peak, result.shape), low, rows)
        l_ref[0, :, cols] = pick_rows(jnp.broadcast_to(total, result.shape), low, rows)


def far_kernel(group, ids_ref, mask_ref, q_ref, *refs):
    token_refs = refs[: group * RAND]
    wkv_ref, oa_ref, ma_ref, la_ref, tok_ref, wo_ref, out_ref, att_ref = refs[group * RAND :]
    width = q_ref.shape[-1]
    rows = q_ref.shape[1]
    scaling = 1.0 / math.sqrt(HD)
    low = lax.broadcasted_iota(jnp.int32, (rows, LANES), 1) < HD
    far_tokens = jnp.concatenate([ref[0] for ref in token_refs], axis=0)
    kv_far = jnp.dot(far_tokens, wkv_ref[...], preferred_element_type=jnp.float32).astype(
        jnp.bfloat16
    )
    keys = RAND * rows
    for g in range(group):
        valid = mask_ref[g] != 0
        kv_rows = kv_far[g * keys : (g + 1) * keys]
        for tile in range(width // LANES):
            lanes = slice(tile * LANES, (tile + 1) * LANES)
            value_lanes = slice(width + tile * LANES, width + (tile + 1) * LANES)
            cols = pl.ds(tile * LANES, LANES)
            q_pair = pair_rows(q_ref[g, :, cols], low)
            scores = lax.dot_general(
                q_pair, kv_rows[:, lanes], CONTRACT, preferred_element_type=jnp.float32
            )
            scores = jnp.where(valid, scores * scaling, -jnp.inf)
            peak = jnp.max(scores, axis=-1, keepdims=True)
            exps = jnp.exp(scores - peak)
            total = jnp.sum(exps, axis=-1, keepdims=True)
            result = jnp.dot(
                exps.astype(jnp.bfloat16), kv_rows[:, value_lanes], preferred_element_type=jnp.float32
            )
            o_b = pick_rows(result, low, rows)
            m_b = pick_rows(jnp.broadcast_to(peak, result.shape), low, rows)
            l_b = pick_rows(jnp.broadcast_to(total, result.shape), low, rows)
            m_a = ma_ref[g, :, cols]
            peak_all = jnp.maximum(m_a, m_b)
            scale_a = jnp.exp(m_a - peak_all)
            scale_b = jnp.exp(m_b - peak_all)
            numerator = oa_ref[g, :, cols] * scale_a + o_b * scale_b
            denominator = la_ref[g, :, cols] * scale_a + l_b * scale_b
            att_ref[g * rows : (g + 1) * rows, cols] = (numerator / denominator).astype(att_ref.dtype)
    mixed = jnp.dot(att_ref[...], wo_ref[...], preferred_element_type=jnp.float32)
    for g in range(group):
        part = mixed[g * rows : (g + 1) * rows] + tok_ref[g].astype(jnp.float32)
        out_ref[g] = part.astype(out_ref.dtype)


def attend_near(mask, q, k_ext, v_ext, k_sum, v_sum):
    blocks, rows, width = q.shape
    keys = k_sum.shape[0]
    block = lambda offset: pl.BlockSpec((1, rows, width), lambda i: (i + offset, 0, 0))
    whole = pl.BlockSpec((keys, width), lambda i: (0, 0))
    local_keys = 3 * rows
    heads = width // HD
    flops = blocks * heads * 2 * rows * 2 * LANES * (local_keys + keys)
    bytes_accessed = 2 * (blocks * rows * width * 7 + 2 * keys * width) + 12 * blocks * rows * width
    part = jax.ShapeDtypeStruct((blocks, rows, width), jnp.float32)
    return pl.pallas_call(
        near_kernel,
        grid=(blocks,),
        in_specs=[pl.BlockSpec((1, 1, local_keys), lambda i: (i, 0, 0)), block(0)]
        + [block(0), block(1), block(2)] * 2
        + [whole, whole],
        out_specs=[block(0)] * 3,
        out_shape=[part] * 3,
        cost_estimate=pl.CostEstimate(
            flops=flops,
            transcendentals=blocks * heads * rows * (local_keys + keys),
            bytes_accessed=bytes_accessed,
        ),
    )(mask, q, k_ext, k_ext, k_ext, v_ext, v_ext, v_ext, k_sum, v_sum)


def attend_far(slot_ids, mask, q, incoming, w_kv, o_a, m_a, l_a, token_blocks, w_out):
    blocks, rows, width = q.shape
    model_dim = incoming.shape[-1]
    group = 2 if blocks % 2 == 0 else 1
    block = pl.BlockSpec((group, rows, width), lambda i, ids: (i, 0, 0))
    token_specs = [
        pl.BlockSpec(
            (1, rows, model_dim), lambda i, ids, n=n: (ids[RAND * group * i + n], 0, 0)
        )
        for n in range(group * RAND)
    ]
    weight = pl.BlockSpec(w_kv.shape, lambda i, ids: (0, 0))
    local_keys = RAND * rows
    heads = width // HD
    flops = blocks * (
        heads * 2 * rows * 2 * LANES * local_keys + 2 * local_keys * model_dim * 2 * width
    )
    bytes_accessed = 2 * blocks * rows * (width * 2 + model_dim * RAND) + 2 * w_kv.size + (
        12 * blocks * rows * width
    )
    grid_spec = pltpu.PrefetchScalarGridSpec(
        num_scalar_prefetch=1,
        grid=(blocks // group,),
        in_specs=[pl.BlockSpec((group, 1, local_keys), lambda i, ids: (i, 0, 0)), block]
        + token_specs
        + [weight, block, block, block, block, pl.BlockSpec(w_out.shape, lambda i, ids: (0, 0))],
        out_specs=block,
        scratch_shapes=[pltpu.VMEM((group * rows, width), jnp.bfloat16)],
    )
    return pl.pallas_call(
        functools.partial(far_kernel, group),
        grid_spec=grid_spec,
        out_shape=jax.ShapeDtypeStruct((blocks, rows, width), jnp.bfloat16),
        cost_estimate=pl.CostEstimate(
            flops=flops,
            transcendentals=blocks * heads * rows * local_keys,
            bytes_accessed=bytes_accessed,
        ),
    )(slot_ids, mask, q, *([incoming] * (group * RAND)), w_kv, o_a, m_a, l_a, token_blocks, w_out)


def local(tokens, w_qkv, w_out, counts, rand_seg, rand_off):
    seq_count = lax.axis_size("seq")
    ctx_count = lax.axis_size("ctx")
    seq_index = lax.axis_index("seq")
    ctx_index = lax.axis_index("ctx")
    dev_count = seq_count * ctx_count
    dev_index = ctx_index * seq_count + seq_index
    tok_rows, model_dim = tokens.shape
    head_total = model_dim // HD
    dev_blocks = tok_rows // BLK
    seg_blocks = dev_blocks * seq_count
    block_total = counts.shape[0]
    capacity = (RAND * dev_blocks + ctx_count - 1) // ctx_count + 1
    first_block = dev_index * dev_blocks
    token_blocks = tokens.reshape(dev_blocks, BLK, model_dim)

    all_owner = rand_seg.reshape(ctx_count, seq_count, dev_blocks * RAND)
    all_offset = rand_off.reshape(ctx_count, seq_count, dev_blocks * RAND)
    col_owner = lax.dynamic_index_in_dim(all_owner, seq_index, axis=1, keepdims=False)
    col_offset = lax.dynamic_index_in_dim(all_offset, seq_index, axis=1, keepdims=False)
    send_off = serve_slots(col_owner, col_offset, ctx_index, capacity)
    outgoing = jnp.take(token_blocks, send_off.reshape(-1), axis=0, mode="clip").reshape(
        ctx_count, capacity, BLK, model_dim
    )
    forward = [(i, i + 1) for i in range(dev_count - 1)]
    backward = [(i + 1, i) for i in range(dev_count - 1)]
    prev_tokens = lax.ppermute(token_blocks[dev_blocks - 1], ("ctx", "seq"), forward)
    next_tokens = lax.ppermute(token_blocks[0], ("ctx", "seq"), backward)

    usable = jnp.arange(BLK, dtype=jnp.int32)[None, :] < lax.dynamic_slice_in_dim(
        counts, first_block, dev_blocks
    )[:, None]
    weighted = jnp.where(usable[:, :, None], token_blocks.astype(jnp.float32), 0.0)
    sums = jnp.sum(weighted, axis=1)
    members = jnp.sum(usable.astype(jnp.float32), axis=1)
    pooled = sums / members[:, None]
    summary = (pooled / jnp.sqrt(jnp.mean(pooled * pooled, axis=1, keepdims=True) + 1e-05)).astype(
        jnp.bfloat16
    )
    copies = jnp.broadcast_to(summary[None], (dev_count,) + summary.shape)
    summary_all = lax.all_to_all(copies, ("ctx", "seq"), 0, 0, tiled=True).reshape(-1, model_dim)
    summary_all, outgoing = lax.optimization_barrier((summary_all, outgoing))
    incoming = lax.all_to_all(outgoing, "ctx", split_axis=0, concat_axis=0, tiled=True)

    w_q, w_k, w_v = split_weights(w_qkv, head_total)
    project = lambda x, w: jnp.dot(x, w, preferred_element_type=jnp.float32).astype(jnp.bfloat16)
    q_own = project(tokens, w_q).reshape(dev_blocks, BLK, model_dim)
    rimmed = jnp.concatenate([prev_tokens, tokens, next_tokens], axis=0)
    k_ext = project(rimmed, w_k).reshape(dev_blocks + 2, BLK, model_dim)
    v_ext = project(rimmed, w_v).reshape(dev_blocks + 2, BLK, model_dim)
    k_sum = project(summary_all, w_k)
    v_sum = project(summary_all, w_v)

    my_owner = lax.dynamic_slice_in_dim(rand_seg, first_block, dev_blocks)
    my_offset = lax.dynamic_slice_in_dim(rand_off, first_block, dev_blocks)
    mine = my_owner.reshape(dev_blocks * RAND)
    slot_ids = mine * capacity + positions_among(mine, ctx_count)

    block_ids = first_block + jnp.arange(dev_blocks, dtype=jnp.int32)
    near_ids = block_ids[:, None] + jnp.arange(-1, 2, dtype=jnp.int32)[None, :]
    existing = (near_ids >= 0) & (near_ids < block_total)
    near_counts = jnp.where(existing, jnp.take(counts, jnp.clip(near_ids, 0, block_total - 1)), 0)
    far_global = my_owner * seg_blocks + seq_index * dev_blocks + my_offset
    far_counts = jnp.take(counts, far_global)
    positions = jnp.arange(BLK, dtype=jnp.int32)[None, None, :]
    near_mask = (positions < near_counts[:, :, None]).astype(jnp.int32).reshape(dev_blocks, 1, -1)
    far_mask = (positions < far_counts[:, :, None]).astype(jnp.int32).reshape(dev_blocks, 1, -1)

    o_a, m_a, l_a = attend_near(near_mask, q_own, k_ext, v_ext, k_sum, v_sum)
    mixed = attend_far(
        slot_ids,
        far_mask,
        q_own,
        incoming.reshape(ctx_count * capacity, BLK, model_dim),
        jnp.concatenate([w_k, w_v], axis=1),
        o_a,
        m_a,
        l_a,
        token_blocks,
        w_out,
    )
    return mixed.reshape(tok_rows, model_dim)


def solution(mesh):
    in_specs = (P(("ctx", "seq"), None), P(), P(), P(), P(), P())
    out_specs = P(("ctx", "seq"), None)
    return jax.shard_map(local, mesh=mesh, in_specs=in_specs, out_specs=out_specs, check_vma=False)
```

```python
import functools
import math

import jax
import jax.numpy as jnp
from jax import lax
from jax.experimental import pallas as pl
from jax.experimental.pallas import tpu as pltpu
from jax.sharding import PartitionSpec as P

HD = 64
BLK = 64
RAND = 3
LANES = 128


def positions_among(owners, owner_count):
    marks = (owners[..., None] == jnp.arange(owner_count, dtype=jnp.int32)).astype(jnp.int32)
    ranks = jnp.cumsum(marks, axis=-2) - 1
    return jnp.sum(ranks * marks, axis=-1)


def serve_slots(owners, offsets, target, capacity):
    matched = owners == target
    ranks = jnp.cumsum(matched.astype(jnp.int32), axis=-1) - 1
    slot_hit = matched[..., None, :] & (
        ranks[..., None, :] == jnp.arange(capacity, dtype=jnp.int32)[:, None]
    )
    return jnp.sum(jnp.where(slot_hit, offsets[..., None, :], 0), axis=-1)


def split_weights(w_qkv, head_total):
    model_dim = w_qkv.shape[0]
    shaped = w_qkv.reshape(model_dim, head_total, 3, HD)
    return [shaped[:, :, j, :].reshape(model_dim, head_total * HD) for j in range(3)]


def pair_rows(q, low):
    blank = jnp.zeros_like(q)
    return jnp.concatenate([jnp.where(low, q, blank), jnp.where(low, blank, q)], axis=0)


def pick_rows(x, low, rows):
    return jnp.where(low, x[:rows], x[rows:])


CONTRACT = (((1,), (1,)), ((), ()))


def near_kernel(mask_ref, q_ref, kp_ref, kc_ref, kn_ref, vp_ref, vc_ref, vn_ref, ks_ref, vs_ref,
                o_ref, m_ref, l_ref):
    width = q_ref.shape[-1]
    rows = q_ref.shape[1]
    scaling = 1.0 / math.sqrt(HD)
    valid = mask_ref[0] != 0
    low = lax.broadcasted_iota(jnp.int32, (rows, LANES), 1) < HD
    for tile in range(width // LANES):
        cols = pl.ds(tile * LANES, LANES)
        q_pair = pair_rows(q_ref[0, :, cols], low)
        k_local = jnp.concatenate([kp_ref[0, :, cols], kc_ref[0, :, cols], kn_ref[0, :, cols]], axis=0)
        v_local = jnp.concatenate([vp_ref[0, :, cols], vc_ref[0, :, cols], vn_ref[0, :, cols]], axis=0)
        near = lax.dot_general(q_pair, k_local, CONTRACT, preferred_element_type=jnp.float32)
        near = jnp.where(valid, near * scaling, -jnp.inf)
        wide = lax.dot_general(q_pair, ks_ref[:, cols], CONTRACT, preferred_element_type=jnp.float32)
        wide = wide * scaling
        peak = jnp.maximum(
            jnp.max(near, axis=-1, keepdims=True), jnp.max(wide, axis=-1, keepdims=True)
        )
        near_exp = jnp.exp(near - peak)
        wide_exp = jnp.exp(wide - peak)
        total = jnp.sum(near_exp, axis=-1, keepdims=True) + jnp.sum(wide_exp, axis=-1, keepdims=True)
        result = jnp.dot(near_exp.astype(jnp.bfloat16), v_local, preferred_element_type=jnp.float32)
        result = result + jnp.dot(
            wide_exp.astype(jnp.bfloat16), vs_ref[:, cols], preferred_element_type=jnp.float32
        )
        o_ref[0, :, cols] = pick_rows(result, low, rows)
        m_ref[0, :, cols] = pick_rows(jnp.broadcast_to(peak, result.shape), low, rows)
        l_ref[0, :, cols] = pick_rows(jnp.broadcast_to(total, result.shape), low, rows)


def far_kernel(group, ids_ref, mask_ref, q_ref, *refs):
    token_refs = refs[: group * RAND]
    (wk_hbm, wv_hbm, wo_hbm, oa_ref, ma_ref, la_ref, tok_ref, out_ref, att_ref,
     wk_ref, wv_ref, wo_ref, sems) = refs[group * RAND :]
    width = q_ref.shape[-1]
    rows = q_ref.shape[1]
    scaling = 1.0 / math.sqrt(HD)
    low = lax.broadcasted_iota(jnp.int32, (rows, LANES), 1) < HD
    first = pl.program_id(0) == 0
    loads = [
        pltpu.make_async_copy(src, dst, sems.at[n])
        for n, (src, dst) in enumerate(((wk_hbm, wk_ref), (wv_hbm, wv_ref), (wo_hbm, wo_ref)))
    ]

    @pl.when(first)
    def _():
        for load in loads:
            load.start()

    def ready(load):
        @pl.when(first)
        def _():
            load.wait()

    far_tokens = jnp.concatenate([ref[0] for ref in token_refs], axis=0)
    ready(loads[0])
    k_far = jnp.dot(far_tokens, wk_ref[...], preferred_element_type=jnp.float32).astype(jnp.bfloat16)
    ready(loads[1])
    v_far = jnp.dot(far_tokens, wv_ref[...], preferred_element_type=jnp.float32).astype(jnp.bfloat16)
    keys = RAND * rows
    for g in range(group):
        valid = mask_ref[g] != 0
        k_rows = k_far[g * keys : (g + 1) * keys]
        v_rows = v_far[g * keys : (g + 1) * keys]
        for tile in range(width // LANES):
            lanes = slice(tile * LANES, (tile + 1) * LANES)
            cols = pl.ds(tile * LANES, LANES)
            q_pair = pair_rows(q_ref[g, :, cols], low)
            scores = lax.dot_general(
                q_pair, k_rows[:, lanes], CONTRACT, preferred_element_type=jnp.float32
            )
            scores = jnp.where(valid, scores * scaling, -jnp.inf)
            peak = jnp.max(scores, axis=-1, keepdims=True)
            exps = jnp.exp(scores - peak)
            total = jnp.sum(exps, axis=-1, keepdims=True)
            result = jnp.dot(
                exps.astype(jnp.bfloat16), v_rows[:, lanes], preferred_element_type=jnp.float32
            )
            o_b = pick_rows(result, low, rows)
            m_b = pick_rows(jnp.broadcast_to(peak, result.shape), low, rows)
            l_b = pick_rows(jnp.broadcast_to(total, result.shape), low, rows)
            m_a = ma_ref[g, :, cols]
            peak_all = jnp.maximum(m_a, m_b)
            scale_a = jnp.exp(m_a - peak_all)
            scale_b = jnp.exp(m_b - peak_all)
            numerator = oa_ref[g, :, cols] * scale_a + o_b * scale_b
            denominator = la_ref[g, :, cols] * scale_a + l_b * scale_b
            att_ref[g * rows : (g + 1) * rows, cols] = (numerator / denominator).astype(att_ref.dtype)
    ready(loads[2])
    mixed = jnp.dot(att_ref[...], wo_ref[...], preferred_element_type=jnp.float32)
    for g in range(group):
        part = mixed[g * rows : (g + 1) * rows] + tok_ref[g].astype(jnp.float32)
        out_ref[g] = part.astype(out_ref.dtype)


def attend_near(mask, q, k_ext, v_ext, k_sum, v_sum):
    blocks, rows, width = q.shape
    keys = k_sum.shape[0]
    block = lambda offset: pl.BlockSpec((1, rows, width), lambda i: (i + offset, 0, 0))
    whole = pl.BlockSpec((keys, width), lambda i: (0, 0))
    local_keys = 3 * rows
    heads = width // HD
    flops = blocks * heads * 2 * rows * 2 * LANES * (local_keys + keys)
    bytes_accessed = 2 * (blocks * rows * width * 7 + 2 * keys * width) + 12 * blocks * rows * width
    part = jax.ShapeDtypeStruct((blocks, rows, width), jnp.float32)
    return pl.pallas_call(
        near_kernel,
        grid=(blocks,),
        in_specs=[pl.BlockSpec((1, 1, local_keys), lambda i: (i, 0, 0)), block(0)]
        + [block(0), block(1), block(2)] * 2
        + [whole, whole],
        out_specs=[block(0)] * 3,
        out_shape=[part] * 3,
        cost_estimate=pl.CostEstimate(
            flops=flops,
            transcendentals=blocks * heads * rows * (local_keys + keys),
            bytes_accessed=bytes_accessed,
        ),
    )(mask, q, k_ext, k_ext, k_ext, v_ext, v_ext, v_ext, k_sum, v_sum)


def attend_far(slot_ids, mask, q, incoming, w_k, w_v, o_a, m_a, l_a, token_blocks, w_out):
    blocks, rows, width = q.shape
    model_dim = incoming.shape[-1]
    group = 2 if blocks % 2 == 0 else 1
    block = pl.BlockSpec((group, rows, width), lambda i, ids: (i, 0, 0))
    token_specs = [
        pl.BlockSpec(
            (1, rows, model_dim), lambda i, ids, n=n: (ids[RAND * group * i + n], 0, 0)
        )
        for n in range(group * RAND)
    ]
    weight = pl.BlockSpec(memory_space=pl.ANY)
    local_keys = RAND * rows
    heads = width // HD
    flops = blocks * (
        heads * 2 * rows * 2 * LANES * local_keys + 2 * local_keys * model_dim * 2 * width
    )
    bytes_accessed = 2 * blocks * rows * (width * 2 + model_dim * RAND) + 2 * (w_k.size + w_v.size + w_out.size) + (
        12 * blocks * rows * width
    )
    grid_spec = pltpu.PrefetchScalarGridSpec(
        num_scalar_prefetch=1,
        grid=(blocks // group,),
        in_specs=[pl.BlockSpec((group, 1, local_keys), lambda i, ids: (i, 0, 0)), block]
        + token_specs
        + [weight, weight, weight, block, block, block, block],
        out_specs=block,
        scratch_shapes=[
            pltpu.VMEM((group * rows, width), jnp.bfloat16),
            pltpu.VMEM(w_k.shape, w_k.dtype),
            pltpu.VMEM(w_v.shape, w_v.dtype),
            pltpu.VMEM(w_out.shape, w_out.dtype),
            pltpu.SemaphoreType.DMA((3,)),
        ],
    )
    return pl.pallas_call(
        functools.partial(far_kernel, group),
        grid_spec=grid_spec,
        out_shape=jax.ShapeDtypeStruct((blocks, rows, width), jnp.bfloat16),
        cost_estimate=pl.CostEstimate(
            flops=flops,
            transcendentals=blocks * heads * rows * local_keys,
            bytes_accessed=bytes_accessed,
        ),
    )(slot_ids, mask, q, *([incoming] * (group * RAND)), w_k, w_v, w_out, o_a, m_a, l_a, token_blocks)


def local(tokens, w_qkv, w_out, counts, rand_seg, rand_off):
    seq_count = lax.axis_size("seq")
    ctx_count = lax.axis_size("ctx")
    seq_index = lax.axis_index("seq")
    ctx_index = lax.axis_index("ctx")
    dev_count = seq_count * ctx_count
    dev_index = ctx_index * seq_count + seq_index
    tok_rows, model_dim = tokens.shape
    head_total = model_dim // HD
    dev_blocks = tok_rows // BLK
    seg_blocks = dev_blocks * seq_count
    block_total = counts.shape[0]
    capacity = (RAND * dev_blocks + ctx_count - 1) // ctx_count + 1
    first_block = dev_index * dev_blocks
    token_blocks = tokens.reshape(dev_blocks, BLK, model_dim)

    all_owner = rand_seg.reshape(ctx_count, seq_count, dev_blocks * RAND)
    all_offset = rand_off.reshape(ctx_count, seq_count, dev_blocks * RAND)
    col_owner = lax.dynamic_index_in_dim(all_owner, seq_index, axis=1, keepdims=False)
    col_offset = lax.dynamic_index_in_dim(all_offset, seq_index, axis=1, keepdims=False)
    send_off = serve_slots(col_owner, col_offset, ctx_index, capacity)
    outgoing = jnp.take(token_blocks, send_off.reshape(-1), axis=0, mode="clip").reshape(
        ctx_count, capacity, BLK, model_dim
    )
    forward = [(i, i + 1) for i in range(dev_count - 1)]
    backward = [(i + 1, i) for i in range(dev_count - 1)]
    prev_tokens = lax.ppermute(token_blocks[dev_blocks - 1], ("ctx", "seq"), forward)
    next_tokens = lax.ppermute(token_blocks[0], ("ctx", "seq"), backward)

    usable = jnp.arange(BLK, dtype=jnp.int32)[None, :] < lax.dynamic_slice_in_dim(
        counts, first_block, dev_blocks
    )[:, None]
    weighted = jnp.where(usable[:, :, None], token_blocks.astype(jnp.float32), 0.0)
    sums = jnp.sum(weighted, axis=1)
    members = jnp.sum(usable.astype(jnp.float32), axis=1)
    pooled = sums / members[:, None]
    summary = (pooled / jnp.sqrt(jnp.mean(pooled * pooled, axis=1, keepdims=True) + 1e-05)).astype(
        jnp.bfloat16
    )
    copies = jnp.broadcast_to(summary[None], (dev_count,) + summary.shape)
    summary_all = lax.all_to_all(copies, ("ctx", "seq"), 0, 0, tiled=True).reshape(-1, model_dim)
    summary_all, outgoing = lax.optimization_barrier((summary_all, outgoing))
    incoming = lax.all_to_all(outgoing, "ctx", split_axis=0, concat_axis=0, tiled=True)

    w_q, w_k, w_v = split_weights(w_qkv, head_total)
    project = lambda x, w: jnp.dot(x, w, preferred_element_type=jnp.float32).astype(jnp.bfloat16)
    q_own = project(tokens, w_q).reshape(dev_blocks, BLK, model_dim)
    rimmed = jnp.concatenate([prev_tokens, tokens, next_tokens], axis=0)
    k_ext = project(rimmed, w_k).reshape(dev_blocks + 2, BLK, model_dim)
    v_ext = project(rimmed, w_v).reshape(dev_blocks + 2, BLK, model_dim)
    k_sum = project(summary_all, w_k)
    v_sum = project(summary_all, w_v)

    my_owner = lax.dynamic_slice_in_dim(rand_seg, first_block, dev_blocks)
    my_offset = lax.dynamic_slice_in_dim(rand_off, first_block, dev_blocks)
    mine = my_owner.reshape(dev_blocks * RAND)
    slot_ids = mine * capacity + positions_among(mine, ctx_count)

    block_ids = first_block + jnp.arange(dev_blocks, dtype=jnp.int32)
    near_ids = block_ids[:, None] + jnp.arange(-1, 2, dtype=jnp.int32)[None, :]
    existing = (near_ids >= 0) & (near_ids < block_total)
    near_counts = jnp.where(existing, jnp.take(counts, jnp.clip(near_ids, 0, block_total - 1)), 0)
    far_global = my_owner * seg_blocks + seq_index * dev_blocks + my_offset
    far_counts = jnp.take(counts, far_global)
    positions = jnp.arange(BLK, dtype=jnp.int32)[None, None, :]
    near_mask = (positions < near_counts[:, :, None]).astype(jnp.int32).reshape(dev_blocks, 1, -1)
    far_mask = (positions < far_counts[:, :, None]).astype(jnp.int32).reshape(dev_blocks, 1, -1)

    o_a, m_a, l_a = attend_near(near_mask, q_own, k_ext, v_ext, k_sum, v_sum)
    mixed = attend_far(
        slot_ids,
        far_mask,
        q_own,
        incoming.reshape(ctx_count * capacity, BLK, model_dim),
        w_k,
        w_v,
        o_a,
        m_a,
        l_a,
        token_blocks,
        w_out,
    )
    return mixed.reshape(tok_rows, model_dim)


def solution(mesh):
    in_specs = (P(("ctx", "seq"), None), P(), P(), P(), P(), P())
    out_specs = P(("ctx", "seq"), None)
    return jax.shard_map(local, mesh=mesh, in_specs=in_specs, out_specs=out_specs, check_vma=False)
```

```python
import functools
import math

import jax
import jax.numpy as jnp
from jax import lax
from jax.experimental import pallas as pl
from jax.experimental.pallas import tpu as pltpu
from jax.sharding import PartitionSpec as P

HD = 64
BLK = 64
RAND = 3
LANES = 128


def positions_among(owners, owner_count):
    marks = (owners[..., None] == jnp.arange(owner_count, dtype=jnp.int32)).astype(jnp.int32)
    ranks = jnp.cumsum(marks, axis=-2) - 1
    return jnp.sum(ranks * marks, axis=-1)


def serve_slots(owners, offsets, target, capacity):
    matched = owners == target
    ranks = jnp.cumsum(matched.astype(jnp.int32), axis=-1) - 1
    slot_hit = matched[..., None, :] & (
        ranks[..., None, :] == jnp.arange(capacity, dtype=jnp.int32)[:, None]
    )
    return jnp.sum(jnp.where(slot_hit, offsets[..., None, :], 0), axis=-1)


def split_weights(w_qkv, head_total):
    model_dim = w_qkv.shape[0]
    shaped = w_qkv.reshape(model_dim, head_total, 3, HD)
    return [shaped[:, :, j, :].reshape(model_dim, head_total * HD) for j in range(3)]


def pair_rows(q, low):
    blank = jnp.zeros_like(q)
    return jnp.concatenate([jnp.where(low, q, blank), jnp.where(low, blank, q)], axis=0)


def pick_rows(x, low, rows):
    return jnp.where(low, x[:rows], x[rows:])


CONTRACT = (((1,), (1,)), ((), ()))


def near_kernel(mask_ref, q_ref, kp_ref, kc_ref, kn_ref, vp_ref, vc_ref, vn_ref, ks_ref, vs_ref,
                o_ref, m_ref, l_ref):
    width = q_ref.shape[-1]
    rows = q_ref.shape[1]
    scaling = 1.0 / math.sqrt(HD)
    valid = mask_ref[0] != 0
    low = lax.broadcasted_iota(jnp.int32, (rows, LANES), 1) < HD
    for tile in range(width // LANES):
        cols = pl.ds(tile * LANES, LANES)
        q_pair = pair_rows(q_ref[0, :, cols], low)
        k_local = jnp.concatenate([kp_ref[0, :, cols], kc_ref[0, :, cols], kn_ref[0, :, cols]], axis=0)
        v_local = jnp.concatenate([vp_ref[0, :, cols], vc_ref[0, :, cols], vn_ref[0, :, cols]], axis=0)
        near = lax.dot_general(q_pair, k_local, CONTRACT, preferred_element_type=jnp.float32)
        near = jnp.where(valid, near * scaling, -jnp.inf)
        wide = lax.dot_general(q_pair, ks_ref[:, cols], CONTRACT, preferred_element_type=jnp.float32)
        wide = wide * scaling
        peak = jnp.maximum(
            jnp.max(near, axis=-1, keepdims=True), jnp.max(wide, axis=-1, keepdims=True)
        )
        near_exp = jnp.exp(near - peak)
        wide_exp = jnp.exp(wide - peak)
        total = jnp.sum(near_exp, axis=-1, keepdims=True) + jnp.sum(wide_exp, axis=-1, keepdims=True)
        result = jnp.dot(near_exp.astype(jnp.bfloat16), v_local, preferred_element_type=jnp.float32)
        result = result + jnp.dot(
            wide_exp.astype(jnp.bfloat16), vs_ref[:, cols], preferred_element_type=jnp.float32
        )
        o_ref[0, :, cols] = pick_rows(result, low, rows)
        m_ref[0, :, cols] = pick_rows(jnp.broadcast_to(peak, result.shape), low, rows)
        l_ref[0, :, cols] = pick_rows(jnp.broadcast_to(total, result.shape), low, rows)


def far_kernel(group, ids_ref, mask_ref, q_ref, *refs):
    token_refs = refs[: group * RAND]
    wkv_ref, oa_ref, ma_ref, la_ref, tok_ref, wo_ref, out_ref, att_ref = refs[group * RAND :]
    width = q_ref.shape[-1]
    rows = q_ref.shape[1]
    scaling = 1.0 / math.sqrt(HD)
    low = lax.broadcasted_iota(jnp.int32, (rows, LANES), 1) < HD
    far_tokens = jnp.concatenate([ref[0] for ref in token_refs], axis=0)
    kv_far = jnp.dot(far_tokens, wkv_ref[...], preferred_element_type=jnp.float32).astype(
        jnp.bfloat16
    )
    keys = RAND * rows
    for g in range(group):
        valid = mask_ref[g] != 0
        kv_rows = kv_far[g * keys : (g + 1) * keys]
        for tile in range(width // LANES):
            lanes = slice(tile * LANES, (tile + 1) * LANES)
            value_lanes = slice(width + tile * LANES, width + (tile + 1) * LANES)
            cols = pl.ds(tile * LANES, LANES)
            q_pair = pair_rows(q_ref[g, :, cols], low)
            scores = lax.dot_general(
                q_pair, kv_rows[:, lanes], CONTRACT, preferred_element_type=jnp.float32
            )
            scores = jnp.where(valid, scores * scaling, -jnp.inf)
            peak = jnp.max(scores, axis=-1, keepdims=True)
            exps = jnp.exp(scores - peak)
            total = jnp.sum(exps, axis=-1, keepdims=True)
            result = jnp.dot(
                exps.astype(jnp.bfloat16), kv_rows[:, value_lanes], preferred_element_type=jnp.float32
            )
            o_b = pick_rows(result, low, rows)
            m_b = pick_rows(jnp.broadcast_to(peak, result.shape), low, rows)
            l_b = pick_rows(jnp.broadcast_to(total, result.shape), low, rows)
            m_a = ma_ref[g, :, cols]
            peak_all = jnp.maximum(m_a, m_b)
            scale_a = jnp.exp(m_a - peak_all)
            scale_b = jnp.exp(m_b - peak_all)
            numerator = oa_ref[g, :, cols] * scale_a + o_b * scale_b
            denominator = la_ref[g, :, cols] * scale_a + l_b * scale_b
            att_ref[g * rows : (g + 1) * rows, cols] = (numerator / denominator).astype(att_ref.dtype)
    mixed = jnp.dot(att_ref[...], wo_ref[...], preferred_element_type=jnp.float32)
    for g in range(group):
        part = mixed[g * rows : (g + 1) * rows] + tok_ref[g].astype(jnp.float32)
        out_ref[g] = part.astype(out_ref.dtype)


def attend_near(mask, q, k_ext, v_ext, k_sum, v_sum):
    blocks, rows, width = q.shape
    keys = k_sum.shape[0]
    block = lambda offset: pl.BlockSpec((1, rows, width), lambda i: (i + offset, 0, 0))
    whole = pl.BlockSpec((keys, width), lambda i: (0, 0))
    local_keys = 3 * rows
    heads = width // HD
    flops = blocks * heads * 2 * rows * 2 * LANES * (local_keys + keys)
    bytes_accessed = 2 * (blocks * rows * width * 7 + 2 * keys * width) + 12 * blocks * rows * width
    part = jax.ShapeDtypeStruct((blocks, rows, width), jnp.float32)
    return pl.pallas_call(
        near_kernel,
        grid=(blocks,),
        in_specs=[pl.BlockSpec((1, 1, local_keys), lambda i: (i, 0, 0)), block(0)]
        + [block(0), block(1), block(2)] * 2
        + [whole, whole],
        out_specs=[block(0)] * 3,
        out_shape=[part] * 3,
        cost_estimate=pl.CostEstimate(
            flops=flops,
            transcendentals=blocks * heads * rows * (local_keys + keys),
            bytes_accessed=bytes_accessed,
        ),
    )(mask, q, k_ext, k_ext, k_ext, v_ext, v_ext, v_ext, k_sum, v_sum)


def attend_far(slot_ids, mask, q, incoming, w_kv, o_a, m_a, l_a, token_blocks, w_out):
    blocks, rows, width = q.shape
    model_dim = incoming.shape[-1]
    group = 4 if blocks % 4 == 0 else 1
    block = pl.BlockSpec((group, rows, width), lambda i, ids: (i, 0, 0))
    token_specs = [
        pl.BlockSpec(
            (1, rows, model_dim), lambda i, ids, n=n: (ids[RAND * group * i + n], 0, 0)
        )
        for n in range(group * RAND)
    ]
    weight = pl.BlockSpec(w_kv.shape, lambda i, ids: (0, 0))
    local_keys = RAND * rows
    heads = width // HD
    flops = blocks * (
        heads * 2 * rows * 2 * LANES * local_keys + 2 * local_keys * model_dim * 2 * width
    )
    bytes_accessed = 2 * blocks * rows * (width * 2 + model_dim * RAND) + 2 * w_kv.size + (
        12 * blocks * rows * width
    )
    grid_spec = pltpu.PrefetchScalarGridSpec(
        num_scalar_prefetch=1,
        grid=(blocks // group,),
        in_specs=[pl.BlockSpec((group, 1, local_keys), lambda i, ids: (i, 0, 0)), block]
        + token_specs
        + [weight, block, block, block, block, pl.BlockSpec(w_out.shape, lambda i, ids: (0, 0))],
        out_specs=block,
        scratch_shapes=[pltpu.VMEM((group * rows, width), jnp.bfloat16)],
    )
    return pl.pallas_call(
        functools.partial(far_kernel, group),
        grid_spec=grid_spec,
        out_shape=jax.ShapeDtypeStruct((blocks, rows, width), jnp.bfloat16),
        cost_estimate=pl.CostEstimate(
            flops=flops,
            transcendentals=blocks * heads * rows * local_keys,
            bytes_accessed=bytes_accessed,
        ),
    )(slot_ids, mask, q, *([incoming] * (group * RAND)), w_kv, o_a, m_a, l_a, token_blocks, w_out)


def local(tokens, w_qkv, w_out, counts, rand_seg, rand_off):
    seq_count = lax.axis_size("seq")
    ctx_count = lax.axis_size("ctx")
    seq_index = lax.axis_index("seq")
    ctx_index = lax.axis_index("ctx")
    dev_count = seq_count * ctx_count
    dev_index = ctx_index * seq_count + seq_index
    tok_rows, model_dim = tokens.shape
    head_total = model_dim // HD
    dev_blocks = tok_rows // BLK
    seg_blocks = dev_blocks * seq_count
    block_total = counts.shape[0]
    capacity = (RAND * dev_blocks + ctx_count - 1) // ctx_count + 1
    first_block = dev_index * dev_blocks
    token_blocks = tokens.reshape(dev_blocks, BLK, model_dim)

    all_owner = rand_seg.reshape(ctx_count, seq_count, dev_blocks * RAND)
    all_offset = rand_off.reshape(ctx_count, seq_count, dev_blocks * RAND)
    col_owner = lax.dynamic_index_in_dim(all_owner, seq_index, axis=1, keepdims=False)
    col_offset = lax.dynamic_index_in_dim(all_offset, seq_index, axis=1, keepdims=False)
    send_off = serve_slots(col_owner, col_offset, ctx_index, capacity)
    outgoing = jnp.take(token_blocks, send_off.reshape(-1), axis=0, mode="clip").reshape(
        ctx_count, capacity, BLK, model_dim
    )
    forward = [(i, i + 1) for i in range(dev_count - 1)]
    backward = [(i + 1, i) for i in range(dev_count - 1)]
    prev_tokens = lax.ppermute(token_blocks[dev_blocks - 1], ("ctx", "seq"), forward)
    next_tokens = lax.ppermute(token_blocks[0], ("ctx", "seq"), backward)

    usable = jnp.arange(BLK, dtype=jnp.int32)[None, :] < lax.dynamic_slice_in_dim(
        counts, first_block, dev_blocks
    )[:, None]
    weighted = jnp.where(usable[:, :, None], token_blocks.astype(jnp.float32), 0.0)
    sums = jnp.sum(weighted, axis=1)
    members = jnp.sum(usable.astype(jnp.float32), axis=1)
    pooled = sums / members[:, None]
    summary = (pooled / jnp.sqrt(jnp.mean(pooled * pooled, axis=1, keepdims=True) + 1e-05)).astype(
        jnp.bfloat16
    )
    copies = jnp.broadcast_to(summary[None], (dev_count,) + summary.shape)
    summary_all = lax.all_to_all(copies, ("ctx", "seq"), 0, 0, tiled=True).reshape(-1, model_dim)
    summary_all, outgoing = lax.optimization_barrier((summary_all, outgoing))
    incoming = lax.all_to_all(outgoing, "ctx", split_axis=0, concat_axis=0, tiled=True)

    w_q, w_k, w_v = split_weights(w_qkv, head_total)
    project = lambda x, w: jnp.dot(x, w, preferred_element_type=jnp.float32).astype(jnp.bfloat16)
    q_own = project(tokens, w_q).reshape(dev_blocks, BLK, model_dim)
    rimmed = jnp.concatenate([prev_tokens, tokens, next_tokens], axis=0)
    k_ext = project(rimmed, w_k).reshape(dev_blocks + 2, BLK, model_dim)
    v_ext = project(rimmed, w_v).reshape(dev_blocks + 2, BLK, model_dim)
    k_sum = project(summary_all, w_k)
    v_sum = project(summary_all, w_v)

    my_owner = lax.dynamic_slice_in_dim(rand_seg, first_block, dev_blocks)
    my_offset = lax.dynamic_slice_in_dim(rand_off, first_block, dev_blocks)
    mine = my_owner.reshape(dev_blocks * RAND)
    slot_ids = mine * capacity + positions_among(mine, ctx_count)

    block_ids = first_block + jnp.arange(dev_blocks, dtype=jnp.int32)
    near_ids = block_ids[:, None] + jnp.arange(-1, 2, dtype=jnp.int32)[None, :]
    existing = (near_ids >= 0) & (near_ids < block_total)
    near_counts = jnp.where(existing, jnp.take(counts, jnp.clip(near_ids, 0, block_total - 1)), 0)
    far_global = my_owner * seg_blocks + seq_index * dev_blocks + my_offset
    far_counts = jnp.take(counts, far_global)
    positions = jnp.arange(BLK, dtype=jnp.int32)[None, None, :]
    near_mask = (positions < near_counts[:, :, None]).astype(jnp.int32).reshape(dev_blocks, 1, -1)
    far_mask = (positions < far_counts[:, :, None]).astype(jnp.int32).reshape(dev_blocks, 1, -1)

    o_a, m_a, l_a = attend_near(near_mask, q_own, k_ext, v_ext, k_sum, v_sum)
    mixed = attend_far(
        slot_ids,
        far_mask,
        q_own,
        incoming.reshape(ctx_count * capacity, BLK, model_dim),
        jnp.concatenate([w_k, w_v], axis=1),
        o_a,
        m_a,
        l_a,
        token_blocks,
        w_out,
    )
    return mixed.reshape(tok_rows, model_dim)


def solution(mesh):
    in_specs = (P(("ctx", "seq"), None), P(), P(), P(), P(), P())
    out_specs = P(("ctx", "seq"), None)
    return jax.shard_map(local, mesh=mesh, in_specs=in_specs, out_specs=out_specs, check_vma=False)
```

```python
import functools
import math

import jax
import jax.numpy as jnp
from jax import lax
from jax.experimental import pallas as pl
from jax.experimental.pallas import tpu as pltpu
from jax.sharding import PartitionSpec as P

HD = 64
BLK = 64
RAND = 3
LANES = 128


def positions_among(owners, owner_count):
    marks = (owners[..., None] == jnp.arange(owner_count, dtype=jnp.int32)).astype(jnp.int32)
    ranks = jnp.cumsum(marks, axis=-2) - 1
    return jnp.sum(ranks * marks, axis=-1)


def serve_slots(owners, offsets, target, capacity):
    matched = owners == target
    ranks = jnp.cumsum(matched.astype(jnp.int32), axis=-1) - 1
    slot_hit = matched[..., None, :] & (
        ranks[..., None, :] == jnp.arange(capacity, dtype=jnp.int32)[:, None]
    )
    return jnp.sum(jnp.where(slot_hit, offsets[..., None, :], 0), axis=-1)


def split_weights(w_qkv, head_total):
    model_dim = w_qkv.shape[0]
    shaped = w_qkv.reshape(model_dim, head_total, 3, HD)
    return [shaped[:, :, j, :].reshape(model_dim, head_total * HD) for j in range(3)]


def pair_rows(q, low):
    blank = jnp.zeros_like(q)
    return jnp.concatenate([jnp.where(low, q, blank), jnp.where(low, blank, q)], axis=0)


def pick_rows(x, low, rows):
    return jnp.where(low, x[:rows], x[rows:])


CONTRACT = (((1,), (1,)), ((), ()))


def near_kernel(mask_ref, q_ref, kp_ref, kc_ref, kn_ref, vp_ref, vc_ref, vn_ref, ks_ref, vs_ref,
                o_ref, m_ref, l_ref):
    width = q_ref.shape[-1]
    rows = q_ref.shape[1]
    scaling = 1.0 / math.sqrt(HD)
    valid = mask_ref[0] != 0
    low = lax.broadcasted_iota(jnp.int32, (rows, LANES), 1) < HD
    for tile in range(width // LANES):
        cols = pl.ds(tile * LANES, LANES)
        q_pair = pair_rows(q_ref[0, :, cols], low)
        k_local = jnp.concatenate([kp_ref[0, :, cols], kc_ref[0, :, cols], kn_ref[0, :, cols]], axis=0)
        v_local = jnp.concatenate([vp_ref[0, :, cols], vc_ref[0, :, cols], vn_ref[0, :, cols]], axis=0)
        near = lax.dot_general(q_pair, k_local, CONTRACT, preferred_element_type=jnp.float32)
        near = jnp.where(valid, near * scaling, -jnp.inf)
        wide = lax.dot_general(q_pair, ks_ref[:, cols], CONTRACT, preferred_element_type=jnp.float32)
        wide = wide * scaling
        peak = jnp.maximum(
            jnp.max(near, axis=-1, keepdims=True), jnp.max(wide, axis=-1, keepdims=True)
        )
        near_exp = jnp.exp(near - peak)
        wide_exp = jnp.exp(wide - peak)
        total = jnp.sum(near_exp, axis=-1, keepdims=True) + jnp.sum(wide_exp, axis=-1, keepdims=True)
        result = jnp.dot(near_exp.astype(jnp.bfloat16), v_local, preferred_element_type=jnp.float32)
        result = result + jnp.dot(
            wide_exp.astype(jnp.bfloat16), vs_ref[:, cols], preferred_element_type=jnp.float32
        )
        o_ref[0, :, cols] = pick_rows(result, low, rows)
        m_ref[0, :, cols] = pick_rows(jnp.broadcast_to(peak, result.shape), low, rows)
        l_ref[0, :, cols] = pick_rows(jnp.broadcast_to(total, result.shape), low, rows)


def far_kernel(group, ids_ref, mask_ref, q_ref, *refs):
    token_refs = refs[: group * RAND]
    wkv_ref, oa_ref, ma_ref, la_ref, tok_ref, wo_ref, out_ref, att_ref = refs[group * RAND :]
    width = q_ref.shape[-1]
    rows = q_ref.shape[1]
    scaling = 1.0 / math.sqrt(HD)
    low = lax.broadcasted_iota(jnp.int32, (rows, LANES), 1) < HD
    far_tokens = jnp.concatenate([ref[0] for ref in token_refs], axis=0)
    kv_far = jnp.dot(far_tokens, wkv_ref[...], preferred_element_type=jnp.float32).astype(
        jnp.bfloat16
    )
    keys = RAND * rows
    for g in range(group):
        valid = mask_ref[g] != 0
        kv_rows = kv_far[g * keys : (g + 1) * keys]
        for tile in range(width // LANES):
            lanes = slice(tile * LANES, (tile + 1) * LANES)
            value_lanes = slice(width + tile * LANES, width + (tile + 1) * LANES)
            cols = pl.ds(tile * LANES, LANES)
            q_pair = pair_rows(q_ref[g, :, cols], low)
            scores = lax.dot_general(
                q_pair, kv_rows[:, lanes], CONTRACT, preferred_element_type=jnp.float32
            )
            scores = jnp.where(valid, scores * scaling, -jnp.inf)
            peak = jnp.max(scores, axis=-1, keepdims=True)
            exps = jnp.exp(scores - peak)
            total = jnp.sum(exps, axis=-1, keepdims=True)
            result = jnp.dot(
                exps.astype(jnp.bfloat16), kv_rows[:, value_lanes], preferred_element_type=jnp.float32
            )
            o_b = pick_rows(result, low, rows)
            m_b = pick_rows(jnp.broadcast_to(peak, result.shape), low, rows)
            l_b = pick_rows(jnp.broadcast_to(total, result.shape), low, rows)
            m_a = ma_ref[g, :, cols]
            peak_all = jnp.maximum(m_a, m_b)
            scale_a = jnp.exp(m_a - peak_all)
            scale_b = jnp.exp(m_b - peak_all)
            numerator = oa_ref[g, :, cols] * scale_a + o_b * scale_b
            denominator = la_ref[g, :, cols] * scale_a + l_b * scale_b
            att_ref[g * rows : (g + 1) * rows, cols] = (numerator / denominator).astype(att_ref.dtype)
    mixed = jnp.dot(att_ref[...], wo_ref[...], preferred_element_type=jnp.float32)
    for g in range(group):
        part = mixed[g * rows : (g + 1) * rows] + tok_ref[g].astype(jnp.float32)
        out_ref[g] = part.astype(out_ref.dtype)


def attend_near(mask, q, k_ext, v_ext, k_sum, v_sum):
    blocks, rows, width = q.shape
    keys = k_sum.shape[0]
    block = lambda offset: pl.BlockSpec((1, rows, width), lambda i: (i + offset, 0, 0))
    whole = pl.BlockSpec((keys, width), lambda i: (0, 0))
    local_keys = 3 * rows
    heads = width // HD
    flops = blocks * heads * 2 * rows * 2 * LANES * (local_keys + keys)
    bytes_accessed = 2 * (blocks * rows * width * 7 + 2 * keys * width) + 12 * blocks * rows * width
    part = jax.ShapeDtypeStruct((blocks, rows, width), jnp.float32)
    return pl.pallas_call(
        near_kernel,
        grid=(blocks,),
        in_specs=[pl.BlockSpec((1, 1, local_keys), lambda i: (i, 0, 0)), block(0)]
        + [block(0), block(1), block(2)] * 2
        + [whole, whole],
        out_specs=[block(0)] * 3,
        out_shape=[part] * 3,
        cost_estimate=pl.CostEstimate(
            flops=flops,
            transcendentals=blocks * heads * rows * (local_keys + keys),
            bytes_accessed=bytes_accessed,
        ),
    )(mask, q, k_ext, k_ext, k_ext, v_ext, v_ext, v_ext, k_sum, v_sum)


def attend_far(slot_ids, mask, q, incoming, w_kv, o_a, m_a, l_a, token_blocks, w_out):
    blocks, rows, width = q.shape
    model_dim = incoming.shape[-1]
    group = 2 if blocks % 2 == 0 else 1
    block = pl.BlockSpec((group, rows, width), lambda i, ids: (i, 0, 0))
    token_specs = [
        pl.BlockSpec(
            (1, rows, model_dim), lambda i, ids, n=n: (ids[RAND * group * i + n], 0, 0)
        )
        for n in range(group * RAND)
    ]
    weight = pl.BlockSpec(w_kv.shape, lambda i, ids: (0, 0))
    local_keys = RAND * rows
    heads = width // HD
    flops = blocks * (
        heads * 2 * rows * 2 * LANES * local_keys + 2 * local_keys * model_dim * 2 * width
    )
    bytes_accessed = 2 * blocks * rows * (width * 2 + model_dim * RAND) + 2 * w_kv.size + (
        12 * blocks * rows * width
    )
    grid_spec = pltpu.PrefetchScalarGridSpec(
        num_scalar_prefetch=1,
        grid=(blocks // group,),
        in_specs=[pl.BlockSpec((group, 1, local_keys), lambda i, ids: (i, 0, 0)), block]
        + token_specs
        + [weight, block, block, block, block, pl.BlockSpec(w_out.shape, lambda i, ids: (0, 0))],
        out_specs=block,
        scratch_shapes=[pltpu.VMEM((group * rows, width), jnp.bfloat16)],
    )
    return pl.pallas_call(
        functools.partial(far_kernel, group),
        grid_spec=grid_spec,
        out_shape=jax.ShapeDtypeStruct((blocks, rows, width), jnp.bfloat16),
        cost_estimate=pl.CostEstimate(
            flops=flops,
            transcendentals=blocks * heads * rows * local_keys,
            bytes_accessed=bytes_accessed,
        ),
    )(slot_ids, mask, q, *([incoming] * (group * RAND)), w_kv, o_a, m_a, l_a, token_blocks, w_out)


def local(tokens, w_qkv, w_out, counts, rand_seg, rand_off):
    seq_count = lax.axis_size("seq")
    ctx_count = lax.axis_size("ctx")
    seq_index = lax.axis_index("seq")
    ctx_index = lax.axis_index("ctx")
    dev_count = seq_count * ctx_count
    dev_index = ctx_index * seq_count + seq_index
    tok_rows, model_dim = tokens.shape
    head_total = model_dim // HD
    dev_blocks = tok_rows // BLK
    seg_blocks = dev_blocks * seq_count
    block_total = counts.shape[0]
    capacity = (RAND * dev_blocks + ctx_count - 1) // ctx_count + 1
    first_block = dev_index * dev_blocks
    token_blocks = tokens.reshape(dev_blocks, BLK, model_dim)

    all_owner = rand_seg.reshape(ctx_count, seq_count, dev_blocks * RAND)
    all_offset = rand_off.reshape(ctx_count, seq_count, dev_blocks * RAND)
    col_owner = lax.dynamic_index_in_dim(all_owner, seq_index, axis=1, keepdims=False)
    col_offset = lax.dynamic_index_in_dim(all_offset, seq_index, axis=1, keepdims=False)
    send_off = serve_slots(col_owner, col_offset, ctx_index, capacity)
    outgoing = jnp.take(token_blocks, send_off.reshape(-1), axis=0, mode="clip").reshape(
        ctx_count, capacity, BLK, model_dim
    )
    forward = [(i, i + 1) for i in range(dev_count - 1)]
    backward = [(i + 1, i) for i in range(dev_count - 1)]
    prev_tokens = lax.ppermute(token_blocks[dev_blocks - 1], ("ctx", "seq"), forward)
    next_tokens = lax.ppermute(token_blocks[0], ("ctx", "seq"), backward)

    own = (first_block + jnp.arange(dev_blocks, dtype=jnp.int32))[:, None] == jnp.arange(
        block_total, dtype=jnp.int32
    )[None, :]
    own_counts = jnp.sum(jnp.where(own, counts[None, :], 0), axis=1)
    usable = jnp.arange(BLK, dtype=jnp.int32)[None, :] < own_counts[:, None]
    weighted = jnp.where(usable[:, :, None], token_blocks.astype(jnp.float32), 0.0)
    sums = jnp.sum(weighted, axis=1)
    members = jnp.sum(usable.astype(jnp.float32), axis=1)
    pooled = sums / members[:, None]
    scale = jnp.sqrt(jnp.mean(pooled * pooled, axis=1, keepdims=True) + 1e-05)
    copies = jnp.broadcast_to(pooled[None], (dev_count,) + pooled.shape)
    copies = (copies / jnp.broadcast_to(scale[None], (dev_count,) + scale.shape)).astype(jnp.bfloat16)
    summary_all = lax.all_to_all(copies, ("ctx", "seq"), 0, 0, tiled=True).reshape(-1, model_dim)
    summary_all, outgoing = lax.optimization_barrier((summary_all, outgoing))
    incoming = lax.all_to_all(outgoing, "ctx", split_axis=0, concat_axis=0, tiled=True)

    w_q, w_k, w_v = split_weights(w_qkv, head_total)
    project = lambda x, w: jnp.dot(x, w, preferred_element_type=jnp.float32).astype(jnp.bfloat16)
    q_own = project(tokens, w_q).reshape(dev_blocks, BLK, model_dim)
    rimmed = jnp.concatenate([prev_tokens, tokens, next_tokens], axis=0)
    k_ext = project(rimmed, w_k).reshape(dev_blocks + 2, BLK, model_dim)
    v_ext = project(rimmed, w_v).reshape(dev_blocks + 2, BLK, model_dim)
    k_sum = project(summary_all, w_k)
    v_sum = project(summary_all, w_v)

    my_owner = lax.dynamic_slice_in_dim(rand_seg, first_block, dev_blocks)
    my_offset = lax.dynamic_slice_in_dim(rand_off, first_block, dev_blocks)
    mine = my_owner.reshape(dev_blocks * RAND)
    slot_ids = mine * capacity + positions_among(mine, ctx_count)

    block_ids = first_block + jnp.arange(dev_blocks, dtype=jnp.int32)
    near_ids = block_ids[:, None] + jnp.arange(-1, 2, dtype=jnp.int32)[None, :]
    existing = (near_ids >= 0) & (near_ids < block_total)
    near_counts = jnp.where(existing, jnp.take(counts, jnp.clip(near_ids, 0, block_total - 1)), 0)
    far_global = my_owner * seg_blocks + seq_index * dev_blocks + my_offset
    far_counts = jnp.take(counts, far_global)
    positions = jnp.arange(BLK, dtype=jnp.int32)[None, None, :]
    near_mask = (positions < near_counts[:, :, None]).astype(jnp.int32).reshape(dev_blocks, 1, -1)
    far_mask = (positions < far_counts[:, :, None]).astype(jnp.int32).reshape(dev_blocks, 1, -1)

    o_a, m_a, l_a = attend_near(near_mask, q_own, k_ext, v_ext, k_sum, v_sum)
    mixed = attend_far(
        slot_ids,
        far_mask,
        q_own,
        incoming.reshape(ctx_count * capacity, BLK, model_dim),
        jnp.concatenate([w_k, w_v], axis=1),
        o_a,
        m_a,
        l_a,
        token_blocks,
        w_out,
    )
    return mixed.reshape(tok_rows, model_dim)


def solution(mesh):
    in_specs = (P(("ctx", "seq"), None), P(), P(), P(), P(), P())
    out_specs = P(("ctx", "seq"), None)
    return jax.shard_map(local, mesh=mesh, in_specs=in_specs, out_specs=out_specs, check_vma=False)
```

```python
import functools
import math

import jax
import jax.numpy as jnp
from jax import lax
from jax.experimental import pallas as pl
from jax.experimental.pallas import tpu as pltpu
from jax.sharding import PartitionSpec as P

HD = 64
BLK = 64
RAND = 3
LANES = 128


def positions_among(owners, owner_count):
    marks = (owners[..., None] == jnp.arange(owner_count, dtype=jnp.int32)).astype(jnp.int32)
    ranks = jnp.cumsum(marks, axis=-2) - 1
    return jnp.sum(ranks * marks, axis=-1)


def serve_slots(owners, offsets, target, capacity):
    matched = owners == target
    ranks = jnp.cumsum(matched.astype(jnp.int32), axis=-1) - 1
    slot_hit = matched[..., None, :] & (
        ranks[..., None, :] == jnp.arange(capacity, dtype=jnp.int32)[:, None]
    )
    return jnp.sum(jnp.where(slot_hit, offsets[..., None, :], 0), axis=-1)


def split_weights(w_qkv, head_total):
    model_dim = w_qkv.shape[0]
    shaped = w_qkv.reshape(model_dim, head_total, 3, HD)
    return [shaped[:, :, j, :].reshape(model_dim, head_total * HD) for j in range(3)]


def pair_rows(q, low):
    blank = jnp.zeros_like(q)
    return jnp.concatenate([jnp.where(low, q, blank), jnp.where(low, blank, q)], axis=0)


def pick_rows(x, low, rows):
    return jnp.where(low, x[:rows], x[rows:])


CONTRACT = (((1,), (1,)), ((), ()))


def near_kernel(mask_ref, q_ref, kp_ref, kc_ref, kn_ref, vp_ref, vc_ref, vn_ref, ks_ref, vs_ref,
                o_ref, m_ref, l_ref):
    width = q_ref.shape[-1]
    rows = q_ref.shape[1]
    scaling = 1.0 / math.sqrt(HD)
    valid = mask_ref[0] != 0
    low = lax.broadcasted_iota(jnp.int32, (rows, LANES), 1) < HD
    for tile in range(width // LANES):
        cols = pl.ds(tile * LANES, LANES)
        q_pair = pair_rows(q_ref[0, :, cols], low)
        k_local = jnp.concatenate([kp_ref[0, :, cols], kc_ref[0, :, cols], kn_ref[0, :, cols]], axis=0)
        v_local = jnp.concatenate([vp_ref[0, :, cols], vc_ref[0, :, cols], vn_ref[0, :, cols]], axis=0)
        near = lax.dot_general(q_pair, k_local, CONTRACT, preferred_element_type=jnp.float32)
        near = jnp.where(valid, near * scaling, -jnp.inf)
        wide = lax.dot_general(q_pair, ks_ref[:, cols], CONTRACT, preferred_element_type=jnp.float32)
        wide = wide * scaling
        peak = jnp.maximum(
            jnp.max(near, axis=-1, keepdims=True), jnp.max(wide, axis=-1, keepdims=True)
        )
        near_exp = jnp.exp(near - peak)
        wide_exp = jnp.exp(wide - peak)
        total = jnp.sum(near_exp, axis=-1, keepdims=True) + jnp.sum(wide_exp, axis=-1, keepdims=True)
        result = jnp.dot(near_exp.astype(jnp.bfloat16), v_local, preferred_element_type=jnp.float32)
        result = result + jnp.dot(
            wide_exp.astype(jnp.bfloat16), vs_ref[:, cols], preferred_element_type=jnp.float32
        )
        o_ref[0, :, cols] = pick_rows(result, low, rows)
        m_ref[0, :, cols] = pick_rows(jnp.broadcast_to(peak, result.shape), low, rows)
        l_ref[0, :, cols] = pick_rows(jnp.broadcast_to(total, result.shape), low, rows)


def far_kernel(group, ids_ref, mask_ref, q_ref, *refs):
    token_refs = refs[: group * RAND]
    wkv_ref, oa_ref, ma_ref, la_ref, tok_ref, wo_ref, out_ref, att_ref = refs[group * RAND :]
    width = q_ref.shape[-1]
    rows = q_ref.shape[1]
    scaling = 1.0 / math.sqrt(HD)
    low = lax.broadcasted_iota(jnp.int32, (rows, LANES), 1) < HD
    for g in range(group):
        valid = mask_ref[g] != 0
        far_tokens = jnp.concatenate(
            [ref[0] for ref in token_refs[g * RAND : (g + 1) * RAND]], axis=0
        )
        kv_rows = jnp.dot(far_tokens, wkv_ref[...], preferred_element_type=jnp.float32).astype(
            jnp.bfloat16
        )
        for tile in range(width // LANES):
            lanes = slice(tile * LANES, (tile + 1) * LANES)
            value_lanes = slice(width + tile * LANES, width + (tile + 1) * LANES)
            cols = pl.ds(tile * LANES, LANES)
            q_pair = pair_rows(q_ref[g, :, cols], low)
            scores = lax.dot_general(
                q_pair, kv_rows[:, lanes], CONTRACT, preferred_element_type=jnp.float32
            )
            scores = jnp.where(valid, scores * scaling, -jnp.inf)
            peak = jnp.max(scores, axis=-1, keepdims=True)
            exps = jnp.exp(scores - peak)
            total = jnp.sum(exps, axis=-1, keepdims=True)
            result = jnp.dot(
                exps.astype(jnp.bfloat16), kv_rows[:, value_lanes], preferred_element_type=jnp.float32
            )
            o_b = pick_rows(result, low, rows)
            m_b = pick_rows(jnp.broadcast_to(peak, result.shape), low, rows)
            l_b = pick_rows(jnp.broadcast_to(total, result.shape), low, rows)
            m_a = ma_ref[g, :, cols]
            peak_all = jnp.maximum(m_a, m_b)
            scale_a = jnp.exp(m_a - peak_all)
            scale_b = jnp.exp(m_b - peak_all)
            numerator = oa_ref[g, :, cols] * scale_a + o_b * scale_b
            denominator = la_ref[g, :, cols] * scale_a + l_b * scale_b
            att_ref[g * rows : (g + 1) * rows, cols] = (numerator / denominator).astype(att_ref.dtype)
    mixed = jnp.dot(att_ref[...], wo_ref[...], preferred_element_type=jnp.float32)
    for g in range(group):
        part = mixed[g * rows : (g + 1) * rows] + tok_ref[g].astype(jnp.float32)
        out_ref[g] = part.astype(out_ref.dtype)


def attend_near(mask, q, k_ext, v_ext, k_sum, v_sum):
    blocks, rows, width = q.shape
    keys = k_sum.shape[0]
    block = lambda offset: pl.BlockSpec((1, rows, width), lambda i: (i + offset, 0, 0))
    whole = pl.BlockSpec((keys, width), lambda i: (0, 0))
    local_keys = 3 * rows
    heads = width // HD
    flops = blocks * heads * 2 * rows * 2 * LANES * (local_keys + keys)
    bytes_accessed = 2 * (blocks * rows * width * 7 + 2 * keys * width) + 12 * blocks * rows * width
    part = jax.ShapeDtypeStruct((blocks, rows, width), jnp.float32)
    return pl.pallas_call(
        near_kernel,
        grid=(blocks,),
        in_specs=[pl.BlockSpec((1, 1, local_keys), lambda i: (i, 0, 0)), block(0)]
        + [block(0), block(1), block(2)] * 2
        + [whole, whole],
        out_specs=[block(0)] * 3,
        out_shape=[part] * 3,
        cost_estimate=pl.CostEstimate(
            flops=flops,
            transcendentals=blocks * heads * rows * (local_keys + keys),
            bytes_accessed=bytes_accessed,
        ),
    )(mask, q, k_ext, k_ext, k_ext, v_ext, v_ext, v_ext, k_sum, v_sum)


def attend_far(slot_ids, mask, q, incoming, w_kv, o_a, m_a, l_a, token_blocks, w_out):
    blocks, rows, width = q.shape
    model_dim = incoming.shape[-1]
    group = 2 if blocks % 2 == 0 else 1
    block = pl.BlockSpec((group, rows, width), lambda i, ids: (i, 0, 0))
    token_specs = [
        pl.BlockSpec(
            (1, rows, model_dim), lambda i, ids, n=n: (ids[RAND * group * i + n], 0, 0)
        )
        for n in range(group * RAND)
    ]
    weight = pl.BlockSpec(w_kv.shape, lambda i, ids: (0, 0))
    local_keys = RAND * rows
    heads = width // HD
    flops = blocks * (
        heads * 2 * rows * 2 * LANES * local_keys + 2 * local_keys * model_dim * 2 * width
    )
    bytes_accessed = 2 * blocks * rows * (width * 2 + model_dim * RAND) + 2 * w_kv.size + (
        12 * blocks * rows * width
    )
    grid_spec = pltpu.PrefetchScalarGridSpec(
        num_scalar_prefetch=1,
        grid=(blocks // group,),
        in_specs=[pl.BlockSpec((group, 1, local_keys), lambda i, ids: (i, 0, 0)), block]
        + token_specs
        + [weight, block, block, block, block, pl.BlockSpec(w_out.shape, lambda i, ids: (0, 0))],
        out_specs=block,
        scratch_shapes=[pltpu.VMEM((group * rows, width), jnp.bfloat16)],
    )
    return pl.pallas_call(
        functools.partial(far_kernel, group),
        grid_spec=grid_spec,
        out_shape=jax.ShapeDtypeStruct((blocks, rows, width), jnp.bfloat16),
        cost_estimate=pl.CostEstimate(
            flops=flops,
            transcendentals=blocks * heads * rows * local_keys,
            bytes_accessed=bytes_accessed,
        ),
    )(slot_ids, mask, q, *([incoming] * (group * RAND)), w_kv, o_a, m_a, l_a, token_blocks, w_out)


def local(tokens, w_qkv, w_out, counts, rand_seg, rand_off):
    seq_count = lax.axis_size("seq")
    ctx_count = lax.axis_size("ctx")
    seq_index = lax.axis_index("seq")
    ctx_index = lax.axis_index("ctx")
    dev_count = seq_count * ctx_count
    dev_index = ctx_index * seq_count + seq_index
    tok_rows, model_dim = tokens.shape
    head_total = model_dim // HD
    dev_blocks = tok_rows // BLK
    seg_blocks = dev_blocks * seq_count
    block_total = counts.shape[0]
    capacity = (RAND * dev_blocks + ctx_count - 1) // ctx_count + 1
    first_block = dev_index * dev_blocks
    token_blocks = tokens.reshape(dev_blocks, BLK, model_dim)

    all_owner = rand_seg.reshape(ctx_count, seq_count, dev_blocks * RAND)
    all_offset = rand_off.reshape(ctx_count, seq_count, dev_blocks * RAND)
    col_owner = lax.dynamic_index_in_dim(all_owner, seq_index, axis=1, keepdims=False)
    col_offset = lax.dynamic_index_in_dim(all_offset, seq_index, axis=1, keepdims=False)
    send_off = serve_slots(col_owner, col_offset, ctx_index, capacity)
    outgoing = jnp.take(token_blocks, send_off.reshape(-1), axis=0, mode="clip").reshape(
        ctx_count, capacity, BLK, model_dim
    )
    forward = [(i, i + 1) for i in range(dev_count - 1)]
    backward = [(i + 1, i) for i in range(dev_count - 1)]
    prev_tokens = lax.ppermute(token_blocks[dev_blocks - 1], ("ctx", "seq"), forward)
    next_tokens = lax.ppermute(token_blocks[0], ("ctx", "seq"), backward)

    own = (first_block + jnp.arange(dev_blocks, dtype=jnp.int32))[:, None] == jnp.arange(
        block_total, dtype=jnp.int32
    )[None, :]
    own_counts = jnp.sum(jnp.where(own, counts[None, :], 0), axis=1)
    usable = jnp.arange(BLK, dtype=jnp.int32)[None, :] < own_counts[:, None]
    weighted = jnp.where(usable[:, :, None], token_blocks.astype(jnp.float32), 0.0)
    sums = jnp.sum(weighted, axis=1)
    members = jnp.sum(usable.astype(jnp.float32), axis=1)
    pooled = sums / members[:, None]
    scale = jnp.sqrt(jnp.mean(pooled * pooled, axis=1, keepdims=True) + 1e-05)
    copies = jnp.broadcast_to(pooled[None], (dev_count,) + pooled.shape)
    copies = (copies / jnp.broadcast_to(scale[None], (dev_count,) + scale.shape)).astype(jnp.bfloat16)
    summary_all = lax.all_to_all(copies, ("ctx", "seq"), 0, 0, tiled=True).reshape(-1, model_dim)
    summary_all, outgoing = lax.optimization_barrier((summary_all, outgoing))
    incoming = lax.all_to_all(outgoing, "ctx", split_axis=0, concat_axis=0, tiled=True)

    w_q, w_k, w_v = split_weights(w_qkv, head_total)
    project = lambda x, w: jnp.dot(x, w, preferred_element_type=jnp.float32).astype(jnp.bfloat16)
    q_own = project(tokens, w_q).reshape(dev_blocks, BLK, model_dim)
    rimmed = jnp.concatenate([prev_tokens, tokens, next_tokens], axis=0)
    k_ext = project(rimmed, w_k).reshape(dev_blocks + 2, BLK, model_dim)
    v_ext = project(rimmed, w_v).reshape(dev_blocks + 2, BLK, model_dim)
    k_sum = project(summary_all, w_k)
    v_sum = project(summary_all, w_v)

    my_owner = lax.dynamic_slice_in_dim(rand_seg, first_block, dev_blocks)
    my_offset = lax.dynamic_slice_in_dim(rand_off, first_block, dev_blocks)
    mine = my_owner.reshape(dev_blocks * RAND)
    slot_ids = mine * capacity + positions_among(mine, ctx_count)

    block_ids = first_block + jnp.arange(dev_blocks, dtype=jnp.int32)
    near_ids = block_ids[:, None] + jnp.arange(-1, 2, dtype=jnp.int32)[None, :]
    existing = (near_ids >= 0) & (near_ids < block_total)
    near_counts = jnp.where(existing, jnp.take(counts, jnp.clip(near_ids, 0, block_total - 1)), 0)
    far_global = my_owner * seg_blocks + seq_index * dev_blocks + my_offset
    far_counts = jnp.take(counts, far_global)
    positions = jnp.arange(BLK, dtype=jnp.int32)[None, None, :]
    near_mask = (positions < near_counts[:, :, None]).astype(jnp.int32).reshape(dev_blocks, 1, -1)
    far_mask = (positions < far_counts[:, :, None]).astype(jnp.int32).reshape(dev_blocks, 1, -1)

    o_a, m_a, l_a = attend_near(near_mask, q_own, k_ext, v_ext, k_sum, v_sum)
    mixed = attend_far(
        slot_ids,
        far_mask,
        q_own,
        incoming.reshape(ctx_count * capacity, BLK, model_dim),
        jnp.concatenate([w_k, w_v], axis=1),
        o_a,
        m_a,
        l_a,
        token_blocks,
        w_out,
    )
    return mixed.reshape(tok_rows, model_dim)


def solution(mesh):
    in_specs = (P(("ctx", "seq"), None), P(), P(), P(), P(), P())
    out_specs = P(("ctx", "seq"), None)
    return jax.shard_map(local, mesh=mesh, in_specs=in_specs, out_specs=out_specs, check_vma=False)
```

```python
import functools
import math

import jax
import jax.numpy as jnp
from jax import lax
from jax.experimental import pallas as pl
from jax.experimental.pallas import tpu as pltpu
from jax.sharding import PartitionSpec as P

HD = 64
BLK = 64
RAND = 3
LANES = 128


def positions_among(owners, owner_count):
    marks = (owners[..., None] == jnp.arange(owner_count, dtype=jnp.int32)).astype(jnp.int32)
    ranks = jnp.cumsum(marks, axis=-2) - 1
    return jnp.sum(ranks * marks, axis=-1)


def serve_slots(owners, offsets, target, capacity):
    matched = owners == target
    ranks = jnp.cumsum(matched.astype(jnp.int32), axis=-1) - 1
    slot_hit = matched[..., None, :] & (
        ranks[..., None, :] == jnp.arange(capacity, dtype=jnp.int32)[:, None]
    )
    return jnp.sum(jnp.where(slot_hit, offsets[..., None, :], 0), axis=-1)


def split_weights(w_qkv, head_total):
    model_dim = w_qkv.shape[0]
    shaped = w_qkv.reshape(model_dim, head_total, 3, HD)
    return [shaped[:, :, j, :].reshape(model_dim, head_total * HD) for j in range(3)]


def pair_rows(q, low):
    blank = jnp.zeros_like(q)
    return jnp.concatenate([jnp.where(low, q, blank), jnp.where(low, blank, q)], axis=0)


def pick_rows(x, low, rows):
    return jnp.where(low, x[:rows], x[rows:])


CONTRACT = (((1,), (1,)), ((), ()))


def near_kernel(mask_ref, q_ref, kp_ref, kc_ref, kn_ref, vp_ref, vc_ref, vn_ref, ks_ref, vs_ref,
                o_ref, m_ref, l_ref):
    width = q_ref.shape[-1]
    rows = q_ref.shape[1]
    scaling = 1.0 / math.sqrt(HD)
    valid = mask_ref[0] != 0
    low = lax.broadcasted_iota(jnp.int32, (rows, LANES), 1) < HD
    for tile in range(width // LANES):
        cols = pl.ds(tile * LANES, LANES)
        q_pair = pair_rows(q_ref[0, :, cols], low)
        k_local = jnp.concatenate([kp_ref[0, :, cols], kc_ref[0, :, cols], kn_ref[0, :, cols]], axis=0)
        v_local = jnp.concatenate([vp_ref[0, :, cols], vc_ref[0, :, cols], vn_ref[0, :, cols]], axis=0)
        near = lax.dot_general(q_pair, k_local, CONTRACT, preferred_element_type=jnp.float32)
        near = jnp.where(valid, near * scaling, -jnp.inf)
        wide = lax.dot_general(q_pair, ks_ref[:, cols], CONTRACT, preferred_element_type=jnp.float32)
        wide = wide * scaling
        peak = jnp.maximum(
            jnp.max(near, axis=-1, keepdims=True), jnp.max(wide, axis=-1, keepdims=True)
        )
        near_exp = jnp.exp(near - peak)
        wide_exp = jnp.exp(wide - peak)
        total = jnp.sum(near_exp, axis=-1, keepdims=True) + jnp.sum(wide_exp, axis=-1, keepdims=True)
        result = jnp.dot(near_exp.astype(jnp.bfloat16), v_local, preferred_element_type=jnp.float32)
        result = result + jnp.dot(
            wide_exp.astype(jnp.bfloat16), vs_ref[:, cols], preferred_element_type=jnp.float32
        )
        o_ref[0, :, cols] = pick_rows(result, low, rows)
        m_ref[0, :, cols] = pick_rows(jnp.broadcast_to(peak, result.shape), low, rows)
        l_ref[0, :, cols] = pick_rows(jnp.broadcast_to(total, result.shape), low, rows)


def far_kernel(group, ids_ref, mask_ref, q_ref, *refs):
    token_refs = refs[: group * RAND]
    wkv_ref, oa_ref, ma_ref, la_ref, tok_ref, wo_ref, out_ref, att_ref = refs[group * RAND :]
    width = q_ref.shape[-1]
    rows = q_ref.shape[1]
    scaling = 1.0 / math.sqrt(HD)
    low = lax.broadcasted_iota(jnp.int32, (rows, LANES), 1) < HD
    for g in range(group):
        valid = mask_ref[g] != 0
        far_tokens = jnp.concatenate(
            [ref[0] for ref in token_refs[g * RAND : (g + 1) * RAND]], axis=0
        )
        kv_rows = jnp.dot(far_tokens, wkv_ref[...], preferred_element_type=jnp.float32).astype(
            jnp.bfloat16
        )
        for tile in range(width // LANES):
            lanes = slice(tile * LANES, (tile + 1) * LANES)
            value_lanes = slice(width + tile * LANES, width + (tile + 1) * LANES)
            cols = pl.ds(tile * LANES, LANES)
            q_pair = pair_rows(q_ref[g, :, cols], low)
            scores = lax.dot_general(
                q_pair, kv_rows[:, lanes], CONTRACT, preferred_element_type=jnp.float32
            )
            scores = jnp.where(valid, scores * scaling, -jnp.inf)
            peak = jnp.max(scores, axis=-1, keepdims=True)
            exps = jnp.exp(scores - peak)
            total = jnp.sum(exps, axis=-1, keepdims=True)
            result = jnp.dot(
                exps.astype(jnp.bfloat16), kv_rows[:, value_lanes], preferred_element_type=jnp.float32
            )
            o_b = pick_rows(result, low, rows)
            m_b = pick_rows(jnp.broadcast_to(peak, result.shape), low, rows)
            l_b = pick_rows(jnp.broadcast_to(total, result.shape), low, rows)
            m_a = ma_ref[g, :, cols]
            peak_all = jnp.maximum(m_a, m_b)
            scale_a = jnp.exp(m_a - peak_all)
            scale_b = jnp.exp(m_b - peak_all)
            numerator = oa_ref[g, :, cols] * scale_a + o_b * scale_b
            denominator = la_ref[g, :, cols] * scale_a + l_b * scale_b
            att_ref[g * rows : (g + 1) * rows, cols] = (numerator / denominator).astype(att_ref.dtype)
    mixed = jnp.dot(att_ref[...], wo_ref[...], preferred_element_type=jnp.float32)
    for g in range(group):
        part = mixed[g * rows : (g + 1) * rows] + tok_ref[g].astype(jnp.float32)
        out_ref[g] = part.astype(out_ref.dtype)


def attend_near(mask, q, k_ext, v_ext, k_sum, v_sum):
    blocks, rows, width = q.shape
    keys = k_sum.shape[0]
    block = lambda offset: pl.BlockSpec((1, rows, width), lambda i: (i + offset, 0, 0))
    whole = pl.BlockSpec((keys, width), lambda i: (0, 0))
    local_keys = 3 * rows
    heads = width // HD
    flops = blocks * heads * 2 * rows * 2 * LANES * (local_keys + keys)
    bytes_accessed = 2 * (blocks * rows * width * 7 + 2 * keys * width) + 12 * blocks * rows * width
    part = jax.ShapeDtypeStruct((blocks, rows, width), jnp.float32)
    return pl.pallas_call(
        near_kernel,
        grid=(blocks,),
        in_specs=[pl.BlockSpec((1, 1, local_keys), lambda i: (i, 0, 0)), block(0)]
        + [block(0), block(1), block(2)] * 2
        + [whole, whole],
        out_specs=[block(0)] * 3,
        out_shape=[part] * 3,
        cost_estimate=pl.CostEstimate(
            flops=flops,
            transcendentals=blocks * heads * rows * (local_keys + keys),
            bytes_accessed=bytes_accessed,
        ),
    )(mask, q, k_ext, k_ext, k_ext, v_ext, v_ext, v_ext, k_sum, v_sum)


def attend_far(slot_ids, mask, q, incoming, w_kv, o_a, m_a, l_a, token_blocks, w_out):
    blocks, rows, width = q.shape
    model_dim = incoming.shape[-1]
    group = 4 if blocks % 4 == 0 else 1
    block = pl.BlockSpec((group, rows, width), lambda i, ids: (i, 0, 0))
    token_specs = [
        pl.BlockSpec(
            (1, rows, model_dim), lambda i, ids, n=n: (ids[RAND * group * i + n], 0, 0)
        )
        for n in range(group * RAND)
    ]
    weight = pl.BlockSpec(w_kv.shape, lambda i, ids: (0, 0))
    local_keys = RAND * rows
    heads = width // HD
    flops = blocks * (
        heads * 2 * rows * 2 * LANES * local_keys + 2 * local_keys * model_dim * 2 * width
    )
    bytes_accessed = 2 * blocks * rows * (width * 2 + model_dim * RAND) + 2 * w_kv.size + (
        12 * blocks * rows * width
    )
    grid_spec = pltpu.PrefetchScalarGridSpec(
        num_scalar_prefetch=1,
        grid=(blocks // group,),
        in_specs=[pl.BlockSpec((group, 1, local_keys), lambda i, ids: (i, 0, 0)), block]
        + token_specs
        + [weight, block, block, block, block, pl.BlockSpec(w_out.shape, lambda i, ids: (0, 0))],
        out_specs=block,
        scratch_shapes=[pltpu.VMEM((group * rows, width), jnp.bfloat16)],
    )
    return pl.pallas_call(
        functools.partial(far_kernel, group),
        grid_spec=grid_spec,
        out_shape=jax.ShapeDtypeStruct((blocks, rows, width), jnp.bfloat16),
        cost_estimate=pl.CostEstimate(
            flops=flops,
            transcendentals=blocks * heads * rows * local_keys,
            bytes_accessed=bytes_accessed,
        ),
    )(slot_ids, mask, q, *([incoming] * (group * RAND)), w_kv, o_a, m_a, l_a, token_blocks, w_out)


def local(tokens, w_qkv, w_out, counts, rand_seg, rand_off):
    seq_count = lax.axis_size("seq")
    ctx_count = lax.axis_size("ctx")
    seq_index = lax.axis_index("seq")
    ctx_index = lax.axis_index("ctx")
    dev_count = seq_count * ctx_count
    dev_index = ctx_index * seq_count + seq_index
    tok_rows, model_dim = tokens.shape
    head_total = model_dim // HD
    dev_blocks = tok_rows // BLK
    seg_blocks = dev_blocks * seq_count
    block_total = counts.shape[0]
    capacity = (RAND * dev_blocks + ctx_count - 1) // ctx_count + 1
    first_block = dev_index * dev_blocks
    token_blocks = tokens.reshape(dev_blocks, BLK, model_dim)

    all_owner = rand_seg.reshape(ctx_count, seq_count, dev_blocks * RAND)
    all_offset = rand_off.reshape(ctx_count, seq_count, dev_blocks * RAND)
    col_owner = lax.dynamic_index_in_dim(all_owner, seq_index, axis=1, keepdims=False)
    col_offset = lax.dynamic_index_in_dim(all_offset, seq_index, axis=1, keepdims=False)
    send_off = serve_slots(col_owner, col_offset, ctx_index, capacity)
    outgoing = jnp.take(token_blocks, send_off.reshape(-1), axis=0, mode="clip").reshape(
        ctx_count, capacity, BLK, model_dim
    )
    forward = [(i, i + 1) for i in range(dev_count - 1)]
    backward = [(i + 1, i) for i in range(dev_count - 1)]
    prev_tokens = lax.ppermute(token_blocks[dev_blocks - 1], ("ctx", "seq"), forward)
    next_tokens = lax.ppermute(token_blocks[0], ("ctx", "seq"), backward)

    own = (first_block + jnp.arange(dev_blocks, dtype=jnp.int32))[:, None] == jnp.arange(
        block_total, dtype=jnp.int32
    )[None, :]
    own_counts = jnp.sum(jnp.where(own, counts[None, :], 0), axis=1)
    usable = jnp.arange(BLK, dtype=jnp.int32)[None, :] < own_counts[:, None]
    weighted = jnp.where(usable[:, :, None], token_blocks.astype(jnp.float32), 0.0)
    sums = jnp.sum(weighted, axis=1)
    members = jnp.sum(usable.astype(jnp.float32), axis=1)
    pooled = sums / members[:, None]
    scale = jnp.sqrt(jnp.mean(pooled * pooled, axis=1, keepdims=True) + 1e-05)
    copies = jnp.broadcast_to(pooled[None], (dev_count,) + pooled.shape)
    copies = (copies / jnp.broadcast_to(scale[None], (dev_count,) + scale.shape)).astype(jnp.bfloat16)
    summary_all = lax.all_to_all(copies, ("ctx", "seq"), 0, 0, tiled=True).reshape(-1, model_dim)
    summary_all, outgoing = lax.optimization_barrier((summary_all, outgoing))
    incoming = lax.all_to_all(outgoing, "ctx", split_axis=0, concat_axis=0, tiled=True)

    w_q, w_k, w_v = split_weights(w_qkv, head_total)
    project = lambda x, w: jnp.dot(x, w, preferred_element_type=jnp.float32).astype(jnp.bfloat16)
    q_own = project(tokens, w_q).reshape(dev_blocks, BLK, model_dim)
    rimmed = jnp.concatenate([prev_tokens, tokens, next_tokens], axis=0)
    k_ext = project(rimmed, w_k).reshape(dev_blocks + 2, BLK, model_dim)
    v_ext = project(rimmed, w_v).reshape(dev_blocks + 2, BLK, model_dim)
    k_sum = project(summary_all, w_k)
    v_sum = project(summary_all, w_v)

    my_owner = lax.dynamic_slice_in_dim(rand_seg, first_block, dev_blocks)
    my_offset = lax.dynamic_slice_in_dim(rand_off, first_block, dev_blocks)
    mine = my_owner.reshape(dev_blocks * RAND)
    slot_ids = mine * capacity + positions_among(mine, ctx_count)

    block_ids = first_block + jnp.arange(dev_blocks, dtype=jnp.int32)
    near_ids = block_ids[:, None] + jnp.arange(-1, 2, dtype=jnp.int32)[None, :]
    existing = (near_ids >= 0) & (near_ids < block_total)
    near_counts = jnp.where(existing, jnp.take(counts, jnp.clip(near_ids, 0, block_total - 1)), 0)
    far_global = my_owner * seg_blocks + seq_index * dev_blocks + my_offset
    far_counts = jnp.take(counts, far_global)
    positions = jnp.arange(BLK, dtype=jnp.int32)[None, None, :]
    near_mask = (positions < near_counts[:, :, None]).astype(jnp.int32).reshape(dev_blocks, 1, -1)
    far_mask = (positions < far_counts[:, :, None]).astype(jnp.int32).reshape(dev_blocks, 1, -1)

    o_a, m_a, l_a = attend_near(near_mask, q_own, k_ext, v_ext, k_sum, v_sum)
    mixed = attend_far(
        slot_ids,
        far_mask,
        q_own,
        incoming.reshape(ctx_count * capacity, BLK, model_dim),
        jnp.concatenate([w_k, w_v], axis=1),
        o_a,
        m_a,
        l_a,
        token_blocks,
        w_out,
    )
    return mixed.reshape(tok_rows, model_dim)


def solution(mesh):
    in_specs = (P(("ctx", "seq"), None), P(), P(), P(), P(), P())
    out_specs = P(("ctx", "seq"), None)
    return jax.shard_map(local, mesh=mesh, in_specs=in_specs, out_specs=out_specs, check_vma=False)
```

```python
import functools
import math

import jax
import jax.numpy as jnp
from jax import lax
from jax.experimental import pallas as pl
from jax.experimental.pallas import tpu as pltpu
from jax.sharding import PartitionSpec as P

HD = 64
BLK = 64
RAND = 3
LANES = 128


def positions_among(owners, owner_count):
    marks = (owners[..., None] == jnp.arange(owner_count, dtype=jnp.int32)).astype(jnp.int32)
    ranks = jnp.cumsum(marks, axis=-2) - 1
    return jnp.sum(ranks * marks, axis=-1)


def serve_slots(owners, offsets, target, capacity):
    matched = owners == target
    ranks = jnp.cumsum(matched.astype(jnp.int32), axis=-1) - 1
    slot_hit = matched[..., None, :] & (
        ranks[..., None, :] == jnp.arange(capacity, dtype=jnp.int32)[:, None]
    )
    return jnp.sum(jnp.where(slot_hit, offsets[..., None, :], 0), axis=-1)


def split_weights(w_qkv, head_total):
    model_dim = w_qkv.shape[0]
    shaped = w_qkv.reshape(model_dim, head_total, 3, HD)
    return [shaped[:, :, j, :].reshape(model_dim, head_total * HD) for j in range(3)]


def pair_rows(q, low):
    blank = jnp.zeros_like(q)
    return jnp.concatenate([jnp.where(low, q, blank), jnp.where(low, blank, q)], axis=0)


def pick_rows(x, low, rows):
    return jnp.where(low, x[:rows], x[rows:])


CONTRACT = (((1,), (1,)), ((), ()))


def near_kernel(mask_ref, q_ref, kp_ref, kc_ref, kn_ref, vp_ref, vc_ref, vn_ref, ks_ref, vs_ref,
                o_ref, m_ref, l_ref):
    width = q_ref.shape[-1]
    rows = q_ref.shape[1]
    scaling = 1.0 / math.sqrt(HD)
    valid = mask_ref[0] != 0
    low = lax.broadcasted_iota(jnp.int32, (rows, LANES), 1) < HD
    for tile in range(width // LANES):
        cols = pl.ds(tile * LANES, LANES)
        q_pair = pair_rows(q_ref[0, :, cols], low)
        k_local = jnp.concatenate([kp_ref[0, :, cols], kc_ref[0, :, cols], kn_ref[0, :, cols]], axis=0)
        v_local = jnp.concatenate([vp_ref[0, :, cols], vc_ref[0, :, cols], vn_ref[0, :, cols]], axis=0)
        near = lax.dot_general(q_pair, k_local, CONTRACT, preferred_element_type=jnp.float32)
        near = jnp.where(valid, near * scaling, -jnp.inf)
        wide = lax.dot_general(q_pair, ks_ref[:, cols], CONTRACT, preferred_element_type=jnp.float32)
        wide = wide * scaling
        peak = jnp.maximum(
            jnp.max(near, axis=-1, keepdims=True), jnp.max(wide, axis=-1, keepdims=True)
        )
        near_exp = jnp.exp(near - peak)
        wide_exp = jnp.exp(wide - peak)
        total = jnp.sum(near_exp, axis=-1, keepdims=True) + jnp.sum(wide_exp, axis=-1, keepdims=True)
        result = jnp.dot(near_exp.astype(jnp.bfloat16), v_local, preferred_element_type=jnp.float32)
        result = result + jnp.dot(
            wide_exp.astype(jnp.bfloat16), vs_ref[:, cols], preferred_element_type=jnp.float32
        )
        o_ref[0, :, cols] = pick_rows(result, low, rows)
        m_ref[0, :, cols] = pick_rows(jnp.broadcast_to(peak, result.shape), low, rows)
        l_ref[0, :, cols] = pick_rows(jnp.broadcast_to(total, result.shape), low, rows)


def far_kernel(group, ids_ref, mask_ref, q_ref, *refs):
    token_refs = refs[: group * RAND]
    wkv_ref, oa_ref, ma_ref, la_ref, tok_ref, wo_ref, out_ref, att_ref = refs[group * RAND :]
    width = q_ref.shape[-1]
    rows = q_ref.shape[1]
    scaling = 1.0 / math.sqrt(HD)
    low = lax.broadcasted_iota(jnp.int32, (rows, LANES), 1) < HD
    for g in range(group):
        valid = mask_ref[g] != 0
        far_tokens = jnp.concatenate(
            [ref[0] for ref in token_refs[g * RAND : (g + 1) * RAND]], axis=0
        )
        kv_rows = jnp.dot(far_tokens, wkv_ref[...], preferred_element_type=jnp.float32).astype(
            jnp.bfloat16
        )
        for tile in range(width // LANES):
            lanes = slice(tile * LANES, (tile + 1) * LANES)
            value_lanes = slice(width + tile * LANES, width + (tile + 1) * LANES)
            cols = pl.ds(tile * LANES, LANES)
            q_pair = pair_rows(q_ref[g, :, cols], low)
            scores = lax.dot_general(
                q_pair, kv_rows[:, lanes], CONTRACT, preferred_element_type=jnp.float32
            )
            scores = jnp.where(valid, scores * scaling, -jnp.inf)
            peak = jnp.max(scores, axis=-1, keepdims=True)
            exps = jnp.exp(scores - peak)
            total = jnp.sum(exps, axis=-1, keepdims=True)
            result = jnp.dot(
                exps.astype(jnp.bfloat16), kv_rows[:, value_lanes], preferred_element_type=jnp.float32
            )
            o_b = pick_rows(result, low, rows)
            m_b = pick_rows(jnp.broadcast_to(peak, result.shape), low, rows)
            l_b = pick_rows(jnp.broadcast_to(total, result.shape), low, rows)
            m_a = ma_ref[g, :, cols]
            peak_all = jnp.maximum(m_a, m_b)
            scale_a = jnp.exp(m_a - peak_all)
            scale_b = jnp.exp(m_b - peak_all)
            numerator = oa_ref[g, :, cols] * scale_a + o_b * scale_b
            denominator = la_ref[g, :, cols] * scale_a + l_b * scale_b
            att_ref[g * rows : (g + 1) * rows, cols] = (numerator / denominator).astype(att_ref.dtype)
        mixed = jnp.dot(
            att_ref[g * rows : (g + 1) * rows, :], wo_ref[...], preferred_element_type=jnp.float32
        )
        out_ref[g] = (mixed + tok_ref[g].astype(jnp.float32)).astype(out_ref.dtype)


def attend_near(mask, q, k_ext, v_ext, k_sum, v_sum):
    blocks, rows, width = q.shape
    keys = k_sum.shape[0]
    block = lambda offset: pl.BlockSpec((1, rows, width), lambda i: (i + offset, 0, 0))
    whole = pl.BlockSpec((keys, width), lambda i: (0, 0))
    local_keys = 3 * rows
    heads = width // HD
    flops = blocks * heads * 2 * rows * 2 * LANES * (local_keys + keys)
    bytes_accessed = 2 * (blocks * rows * width * 7 + 2 * keys * width) + 12 * blocks * rows * width
    part = jax.ShapeDtypeStruct((blocks, rows, width), jnp.float32)
    return pl.pallas_call(
        near_kernel,
        grid=(blocks,),
        in_specs=[pl.BlockSpec((1, 1, local_keys), lambda i: (i, 0, 0)), block(0)]
        + [block(0), block(1), block(2)] * 2
        + [whole, whole],
        out_specs=[block(0)] * 3,
        out_shape=[part] * 3,
        cost_estimate=pl.CostEstimate(
            flops=flops,
            transcendentals=blocks * heads * rows * (local_keys + keys),
            bytes_accessed=bytes_accessed,
        ),
    )(mask, q, k_ext, k_ext, k_ext, v_ext, v_ext, v_ext, k_sum, v_sum)


def attend_far(slot_ids, mask, q, incoming, w_kv, o_a, m_a, l_a, token_blocks, w_out):
    blocks, rows, width = q.shape
    model_dim = incoming.shape[-1]
    group = 2 if blocks % 2 == 0 else 1
    block = pl.BlockSpec((group, rows, width), lambda i, ids: (i, 0, 0))
    token_specs = [
        pl.BlockSpec(
            (1, rows, model_dim), lambda i, ids, n=n: (ids[RAND * group * i + n], 0, 0)
        )
        for n in range(group * RAND)
    ]
    weight = pl.BlockSpec(w_kv.shape, lambda i, ids: (0, 0))
    local_keys = RAND * rows
    heads = width // HD
    flops = blocks * (
        heads * 2 * rows * 2 * LANES * local_keys + 2 * local_keys * model_dim * 2 * width
    )
    bytes_accessed = 2 * blocks * rows * (width * 2 + model_dim * RAND) + 2 * w_kv.size + (
        12 * blocks * rows * width
    )
    grid_spec = pltpu.PrefetchScalarGridSpec(
        num_scalar_prefetch=1,
        grid=(blocks // group,),
        in_specs=[pl.BlockSpec((group, 1, local_keys), lambda i, ids: (i, 0, 0)), block]
        + token_specs
        + [weight, block, block, block, block, pl.BlockSpec(w_out.shape, lambda i, ids: (0, 0))],
        out_specs=block,
        scratch_shapes=[pltpu.VMEM((group * rows, width), jnp.bfloat16)],
    )
    return pl.pallas_call(
        functools.partial(far_kernel, group),
        grid_spec=grid_spec,
        out_shape=jax.ShapeDtypeStruct((blocks, rows, width), jnp.bfloat16),
        cost_estimate=pl.CostEstimate(
            flops=flops,
            transcendentals=blocks * heads * rows * local_keys,
            bytes_accessed=bytes_accessed,
        ),
    )(slot_ids, mask, q, *([incoming] * (group * RAND)), w_kv, o_a, m_a, l_a, token_blocks, w_out)


def local(tokens, w_qkv, w_out, counts, rand_seg, rand_off):
    seq_count = lax.axis_size("seq")
    ctx_count = lax.axis_size("ctx")
    seq_index = lax.axis_index("seq")
    ctx_index = lax.axis_index("ctx")
    dev_count = seq_count * ctx_count
    dev_index = ctx_index * seq_count + seq_index
    tok_rows, model_dim = tokens.shape
    head_total = model_dim // HD
    dev_blocks = tok_rows // BLK
    seg_blocks = dev_blocks * seq_count
    block_total = counts.shape[0]
    capacity = (RAND * dev_blocks + ctx_count - 1) // ctx_count + 1
    first_block = dev_index * dev_blocks
    token_blocks = tokens.reshape(dev_blocks, BLK, model_dim)

    all_owner = rand_seg.reshape(ctx_count, seq_count, dev_blocks * RAND)
    all_offset = rand_off.reshape(ctx_count, seq_count, dev_blocks * RAND)
    col_owner = lax.dynamic_index_in_dim(all_owner, seq_index, axis=1, keepdims=False)
    col_offset = lax.dynamic_index_in_dim(all_offset, seq_index, axis=1, keepdims=False)
    send_off = serve_slots(col_owner, col_offset, ctx_index, capacity)
    outgoing = jnp.take(token_blocks, send_off.reshape(-1), axis=0, mode="clip").reshape(
        ctx_count, capacity, BLK, model_dim
    )
    forward = [(i, i + 1) for i in range(dev_count - 1)]
    backward = [(i + 1, i) for i in range(dev_count - 1)]
    prev_tokens = lax.ppermute(token_blocks[dev_blocks - 1], ("ctx", "seq"), forward)
    next_tokens = lax.ppermute(token_blocks[0], ("ctx", "seq"), backward)

    own = (first_block + jnp.arange(dev_blocks, dtype=jnp.int32))[:, None] == jnp.arange(
        block_total, dtype=jnp.int32
    )[None, :]
    own_counts = jnp.sum(jnp.where(own, counts[None, :], 0), axis=1)
    usable = jnp.arange(BLK, dtype=jnp.int32)[None, :] < own_counts[:, None]
    weighted = jnp.where(usable[:, :, None], token_blocks.astype(jnp.float32), 0.0)
    sums = jnp.sum(weighted, axis=1)
    members = jnp.sum(usable.astype(jnp.float32), axis=1)
    pooled = sums / members[:, None]
    scale = jnp.sqrt(jnp.mean(pooled * pooled, axis=1, keepdims=True) + 1e-05)
    copies = jnp.broadcast_to(pooled[None], (dev_count,) + pooled.shape)
    copies = (copies / jnp.broadcast_to(scale[None], (dev_count,) + scale.shape)).astype(jnp.bfloat16)
    summary_all = lax.all_to_all(copies, ("ctx", "seq"), 0, 0, tiled=True).reshape(-1, model_dim)
    summary_all, outgoing = lax.optimization_barrier((summary_all, outgoing))
    incoming = lax.all_to_all(outgoing, "ctx", split_axis=0, concat_axis=0, tiled=True)

    w_q, w_k, w_v = split_weights(w_qkv, head_total)
    project = lambda x, w: jnp.dot(x, w, preferred_element_type=jnp.float32).astype(jnp.bfloat16)
    q_own = project(tokens, w_q).reshape(dev_blocks, BLK, model_dim)
    rimmed = jnp.concatenate([prev_tokens, tokens, next_tokens], axis=0)
    k_ext = project(rimmed, w_k).reshape(dev_blocks + 2, BLK, model_dim)
    v_ext = project(rimmed, w_v).reshape(dev_blocks + 2, BLK, model_dim)
    k_sum = project(summary_all, w_k)
    v_sum = project(summary_all, w_v)

    my_owner = lax.dynamic_slice_in_dim(rand_seg, first_block, dev_blocks)
    my_offset = lax.dynamic_slice_in_dim(rand_off, first_block, dev_blocks)
    mine = my_owner.reshape(dev_blocks * RAND)
    slot_ids = mine * capacity + positions_among(mine, ctx_count)

    block_ids = first_block + jnp.arange(dev_blocks, dtype=jnp.int32)
    near_ids = block_ids[:, None] + jnp.arange(-1, 2, dtype=jnp.int32)[None, :]
    existing = (near_ids >= 0) & (near_ids < block_total)
    near_counts = jnp.where(existing, jnp.take(counts, jnp.clip(near_ids, 0, block_total - 1)), 0)
    far_global = my_owner * seg_blocks + seq_index * dev_blocks + my_offset
    far_counts = jnp.take(counts, far_global)
    positions = jnp.arange(BLK, dtype=jnp.int32)[None, None, :]
    near_mask = (positions < near_counts[:, :, None]).astype(jnp.int32).reshape(dev_blocks, 1, -1)
    far_mask = (positions < far_counts[:, :, None]).astype(jnp.int32).reshape(dev_blocks, 1, -1)

    o_a, m_a, l_a = attend_near(near_mask, q_own, k_ext, v_ext, k_sum, v_sum)
    mixed = attend_far(
        slot_ids,
        far_mask,
        q_own,
        incoming.reshape(ctx_count * capacity, BLK, model_dim),
        jnp.concatenate([w_k, w_v], axis=1),
        o_a,
        m_a,
        l_a,
        token_blocks,
        w_out,
    )
    return mixed.reshape(tok_rows, model_dim)


def solution(mesh):
    in_specs = (P(("ctx", "seq"), None), P(), P(), P(), P(), P())
    out_specs = P(("ctx", "seq"), None)
    return jax.shard_map(local, mesh=mesh, in_specs=in_specs, out_specs=out_specs, check_vma=False)
```

```python
import functools
import math

import jax
import jax.numpy as jnp
from jax import lax
from jax.experimental import pallas as pl
from jax.experimental.pallas import tpu as pltpu
from jax.sharding import PartitionSpec as P

HD = 64
BLK = 64
RAND = 3
LANES = 128


def positions_among(owners, owner_count):
    marks = (owners[..., None] == jnp.arange(owner_count, dtype=jnp.int32)).astype(jnp.int32)
    ranks = jnp.cumsum(marks, axis=-2) - 1
    return jnp.sum(ranks * marks, axis=-1)


def serve_slots(owners, offsets, target, capacity):
    matched = owners == target
    ranks = jnp.cumsum(matched.astype(jnp.int32), axis=-1) - 1
    slot_hit = matched[..., None, :] & (
        ranks[..., None, :] == jnp.arange(capacity, dtype=jnp.int32)[:, None]
    )
    return jnp.sum(jnp.where(slot_hit, offsets[..., None, :], 0), axis=-1)


def split_weights(w_qkv, head_total):
    model_dim = w_qkv.shape[0]
    shaped = w_qkv.reshape(model_dim, head_total, 3, HD)
    return [shaped[:, :, j, :].reshape(model_dim, head_total * HD) for j in range(3)]


def pair_rows(q, low):
    blank = jnp.zeros_like(q)
    return jnp.concatenate([jnp.where(low, q, blank), jnp.where(low, blank, q)], axis=0)


def pick_rows(x, low, rows):
    return jnp.where(low, x[:rows], x[rows:])


CONTRACT = (((1,), (1,)), ((), ()))


def near_kernel(mask_ref, q_ref, kp_ref, kc_ref, kn_ref, vp_ref, vc_ref, vn_ref, ks_ref, vs_ref,
                o_ref, m_ref, l_ref):
    width = q_ref.shape[-1]
    rows = q_ref.shape[1]
    scaling = 1.0 / math.sqrt(HD)
    valid = mask_ref[0] != 0
    low = lax.broadcasted_iota(jnp.int32, (rows, LANES), 1) < HD
    for tile in range(width // LANES):
        cols = pl.ds(tile * LANES, LANES)
        q_pair = pair_rows(q_ref[0, :, cols], low)
        k_local = jnp.concatenate([kp_ref[0, :, cols], kc_ref[0, :, cols], kn_ref[0, :, cols]], axis=0)
        v_local = jnp.concatenate([vp_ref[0, :, cols], vc_ref[0, :, cols], vn_ref[0, :, cols]], axis=0)
        near = lax.dot_general(q_pair, k_local, CONTRACT, preferred_element_type=jnp.float32)
        near = jnp.where(valid, near * scaling, -jnp.inf)
        wide = lax.dot_general(q_pair, ks_ref[:, cols], CONTRACT, preferred_element_type=jnp.float32)
        wide = wide * scaling
        peak = jnp.maximum(
            jnp.max(near, axis=-1, keepdims=True), jnp.max(wide, axis=-1, keepdims=True)
        )
        near_exp = jnp.exp(near - peak)
        wide_exp = jnp.exp(wide - peak)
        total = jnp.sum(near_exp, axis=-1, keepdims=True) + jnp.sum(wide_exp, axis=-1, keepdims=True)
        result = jnp.dot(near_exp.astype(jnp.bfloat16), v_local, preferred_element_type=jnp.float32)
        result = result + jnp.dot(
            wide_exp.astype(jnp.bfloat16), vs_ref[:, cols], preferred_element_type=jnp.float32
        )
        o_ref[0, :, cols] = pick_rows(result, low, rows)
        m_ref[0, :, cols] = pick_rows(jnp.broadcast_to(peak, result.shape), low, rows)
        l_ref[0, :, cols] = pick_rows(jnp.broadcast_to(total, result.shape), low, rows)


def far_kernel(group, ids_ref, mask_ref, q_ref, *refs):
    token_refs = refs[: group * RAND]
    wk_ref, wv_ref, oa_ref, ma_ref, la_ref, tok_ref, wo_ref, out_ref, att_ref = refs[group * RAND :]
    width = q_ref.shape[-1]
    rows = q_ref.shape[1]
    scaling = 1.0 / math.sqrt(HD)
    low = lax.broadcasted_iota(jnp.int32, (rows, LANES), 1) < HD
    for g in range(group):
        valid = mask_ref[g] != 0
        far_tokens = jnp.concatenate(
            [ref[0] for ref in token_refs[g * RAND : (g + 1) * RAND]], axis=0
        )
        k_rows = jnp.dot(far_tokens, wk_ref[...], preferred_element_type=jnp.float32).astype(
            jnp.bfloat16
        )
        v_rows = jnp.dot(far_tokens, wv_ref[...], preferred_element_type=jnp.float32).astype(
            jnp.bfloat16
        )
        for tile in range(width // LANES):
            lanes = slice(tile * LANES, (tile + 1) * LANES)
            cols = pl.ds(tile * LANES, LANES)
            q_pair = pair_rows(q_ref[g, :, cols], low)
            scores = lax.dot_general(
                q_pair, k_rows[:, lanes], CONTRACT, preferred_element_type=jnp.float32
            )
            scores = jnp.where(valid, scores * scaling, -jnp.inf)
            peak = jnp.max(scores, axis=-1, keepdims=True)
            exps = jnp.exp(scores - peak)
            total = jnp.sum(exps, axis=-1, keepdims=True)
            result = jnp.dot(
                exps.astype(jnp.bfloat16), v_rows[:, lanes], preferred_element_type=jnp.float32
            )
            o_b = pick_rows(result, low, rows)
            m_b = pick_rows(jnp.broadcast_to(peak, result.shape), low, rows)
            l_b = pick_rows(jnp.broadcast_to(total, result.shape), low, rows)
            m_a = ma_ref[g, :, cols]
            peak_all = jnp.maximum(m_a, m_b)
            scale_a = jnp.exp(m_a - peak_all)
            scale_b = jnp.exp(m_b - peak_all)
            numerator = oa_ref[g, :, cols] * scale_a + o_b * scale_b
            denominator = la_ref[g, :, cols] * scale_a + l_b * scale_b
            att_ref[g * rows : (g + 1) * rows, cols] = (numerator / denominator).astype(att_ref.dtype)
    mixed = jnp.dot(att_ref[...], wo_ref[...], preferred_element_type=jnp.float32)
    for g in range(group):
        part = mixed[g * rows : (g + 1) * rows] + tok_ref[g].astype(jnp.float32)
        out_ref[g] = part.astype(out_ref.dtype)


def attend_near(mask, q, k_ext, v_ext, k_sum, v_sum):
    blocks, rows, width = q.shape
    keys = k_sum.shape[0]
    block = lambda offset: pl.BlockSpec((1, rows, width), lambda i: (i + offset, 0, 0))
    whole = pl.BlockSpec((keys, width), lambda i: (0, 0))
    local_keys = 3 * rows
    heads = width // HD
    flops = blocks * heads * 2 * rows * 2 * LANES * (local_keys + keys)
    bytes_accessed = 2 * (blocks * rows * width * 7 + 2 * keys * width) + 12 * blocks * rows * width
    part = jax.ShapeDtypeStruct((blocks, rows, width), jnp.float32)
    return pl.pallas_call(
        near_kernel,
        grid=(blocks,),
        in_specs=[pl.BlockSpec((1, 1, local_keys), lambda i: (i, 0, 0)), block(0)]
        + [block(0), block(1), block(2)] * 2
        + [whole, whole],
        out_specs=[block(0)] * 3,
        out_shape=[part] * 3,
        cost_estimate=pl.CostEstimate(
            flops=flops,
            transcendentals=blocks * heads * rows * (local_keys + keys),
            bytes_accessed=bytes_accessed,
        ),
    )(mask, q, k_ext, k_ext, k_ext, v_ext, v_ext, v_ext, k_sum, v_sum)


def attend_far(slot_ids, mask, q, incoming, w_k, w_v, o_a, m_a, l_a, token_blocks, w_out):
    blocks, rows, width = q.shape
    model_dim = incoming.shape[-1]
    group = 2 if blocks % 2 == 0 else 1
    block = pl.BlockSpec((group, rows, width), lambda i, ids: (i, 0, 0))
    token_specs = [
        pl.BlockSpec(
            (1, rows, model_dim), lambda i, ids, n=n: (ids[RAND * group * i + n], 0, 0)
        )
        for n in range(group * RAND)
    ]
    weight = pl.BlockSpec(w_k.shape, lambda i, ids: (0, 0))
    local_keys = RAND * rows
    heads = width // HD
    flops = blocks * (
        heads * 2 * rows * 2 * LANES * local_keys + 2 * local_keys * model_dim * 2 * width
    )
    bytes_accessed = 2 * blocks * rows * (width * 2 + model_dim * RAND) + 2 * (w_k.size + w_v.size) + (
        12 * blocks * rows * width
    )
    grid_spec = pltpu.PrefetchScalarGridSpec(
        num_scalar_prefetch=1,
        grid=(blocks // group,),
        in_specs=[pl.BlockSpec((group, 1, local_keys), lambda i, ids: (i, 0, 0)), block]
        + token_specs
        + [weight, weight, block, block, block, block, pl.BlockSpec(w_out.shape, lambda i, ids: (0, 0))],
        out_specs=block,
        scratch_shapes=[pltpu.VMEM((group * rows, width), jnp.bfloat16)],
    )
    return pl.pallas_call(
        functools.partial(far_kernel, group),
        grid_spec=grid_spec,
        out_shape=jax.ShapeDtypeStruct((blocks, rows, width), jnp.bfloat16),
        cost_estimate=pl.CostEstimate(
            flops=flops,
            transcendentals=blocks * heads * rows * local_keys,
            bytes_accessed=bytes_accessed,
        ),
    )(slot_ids, mask, q, *([incoming] * (group * RAND)), w_k, w_v, o_a, m_a, l_a, token_blocks, w_out)


def local(tokens, w_qkv, w_out, counts, rand_seg, rand_off):
    seq_count = lax.axis_size("seq")
    ctx_count = lax.axis_size("ctx")
    seq_index = lax.axis_index("seq")
    ctx_index = lax.axis_index("ctx")
    dev_count = seq_count * ctx_count
    dev_index = ctx_index * seq_count + seq_index
    tok_rows, model_dim = tokens.shape
    head_total = model_dim // HD
    dev_blocks = tok_rows // BLK
    seg_blocks = dev_blocks * seq_count
    block_total = counts.shape[0]
    capacity = (RAND * dev_blocks + ctx_count - 1) // ctx_count + 1
    first_block = dev_index * dev_blocks
    token_blocks = tokens.reshape(dev_blocks, BLK, model_dim)

    all_owner = rand_seg.reshape(ctx_count, seq_count, dev_blocks * RAND)
    all_offset = rand_off.reshape(ctx_count, seq_count, dev_blocks * RAND)
    col_owner = lax.dynamic_index_in_dim(all_owner, seq_index, axis=1, keepdims=False)
    col_offset = lax.dynamic_index_in_dim(all_offset, seq_index, axis=1, keepdims=False)
    send_off = serve_slots(col_owner, col_offset, ctx_index, capacity)
    outgoing = jnp.take(token_blocks, send_off.reshape(-1), axis=0, mode="clip").reshape(
        ctx_count, capacity, BLK, model_dim
    )
    forward = [(i, i + 1) for i in range(dev_count - 1)]
    backward = [(i + 1, i) for i in range(dev_count - 1)]
    prev_tokens = lax.ppermute(token_blocks[dev_blocks - 1], ("ctx", "seq"), forward)
    next_tokens = lax.ppermute(token_blocks[0], ("ctx", "seq"), backward)

    own = (first_block + jnp.arange(dev_blocks, dtype=jnp.int32))[:, None] == jnp.arange(
        block_total, dtype=jnp.int32
    )[None, :]
    own_counts = jnp.sum(jnp.where(own, counts[None, :], 0), axis=1)
    usable = jnp.arange(BLK, dtype=jnp.int32)[None, :] < own_counts[:, None]
    weighted = jnp.where(usable[:, :, None], token_blocks.astype(jnp.float32), 0.0)
    sums = jnp.sum(weighted, axis=1)
    members = jnp.sum(usable.astype(jnp.float32), axis=1)
    pooled = sums / members[:, None]
    scale = jnp.sqrt(jnp.mean(pooled * pooled, axis=1, keepdims=True) + 1e-05)
    copies = jnp.broadcast_to(pooled[None], (dev_count,) + pooled.shape)
    copies = (copies / jnp.broadcast_to(scale[None], (dev_count,) + scale.shape)).astype(jnp.bfloat16)
    summary_all = lax.all_to_all(copies, ("ctx", "seq"), 0, 0, tiled=True).reshape(-1, model_dim)
    summary_all, outgoing = lax.optimization_barrier((summary_all, outgoing))
    incoming = lax.all_to_all(outgoing, "ctx", split_axis=0, concat_axis=0, tiled=True)

    w_q, w_k, w_v = split_weights(w_qkv, head_total)
    project = lambda x, w: jnp.dot(x, w, preferred_element_type=jnp.float32).astype(jnp.bfloat16)
    q_own = project(tokens, w_q).reshape(dev_blocks, BLK, model_dim)
    rimmed = jnp.concatenate([prev_tokens, tokens, next_tokens], axis=0)
    k_ext = project(rimmed, w_k).reshape(dev_blocks + 2, BLK, model_dim)
    v_ext = project(rimmed, w_v).reshape(dev_blocks + 2, BLK, model_dim)
    k_sum = project(summary_all, w_k)
    v_sum = project(summary_all, w_v)

    my_owner = lax.dynamic_slice_in_dim(rand_seg, first_block, dev_blocks)
    my_offset = lax.dynamic_slice_in_dim(rand_off, first_block, dev_blocks)
    mine = my_owner.reshape(dev_blocks * RAND)
    slot_ids = mine * capacity + positions_among(mine, ctx_count)

    block_ids = first_block + jnp.arange(dev_blocks, dtype=jnp.int32)
    near_ids = block_ids[:, None] + jnp.arange(-1, 2, dtype=jnp.int32)[None, :]
    existing = (near_ids >= 0) & (near_ids < block_total)
    near_counts = jnp.where(existing, jnp.take(counts, jnp.clip(near_ids, 0, block_total - 1)), 0)
    far_global = my_owner * seg_blocks + seq_index * dev_blocks + my_offset
    far_counts = jnp.take(counts, far_global)
    positions = jnp.arange(BLK, dtype=jnp.int32)[None, None, :]
    near_mask = (positions < near_counts[:, :, None]).astype(jnp.int32).reshape(dev_blocks, 1, -1)
    far_mask = (positions < far_counts[:, :, None]).astype(jnp.int32).reshape(dev_blocks, 1, -1)

    o_a, m_a, l_a = attend_near(near_mask, q_own, k_ext, v_ext, k_sum, v_sum)
    mixed = attend_far(
        slot_ids,
        far_mask,
        q_own,
        incoming.reshape(ctx_count * capacity, BLK, model_dim),
        w_k,
        w_v,
        o_a,
        m_a,
        l_a,
        token_blocks,
        w_out,
    )
    return mixed.reshape(tok_rows, model_dim)


def solution(mesh):
    in_specs = (P(("ctx", "seq"), None), P(), P(), P(), P(), P())
    out_specs = P(("ctx", "seq"), None)
    return jax.shard_map(local, mesh=mesh, in_specs=in_specs, out_specs=out_specs, check_vma=False)
```

```python
import functools
import math

import jax
import jax.numpy as jnp
from jax import lax
from jax.experimental import pallas as pl
from jax.experimental.pallas import tpu as pltpu
from jax.sharding import PartitionSpec as P

HD = 64
BLK = 64
RAND = 3
LANES = 128


def positions_among(owners, owner_count):
    marks = (owners[..., None] == jnp.arange(owner_count, dtype=jnp.int32)).astype(jnp.int32)
    ranks = jnp.cumsum(marks, axis=-2) - 1
    return jnp.sum(ranks * marks, axis=-1)


def serve_slots(owners, offsets, target, capacity):
    matched = owners == target
    ranks = jnp.cumsum(matched.astype(jnp.int32), axis=-1) - 1
    slot_hit = matched[..., None, :] & (
        ranks[..., None, :] == jnp.arange(capacity, dtype=jnp.int32)[:, None]
    )
    return jnp.sum(jnp.where(slot_hit, offsets[..., None, :], 0), axis=-1)


def split_weights(w_qkv, head_total):
    model_dim = w_qkv.shape[0]
    shaped = w_qkv.reshape(model_dim, head_total, 3, HD)
    return [shaped[:, :, j, :].reshape(model_dim, head_total * HD) for j in range(3)]


def pair_rows(q, low):
    blank = jnp.zeros_like(q)
    return jnp.concatenate([jnp.where(low, q, blank), jnp.where(low, blank, q)], axis=0)


def pick_rows(x, low, rows):
    return jnp.where(low, x[:rows], x[rows:])


CONTRACT = (((1,), (1,)), ((), ()))


def near_kernel(mask_ref, q_ref, kp_ref, kc_ref, kn_ref, vp_ref, vc_ref, vn_ref, ks_ref, vs_ref,
                o_ref, m_ref, l_ref):
    width = q_ref.shape[-1]
    rows = q_ref.shape[1]
    scaling = 1.0 / math.sqrt(HD)
    valid = mask_ref[0] != 0
    low = lax.broadcasted_iota(jnp.int32, (rows, LANES), 1) < HD
    for tile in range(width // LANES):
        cols = pl.ds(tile * LANES, LANES)
        q_pair = pair_rows(q_ref[0, :, cols], low)
        k_local = jnp.concatenate([kp_ref[0, :, cols], kc_ref[0, :, cols], kn_ref[0, :, cols]], axis=0)
        v_local = jnp.concatenate([vp_ref[0, :, cols], vc_ref[0, :, cols], vn_ref[0, :, cols]], axis=0)
        near = lax.dot_general(q_pair, k_local, CONTRACT, preferred_element_type=jnp.float32)
        near = jnp.where(valid, near * scaling, -jnp.inf)
        wide = lax.dot_general(q_pair, ks_ref[:, cols], CONTRACT, preferred_element_type=jnp.float32)
        wide = wide * scaling
        peak = jnp.maximum(
            jnp.max(near, axis=-1, keepdims=True), jnp.max(wide, axis=-1, keepdims=True)
        )
        near_exp = jnp.exp(near - peak)
        wide_exp = jnp.exp(wide - peak)
        total = jnp.sum(near_exp, axis=-1, keepdims=True) + jnp.sum(wide_exp, axis=-1, keepdims=True)
        result = jnp.dot(near_exp.astype(jnp.bfloat16), v_local, preferred_element_type=jnp.float32)
        result = result + jnp.dot(
            wide_exp.astype(jnp.bfloat16), vs_ref[:, cols], preferred_element_type=jnp.float32
        )
        o_ref[0, :, cols] = pick_rows(result, low, rows)
        m_ref[0, :, cols] = pick_rows(jnp.broadcast_to(peak, result.shape), low, rows)
        l_ref[0, :, cols] = pick_rows(jnp.broadcast_to(total, result.shape), low, rows)


def far_kernel(group, ids_ref, mask_ref, q_ref, *refs):
    token_refs = refs[: group * RAND]
    wk_ref, wv_ref, oa_ref, ma_ref, la_ref, tok_ref, wo_ref, out_ref, att_ref = refs[group * RAND :]
    width = q_ref.shape[-1]
    rows = q_ref.shape[1]
    scaling = 1.0 / math.sqrt(HD)
    low = lax.broadcasted_iota(jnp.int32, (rows, LANES), 1) < HD
    for g in range(group):
        valid = mask_ref[g] != 0
        far_tokens = jnp.concatenate(
            [ref[0] for ref in token_refs[g * RAND : (g + 1) * RAND]], axis=0
        )
        k_rows = jnp.dot(far_tokens, wk_ref[...], preferred_element_type=jnp.float32).astype(
            jnp.bfloat16
        )
        v_rows = jnp.dot(far_tokens, wv_ref[...], preferred_element_type=jnp.float32).astype(
            jnp.bfloat16
        )
        for tile in range(width // LANES):
            lanes = slice(tile * LANES, (tile + 1) * LANES)
            cols = pl.ds(tile * LANES, LANES)
            q_pair = pair_rows(q_ref[g, :, cols], low)
            scores = lax.dot_general(
                q_pair, k_rows[:, lanes], CONTRACT, preferred_element_type=jnp.float32
            )
            scores = jnp.where(valid, scores * scaling, -jnp.inf)
            peak = jnp.max(scores, axis=-1, keepdims=True)
            exps = jnp.exp(scores - peak)
            total = jnp.sum(exps, axis=-1, keepdims=True)
            result = jnp.dot(
                exps.astype(jnp.bfloat16), v_rows[:, lanes], preferred_element_type=jnp.float32
            )
            o_b = pick_rows(result, low, rows)
            m_b = pick_rows(jnp.broadcast_to(peak, result.shape), low, rows)
            l_b = pick_rows(jnp.broadcast_to(total, result.shape), low, rows)
            m_a = ma_ref[g, :, cols]
            peak_all = jnp.maximum(m_a, m_b)
            scale_a = jnp.exp(m_a - peak_all)
            scale_b = jnp.exp(m_b - peak_all)
            numerator = oa_ref[g, :, cols] * scale_a + o_b * scale_b
            denominator = la_ref[g, :, cols] * scale_a + l_b * scale_b
            att_ref[g * rows : (g + 1) * rows, cols] = (numerator / denominator).astype(att_ref.dtype)
    mixed = jnp.dot(att_ref[...], wo_ref[...], preferred_element_type=jnp.float32)
    for g in range(group):
        part = mixed[g * rows : (g + 1) * rows] + tok_ref[g].astype(jnp.float32)
        out_ref[g] = part.astype(out_ref.dtype)


def attend_near(mask, q, k_ext, v_ext, k_sum, v_sum):
    blocks, rows, width = q.shape
    keys = k_sum.shape[0]
    block = lambda offset: pl.BlockSpec((1, rows, width), lambda i: (i + offset, 0, 0))
    whole = pl.BlockSpec((keys, width), lambda i: (0, 0))
    local_keys = 3 * rows
    heads = width // HD
    flops = blocks * heads * 2 * rows * 2 * LANES * (local_keys + keys)
    bytes_accessed = 2 * (blocks * rows * width * 7 + 2 * keys * width) + 12 * blocks * rows * width
    part = jax.ShapeDtypeStruct((blocks, rows, width), jnp.float32)
    return pl.pallas_call(
        near_kernel,
        grid=(blocks,),
        in_specs=[pl.BlockSpec((1, 1, local_keys), lambda i: (i, 0, 0)), block(0)]
        + [block(0), block(1), block(2)] * 2
        + [whole, whole],
        out_specs=[block(0)] * 3,
        out_shape=[part] * 3,
        cost_estimate=pl.CostEstimate(
            flops=flops,
            transcendentals=blocks * heads * rows * (local_keys + keys),
            bytes_accessed=bytes_accessed,
        ),
    )(mask, q, k_ext, k_ext, k_ext, v_ext, v_ext, v_ext, k_sum, v_sum)


def attend_far(slot_ids, mask, q, incoming, w_k, w_v, o_a, m_a, l_a, token_blocks, w_out):
    blocks, rows, width = q.shape
    model_dim = incoming.shape[-1]
    group = 1
    block = pl.BlockSpec((group, rows, width), lambda i, ids: (i, 0, 0))
    token_specs = [
        pl.BlockSpec(
            (1, rows, model_dim), lambda i, ids, n=n: (ids[RAND * group * i + n], 0, 0)
        )
        for n in range(group * RAND)
    ]
    weight = pl.BlockSpec(w_k.shape, lambda i, ids: (0, 0))
    local_keys = RAND * rows
    heads = width // HD
    flops = blocks * (
        heads * 2 * rows * 2 * LANES * local_keys + 2 * local_keys * model_dim * 2 * width
    )
    bytes_accessed = 2 * blocks * rows * (width * 2 + model_dim * RAND) + 2 * (w_k.size + w_v.size) + (
        12 * blocks * rows * width
    )
    grid_spec = pltpu.PrefetchScalarGridSpec(
        num_scalar_prefetch=1,
        grid=(blocks // group,),
        in_specs=[pl.BlockSpec((group, 1, local_keys), lambda i, ids: (i, 0, 0)), block]
        + token_specs
        + [weight, weight, block, block, block, block, pl.BlockSpec(w_out.shape, lambda i, ids: (0, 0))],
        out_specs=block,
        scratch_shapes=[pltpu.VMEM((group * rows, width), jnp.bfloat16)],
    )
    return pl.pallas_call(
        functools.partial(far_kernel, group),
        grid_spec=grid_spec,
        out_shape=jax.ShapeDtypeStruct((blocks, rows, width), jnp.bfloat16),
        cost_estimate=pl.CostEstimate(
            flops=flops,
            transcendentals=blocks * heads * rows * local_keys,
            bytes_accessed=bytes_accessed,
        ),
    )(slot_ids, mask, q, *([incoming] * (group * RAND)), w_k, w_v, o_a, m_a, l_a, token_blocks, w_out)


def local(tokens, w_qkv, w_out, counts, rand_seg, rand_off):
    seq_count = lax.axis_size("seq")
    ctx_count = lax.axis_size("ctx")
    seq_index = lax.axis_index("seq")
    ctx_index = lax.axis_index("ctx")
    dev_count = seq_count * ctx_count
    dev_index = ctx_index * seq_count + seq_index
    tok_rows, model_dim = tokens.shape
    head_total = model_dim // HD
    dev_blocks = tok_rows // BLK
    seg_blocks = dev_blocks * seq_count
    block_total = counts.shape[0]
    capacity = (RAND * dev_blocks + ctx_count - 1) // ctx_count + 1
    first_block = dev_index * dev_blocks
    token_blocks = tokens.reshape(dev_blocks, BLK, model_dim)

    all_owner = rand_seg.reshape(ctx_count, seq_count, dev_blocks * RAND)
    all_offset = rand_off.reshape(ctx_count, seq_count, dev_blocks * RAND)
    col_owner = lax.dynamic_index_in_dim(all_owner, seq_index, axis=1, keepdims=False)
    col_offset = lax.dynamic_index_in_dim(all_offset, seq_index, axis=1, keepdims=False)
    send_off = serve_slots(col_owner, col_offset, ctx_index, capacity)
    outgoing = jnp.take(token_blocks, send_off.reshape(-1), axis=0, mode="clip").reshape(
        ctx_count, capacity, BLK, model_dim
    )
    forward = [(i, i + 1) for i in range(dev_count - 1)]
    backward = [(i + 1, i) for i in range(dev_count - 1)]
    prev_tokens = lax.ppermute(token_blocks[dev_blocks - 1], ("ctx", "seq"), forward)
    next_tokens = lax.ppermute(token_blocks[0], ("ctx", "seq"), backward)

    own = (first_block + jnp.arange(dev_blocks, dtype=jnp.int32))[:, None] == jnp.arange(
        block_total, dtype=jnp.int32
    )[None, :]
    own_counts = jnp.sum(jnp.where(own, counts[None, :], 0), axis=1)
    usable = jnp.arange(BLK, dtype=jnp.int32)[None, :] < own_counts[:, None]
    weighted = jnp.where(usable[:, :, None], token_blocks.astype(jnp.float32), 0.0)
    sums = jnp.sum(weighted, axis=1)
    members = jnp.sum(usable.astype(jnp.float32), axis=1)
    pooled = sums / members[:, None]
    scale = jnp.sqrt(jnp.mean(pooled * pooled, axis=1, keepdims=True) + 1e-05)
    copies = jnp.broadcast_to(pooled[None], (dev_count,) + pooled.shape)
    copies = (copies / jnp.broadcast_to(scale[None], (dev_count,) + scale.shape)).astype(jnp.bfloat16)
    summary_all = lax.all_to_all(copies, ("ctx", "seq"), 0, 0, tiled=True).reshape(-1, model_dim)
    summary_all, outgoing = lax.optimization_barrier((summary_all, outgoing))
    incoming = lax.all_to_all(outgoing, "ctx", split_axis=0, concat_axis=0, tiled=True)

    w_q, w_k, w_v = split_weights(w_qkv, head_total)
    project = lambda x, w: jnp.dot(x, w, preferred_element_type=jnp.float32).astype(jnp.bfloat16)
    q_own = project(tokens, w_q).reshape(dev_blocks, BLK, model_dim)
    rimmed = jnp.concatenate([prev_tokens, tokens, next_tokens], axis=0)
    k_ext = project(rimmed, w_k).reshape(dev_blocks + 2, BLK, model_dim)
    v_ext = project(rimmed, w_v).reshape(dev_blocks + 2, BLK, model_dim)
    k_sum = project(summary_all, w_k)
    v_sum = project(summary_all, w_v)

    my_owner = lax.dynamic_slice_in_dim(rand_seg, first_block, dev_blocks)
    my_offset = lax.dynamic_slice_in_dim(rand_off, first_block, dev_blocks)
    mine = my_owner.reshape(dev_blocks * RAND)
    slot_ids = mine * capacity + positions_among(mine, ctx_count)

    block_ids = first_block + jnp.arange(dev_blocks, dtype=jnp.int32)
    near_ids = block_ids[:, None] + jnp.arange(-1, 2, dtype=jnp.int32)[None, :]
    existing = (near_ids >= 0) & (near_ids < block_total)
    near_counts = jnp.where(existing, jnp.take(counts, jnp.clip(near_ids, 0, block_total - 1)), 0)
    far_global = my_owner * seg_blocks + seq_index * dev_blocks + my_offset
    far_counts = jnp.take(counts, far_global)
    positions = jnp.arange(BLK, dtype=jnp.int32)[None, None, :]
    near_mask = (positions < near_counts[:, :, None]).astype(jnp.int32).reshape(dev_blocks, 1, -1)
    far_mask = (positions < far_counts[:, :, None]).astype(jnp.int32).reshape(dev_blocks, 1, -1)

    o_a, m_a, l_a = attend_near(near_mask, q_own, k_ext, v_ext, k_sum, v_sum)
    mixed = attend_far(
        slot_ids,
        far_mask,
        q_own,
        incoming.reshape(ctx_count * capacity, BLK, model_dim),
        w_k,
        w_v,
        o_a,
        m_a,
        l_a,
        token_blocks,
        w_out,
    )
    return mixed.reshape(tok_rows, model_dim)


def solution(mesh):
    in_specs = (P(("ctx", "seq"), None), P(), P(), P(), P(), P())
    out_specs = P(("ctx", "seq"), None)
    return jax.shard_map(local, mesh=mesh, in_specs=in_specs, out_specs=out_specs, check_vma=False)
```

```python
import functools
import math

import jax
import jax.numpy as jnp
from jax import lax
from jax.experimental import pallas as pl
from jax.experimental.pallas import tpu as pltpu
from jax.sharding import PartitionSpec as P

HD = 64
BLK = 64
RAND = 3
LANES = 128


def positions_among(owners, owner_count):
    marks = (owners[..., None] == jnp.arange(owner_count, dtype=jnp.int32)).astype(jnp.int32)
    ranks = jnp.cumsum(marks, axis=-2) - 1
    return jnp.sum(ranks * marks, axis=-1)


def serve_slots(owners, offsets, target, capacity):
    matched = owners == target
    ranks = jnp.cumsum(matched.astype(jnp.int32), axis=-1) - 1
    slot_hit = matched[..., None, :] & (
        ranks[..., None, :] == jnp.arange(capacity, dtype=jnp.int32)[:, None]
    )
    return jnp.sum(jnp.where(slot_hit, offsets[..., None, :], 0), axis=-1)


def split_weights(w_qkv, head_total):
    model_dim = w_qkv.shape[0]
    shaped = w_qkv.reshape(model_dim, head_total, 3, HD)
    return [shaped[:, :, j, :].reshape(model_dim, head_total * HD) for j in range(3)]


def pair_rows(q, low):
    blank = jnp.zeros_like(q)
    return jnp.concatenate([jnp.where(low, q, blank), jnp.where(low, blank, q)], axis=0)


def pick_rows(x, low, rows):
    return jnp.where(low, x[:rows], x[rows:])


CONTRACT = (((1,), (1,)), ((), ()))


def near_kernel(mask_ref, q_ref, kp_ref, kc_ref, kn_ref, vp_ref, vc_ref, vn_ref, ks_ref, vs_ref,
                o_ref, m_ref, l_ref):
    width = q_ref.shape[-1]
    rows = q_ref.shape[1]
    scaling = 1.0 / math.sqrt(HD)
    valid = mask_ref[0] != 0
    low = lax.broadcasted_iota(jnp.int32, (rows, LANES), 1) < HD
    for tile in range(width // LANES):
        cols = pl.ds(tile * LANES, LANES)
        q_pair = pair_rows(q_ref[0, :, cols], low)
        k_local = jnp.concatenate([kp_ref[0, :, cols], kc_ref[0, :, cols], kn_ref[0, :, cols]], axis=0)
        v_local = jnp.concatenate([vp_ref[0, :, cols], vc_ref[0, :, cols], vn_ref[0, :, cols]], axis=0)
        near = lax.dot_general(q_pair, k_local, CONTRACT, preferred_element_type=jnp.float32)
        near = jnp.where(valid, near * scaling, -jnp.inf)
        wide = lax.dot_general(q_pair, ks_ref[:, cols], CONTRACT, preferred_element_type=jnp.float32)
        wide = wide * scaling
        peak = jnp.maximum(
            jnp.max(near, axis=-1, keepdims=True), jnp.max(wide, axis=-1, keepdims=True)
        )
        near_exp = jnp.exp(near - peak)
        wide_exp = jnp.exp(wide - peak)
        total = jnp.sum(near_exp, axis=-1, keepdims=True) + jnp.sum(wide_exp, axis=-1, keepdims=True)
        result = jnp.dot(near_exp.astype(jnp.bfloat16), v_local, preferred_element_type=jnp.float32)
        result = result + jnp.dot(
            wide_exp.astype(jnp.bfloat16), vs_ref[:, cols], preferred_element_type=jnp.float32
        )
        o_ref[0, :, cols] = pick_rows(result, low, rows)
        m_ref[0, :, cols] = pick_rows(jnp.broadcast_to(peak, result.shape), low, rows)
        l_ref[0, :, cols] = pick_rows(jnp.broadcast_to(total, result.shape), low, rows)


def far_kernel(group, ids_ref, mask_ref, q_ref, *refs):
    token_refs = refs[: group * RAND]
    wk_ref, wv_ref, oa_ref, ma_ref, la_ref, tok_ref, wo_ref, out_ref, att_ref = refs[group * RAND :]
    width = q_ref.shape[-1]
    rows = q_ref.shape[1]
    scaling = 1.0 / math.sqrt(HD)
    low = lax.broadcasted_iota(jnp.int32, (rows, LANES), 1) < HD
    for g in range(group):
        valid = mask_ref[g] != 0
        far_tokens = jnp.concatenate(
            [ref[0] for ref in token_refs[g * RAND : (g + 1) * RAND]], axis=0
        )
        k_rows = jnp.dot(far_tokens, wk_ref[...], preferred_element_type=jnp.float32).astype(
            jnp.bfloat16
        )
        v_rows = jnp.dot(far_tokens, wv_ref[...], preferred_element_type=jnp.float32).astype(
            jnp.bfloat16
        )
        for tile in range(width // LANES):
            lanes = slice(tile * LANES, (tile + 1) * LANES)
            cols = pl.ds(tile * LANES, LANES)
            q_pair = pair_rows(q_ref[g, :, cols], low)
            scores = lax.dot_general(
                q_pair, k_rows[:, lanes], CONTRACT, preferred_element_type=jnp.float32
            )
            scores = jnp.where(valid, scores * scaling, -jnp.inf)
            peak = jnp.max(scores, axis=-1, keepdims=True)
            exps = jnp.exp(scores - peak)
            total = jnp.sum(exps, axis=-1, keepdims=True)
            result = jnp.dot(
                exps.astype(jnp.bfloat16), v_rows[:, lanes], preferred_element_type=jnp.float32
            )
            o_b = pick_rows(result, low, rows)
            m_b = pick_rows(jnp.broadcast_to(peak, result.shape), low, rows)
            l_b = pick_rows(jnp.broadcast_to(total, result.shape), low, rows)
            m_a = ma_ref[g, :, cols]
            peak_all = jnp.maximum(m_a, m_b)
            scale_a = jnp.exp(m_a - peak_all)
            scale_b = jnp.exp(m_b - peak_all)
            numerator = oa_ref[g, :, cols] * scale_a + o_b * scale_b
            denominator = la_ref[g, :, cols] * scale_a + l_b * scale_b
            att_ref[g * rows : (g + 1) * rows, cols] = (numerator / denominator).astype(att_ref.dtype)
    mixed = jnp.dot(att_ref[...], wo_ref[...], preferred_element_type=jnp.float32)
    for g in range(group):
        part = mixed[g * rows : (g + 1) * rows] + tok_ref[g].astype(jnp.float32)
        out_ref[g] = part.astype(out_ref.dtype)


def attend_near(mask, q, k_ext, v_ext, k_sum, v_sum):
    blocks, rows, width = q.shape
    keys = k_sum.shape[0]
    block = lambda offset: pl.BlockSpec((1, rows, width), lambda i: (i + offset, 0, 0))
    whole = pl.BlockSpec((keys, width), lambda i: (0, 0))
    local_keys = 3 * rows
    heads = width // HD
    flops = blocks * heads * 2 * rows * 2 * LANES * (local_keys + keys)
    bytes_accessed = 2 * (blocks * rows * width * 7 + 2 * keys * width) + 12 * blocks * rows * width
    part = jax.ShapeDtypeStruct((blocks, rows, width), jnp.float32)
    return pl.pallas_call(
        near_kernel,
        grid=(blocks,),
        in_specs=[pl.BlockSpec((1, 1, local_keys), lambda i: (i, 0, 0)), block(0)]
        + [block(0), block(1), block(2)] * 2
        + [whole, whole],
        out_specs=[block(0)] * 3,
        out_shape=[part] * 3,
        cost_estimate=pl.CostEstimate(
            flops=flops,
            transcendentals=blocks * heads * rows * (local_keys + keys),
            bytes_accessed=bytes_accessed,
        ),
    )(mask, q, k_ext, k_ext, k_ext, v_ext, v_ext, v_ext, k_sum, v_sum)


def attend_far(slot_ids, mask, q, incoming, w_k, w_v, o_a, m_a, l_a, token_blocks, w_out):
    blocks, rows, width = q.shape
    model_dim = incoming.shape[-1]
    group = 4 if blocks % 4 == 0 else 1
    block = pl.BlockSpec((group, rows, width), lambda i, ids: (i, 0, 0))
    token_specs = [
        pl.BlockSpec(
            (1, rows, model_dim), lambda i, ids, n=n: (ids[RAND * group * i + n], 0, 0)
        )
        for n in range(group * RAND)
    ]
    weight = pl.BlockSpec(w_k.shape, lambda i, ids: (0, 0))
    local_keys = RAND * rows
    heads = width // HD
    flops = blocks * (
        heads * 2 * rows * 2 * LANES * local_keys + 2 * local_keys * model_dim * 2 * width
    )
    bytes_accessed = 2 * blocks * rows * (width * 2 + model_dim * RAND) + 2 * (w_k.size + w_v.size) + (
        12 * blocks * rows * width
    )
    grid_spec = pltpu.PrefetchScalarGridSpec(
        num_scalar_prefetch=1,
        grid=(blocks // group,),
        in_specs=[pl.BlockSpec((group, 1, local_keys), lambda i, ids: (i, 0, 0)), block]
        + token_specs
        + [weight, weight, block, block, block, block, pl.BlockSpec(w_out.shape, lambda i, ids: (0, 0))],
        out_specs=block,
        scratch_shapes=[pltpu.VMEM((group * rows, width), jnp.bfloat16)],
    )
    return pl.pallas_call(
        functools.partial(far_kernel, group),
        grid_spec=grid_spec,
        out_shape=jax.ShapeDtypeStruct((blocks, rows, width), jnp.bfloat16),
        cost_estimate=pl.CostEstimate(
            flops=flops,
            transcendentals=blocks * heads * rows * local_keys,
            bytes_accessed=bytes_accessed,
        ),
    )(slot_ids, mask, q, *([incoming] * (group * RAND)), w_k, w_v, o_a, m_a, l_a, token_blocks, w_out)


def local(tokens, w_qkv, w_out, counts, rand_seg, rand_off):
    seq_count = lax.axis_size("seq")
    ctx_count = lax.axis_size("ctx")
    seq_index = lax.axis_index("seq")
    ctx_index = lax.axis_index("ctx")
    dev_count = seq_count * ctx_count
    dev_index = ctx_index * seq_count + seq_index
    tok_rows, model_dim = tokens.shape
    head_total = model_dim // HD
    dev_blocks = tok_rows // BLK
    seg_blocks = dev_blocks * seq_count
    block_total = counts.shape[0]
    capacity = (RAND * dev_blocks + ctx_count - 1) // ctx_count + 1
    first_block = dev_index * dev_blocks
    token_blocks = tokens.reshape(dev_blocks, BLK, model_dim)

    all_owner = rand_seg.reshape(ctx_count, seq_count, dev_blocks * RAND)
    all_offset = rand_off.reshape(ctx_count, seq_count, dev_blocks * RAND)
    col_owner = lax.dynamic_index_in_dim(all_owner, seq_index, axis=1, keepdims=False)
    col_offset = lax.dynamic_index_in_dim(all_offset, seq_index, axis=1, keepdims=False)
    send_off = serve_slots(col_owner, col_offset, ctx_index, capacity)
    outgoing = jnp.take(token_blocks, send_off.reshape(-1), axis=0, mode="clip").reshape(
        ctx_count, capacity, BLK, model_dim
    )
    forward = [(i, i + 1) for i in range(dev_count - 1)]
    backward = [(i + 1, i) for i in range(dev_count - 1)]
    prev_tokens = lax.ppermute(token_blocks[dev_blocks - 1], ("ctx", "seq"), forward)
    next_tokens = lax.ppermute(token_blocks[0], ("ctx", "seq"), backward)

    own = (first_block + jnp.arange(dev_blocks, dtype=jnp.int32))[:, None] == jnp.arange(
        block_total, dtype=jnp.int32
    )[None, :]
    own_counts = jnp.sum(jnp.where(own, counts[None, :], 0), axis=1)
    usable = jnp.arange(BLK, dtype=jnp.int32)[None, :] < own_counts[:, None]
    weighted = jnp.where(usable[:, :, None], token_blocks.astype(jnp.float32), 0.0)
    sums = jnp.sum(weighted, axis=1)
    members = jnp.sum(usable.astype(jnp.float32), axis=1)
    pooled = sums / members[:, None]
    scale = jnp.sqrt(jnp.mean(pooled * pooled, axis=1, keepdims=True) + 1e-05)
    copies = jnp.broadcast_to(pooled[None], (dev_count,) + pooled.shape)
    copies = (copies / jnp.broadcast_to(scale[None], (dev_count,) + scale.shape)).astype(jnp.bfloat16)
    summary_all = lax.all_to_all(copies, ("ctx", "seq"), 0, 0, tiled=True).reshape(-1, model_dim)
    summary_all, outgoing = lax.optimization_barrier((summary_all, outgoing))
    incoming = lax.all_to_all(outgoing, "ctx", split_axis=0, concat_axis=0, tiled=True)

    w_q, w_k, w_v = split_weights(w_qkv, head_total)
    project = lambda x, w: jnp.dot(x, w, preferred_element_type=jnp.float32).astype(jnp.bfloat16)
    q_own = project(tokens, w_q).reshape(dev_blocks, BLK, model_dim)
    rimmed = jnp.concatenate([prev_tokens, tokens, next_tokens], axis=0)
    k_ext = project(rimmed, w_k).reshape(dev_blocks + 2, BLK, model_dim)
    v_ext = project(rimmed, w_v).reshape(dev_blocks + 2, BLK, model_dim)
    k_sum = project(summary_all, w_k)
    v_sum = project(summary_all, w_v)

    my_owner = lax.dynamic_slice_in_dim(rand_seg, first_block, dev_blocks)
    my_offset = lax.dynamic_slice_in_dim(rand_off, first_block, dev_blocks)
    mine = my_owner.reshape(dev_blocks * RAND)
    slot_ids = mine * capacity + positions_among(mine, ctx_count)

    block_ids = first_block + jnp.arange(dev_blocks, dtype=jnp.int32)
    near_ids = block_ids[:, None] + jnp.arange(-1, 2, dtype=jnp.int32)[None, :]
    existing = (near_ids >= 0) & (near_ids < block_total)
    near_counts = jnp.where(existing, jnp.take(counts, jnp.clip(near_ids, 0, block_total - 1)), 0)
    far_global = my_owner * seg_blocks + seq_index * dev_blocks + my_offset
    far_counts = jnp.take(counts, far_global)
    positions = jnp.arange(BLK, dtype=jnp.int32)[None, None, :]
    near_mask = (positions < near_counts[:, :, None]).astype(jnp.int32).reshape(dev_blocks, 1, -1)
    far_mask = (positions < far_counts[:, :, None]).astype(jnp.int32).reshape(dev_blocks, 1, -1)

    o_a, m_a, l_a = attend_near(near_mask, q_own, k_ext, v_ext, k_sum, v_sum)
    mixed = attend_far(
        slot_ids,
        far_mask,
        q_own,
        incoming.reshape(ctx_count * capacity, BLK, model_dim),
        w_k,
        w_v,
        o_a,
        m_a,
        l_a,
        token_blocks,
        w_out,
    )
    return mixed.reshape(tok_rows, model_dim)


def solution(mesh):
    in_specs = (P(("ctx", "seq"), None), P(), P(), P(), P(), P())
    out_specs = P(("ctx", "seq"), None)
    return jax.shard_map(local, mesh=mesh, in_specs=in_specs, out_specs=out_specs, check_vma=False)
```
